512 devices in a mesh: gx: 8 (over z), gy: 8 (over y), gz: 8 (over x, core).
Axes of the slice: x: 4, y: 8, z: 8, core: 2. Of those that a mesh axis runs over, the one named last changes fastest.
Arguments:
- reference_image: bfloat16 [128, 128, 1024], P('gx', 'gy', 'gz'), may hold values from -60 to 60
- deformed_image: bfloat16 [128, 128, 1024], P('gx', 'gy', 'gz'), may hold values from -60 to 60
- roi_mask: int32 [128, 128, 1024], P('gx', 'gy', 'gz'), may hold values 0 or 1
- displacement: float32 [3, 32768, 8], P(None, ('gx', 'gy', 'gz')), may hold values from -12 to 12
- node_map: int32 [32768], P(('gx', 'gy', 'gz')), may hold values from 0 to 4095, as said below
Outputs:
- displacement_out: float32 [3, 32768, 8], P(None, ('gx', 'gy', 'gz'))
The draws below stay inside these ranges and needn't reach their ends.
Inputs may be any that keep to these rules, and one draw needn't show every extreme that they name: Within each slab (devices with one gx index) node_map is a permutation of 0 to 4095. Every device lists exactly 2 blocks of one tile and at most one block of each other tile.
All inputs are finite; a program needn't handle non-finite values. No bound on the sum of `roi_mask` on one device may be relied on, other than what follows from the above.
Results may differ from the reference program's by a relative error of at most 0.00083.
Values may be sent and summed in bfloat16 or wider, within the bound.
No kernel may reach another device: no remote copies, remote signals or barrier semaphores. Data moves between devices by JAX's collectives and lax.ppermute only.
A program may use at most 64 MiB of HBM per device.

```python
import jax
import jax.numpy as jnp
from jax import lax

ELEM = 4
ITERS = 2
NX = 128
NY = 128
NZ = 1024
EX = 4
EY = 4
EZ = 32
NBT = 64
BN = 8
SLABS = 8
SLOTS = 32768
N_GX = 8
N_GY = 8
N_GZ = 8


def shuffled_rows(row_keys, length):
    ordered = jnp.arange(length, dtype=jnp.int32)

    def single(row_key):
        return jax.random.permutation(row_key, ordered)
    return jax.vmap(single)(row_keys)


def one_slab(slab_key):
    members = NBT
    shift_key, rest_key, tile_key, slot_key = jax.random.split(slab_key, 4)
    heavy_shift = jax.random.randint(shift_key, (1,), 0, members).astype(jnp.int32)
    others = (heavy_shift + 1 + jax.random.permutation(rest_key, jnp.arange(members - 1, dtype=jnp.int32))) % members
    shifts = jnp.concatenate([heavy_shift, heavy_shift, others[:members - 2]])
    tile_orders = shuffled_rows(jax.random.split(tile_key, members), members)
    owner_index = jnp.arange(members, dtype=jnp.int32)[:, None]
    column_index = jnp.arange(members, dtype=jnp.int32)[None, :]
    source_tile = (owner_index - shifts[None, :]) % members
    block_ids = source_tile * members + tile_orders[source_tile, column_index]
    slot_orders = shuffled_rows(jax.random.split(slot_key, members), members)
    return jnp.take_along_axis(block_ids, slot_orders, axis=1).reshape(-1)


def draw_node_map(key, part):
    slab_keys = jax.random.split(jax.random.fold_in(key, 17), SLABS)
    return jax.vmap(one_slab)(slab_keys).reshape(-1).astype(jnp.int32)


def with_ends(array, own_key, smallest, largest):
    dims = array.shape
    spot = [jax.random.randint(jax.random.fold_in(own_key, axis), (), 0, dims[axis]) for axis in range(len(dims))]
    array = array.at[tuple(spot)].set(smallest)
    longest = dims.index(max(dims))
    spot[longest] = (spot[longest] + 1) % dims[longest]
    return array.at[tuple(spot)].set(largest)


def block_scale(rng, extent, cuts, smallest, top_value):
    level, own = 1.0, jax.random.fold_in(rng, 6)
    for dim, blocks in cuts:
        steps = jnp.exp(jax.random.uniform(jax.random.fold_in(own, dim), (blocks,), jnp.float32, smallest / len(cuts), top_value / len(cuts)))
        level = level * jnp.repeat(steps, extent[dim] // blocks).reshape([-1 if axis == dim else 1 for axis in range(len(extent))])
    return level


def centred(rng, shape, scale, most, shards=(), held_as=jnp.bfloat16):
    factor_of = block_scale(rng, shape, shards, -0.22, 0.18) if shards else 1.0
    values = jax.random.normal(rng, shape, jnp.float32) * scale * factor_of
    return jnp.minimum(jnp.maximum(values, -most), most).astype(held_as)


def setup_inputs(seed: int = 0) -> dict:
    seeds = jax.random.split(jax.random.key(seed), 6)
    return {
        "reference_image": centred(seeds[0], (NX, NY, NZ), 10.0, 60.0, ((0, 8), (1, 8), (2, 8))),
        "deformed_image": centred(seeds[1], (NX, NY, NZ), 10.0, 60.0, ((0, 8), (1, 8), (2, 8))),
        "roi_mask": with_ends((jax.random.randint(seeds[2], (NX, NY, NZ), 0, 4) < 3).astype(jnp.int32), jax.random.fold_in(seeds[2], 1), 0, 1),
        "displacement": centred(seeds[3], (3, SLOTS, BN), 2.0, 12.0, ((1, 512),), jnp.float32),
        "node_map": draw_node_map(jax.random.fold_in(seeds[5], 71), 0),
    }


binomial = (0.0625, 0.25, 0.375, 0.25, 0.0625)
lame_lambda = 1.0
shear_modulus = 0.5
elastic_weight = 2.0
diagonal_shift = 6.0


def smooth_axis(volume, dimension):
    length = volume.shape[dimension] - 4
    summed = binomial[0] * lax.slice_in_dim(volume, 0, length, axis=dimension)
    for offset in range(1, 5):
        summed = summed + binomial[offset] * lax.slice_in_dim(volume, offset, offset + length, axis=dimension)
    return summed


def derive_fields(first_padded, second_padded):
    first_smooth = first_padded
    second_smooth = second_padded
    for dimension in range(3):
        first_smooth = smooth_axis(first_smooth, dimension)
        second_smooth = smooth_axis(second_smooth, dimension)
    average = (first_smooth + second_smooth) * 0.5
    contrast = (second_smooth - first_smooth)[1:-1, 1:-1, 1:-1].astype(jnp.bfloat16)
    slopes = []
    for dimension in range(3):
        length = average.shape[dimension] - 2
        forward_part = lax.slice_in_dim(average, 2, length + 2, axis=dimension)
        backward_part = lax.slice_in_dim(average, 0, length, axis=dimension)
        gradient = (forward_part - backward_part) * 0.5
        for cropped_dim in range(3):
            if cropped_dim != dimension:
                gradient = lax.slice_in_dim(gradient, 1, gradient.shape[cropped_dim] - 1, axis=cropped_dim)
        slopes.append(gradient.astype(jnp.bfloat16))
    return jnp.stack([contrast] + slopes)


def interp_axis(volume, dimension, cells_edge):
    length = volume.shape[dimension]
    before = lax.slice_in_dim(volume, 0, length - 1, axis=dimension)
    after = lax.slice_in_dim(volume, 1, length, axis=dimension)
    shape_one = [1] * (volume.ndim + 1)
    shape_one[dimension + 1] = cells_edge
    fraction = (jnp.arange(cells_edge, dtype=jnp.float32) / cells_edge).reshape(shape_one)
    merged = jnp.expand_dims(before, dimension + 1) * (1.0 - fraction) + jnp.expand_dims(after, dimension + 1) * fraction
    new_shape = list(volume.shape)
    new_shape[dimension] = (length - 1) * cells_edge
    return merged.reshape(new_shape)


def collect_axis(volume, dimension, cells_edge, squared):
    elements = volume.shape[dimension] // cells_edge
    split_shape = list(volume.shape[:dimension]) + [elements, cells_edge] + list(volume.shape[dimension + 1:])
    pieces = volume.reshape(split_shape)
    shape_one = [1] * len(split_shape)
    shape_one[dimension + 1] = cells_edge
    fraction = (jnp.arange(cells_edge, dtype=jnp.float32) / cells_edge).reshape(shape_one)
    weight_low = 1.0 - fraction
    weight_high = fraction
    if squared:
        weight_low = weight_low * weight_low
        weight_high = weight_high * weight_high
    low_side = jnp.sum(pieces * weight_low, axis=dimension + 1)
    high_side = jnp.sum(pieces * weight_high, axis=dimension + 1)
    return lax.slice_in_dim(low_side, 1, elements, axis=dimension) + lax.slice_in_dim(high_side, 0, elements - 1, axis=dimension)


def pair_op(volume, dimension, factor):
    length = volume.shape[dimension]
    return lax.slice_in_dim(volume, 1, length, axis=dimension) + factor * lax.slice_in_dim(volume, 0, length - 1, axis=dimension)


def cross_pairs(volume, chosen, factor, offset):
    for dimension in range(3):
        volume = pair_op(volume, dimension + offset, factor if dimension == chosen else 1.0)
    return volume


def elastic_force(padded):
    gradients = [cross_pairs(padded, chosen, -1.0, 1) * (1.0 / (4.0 * ELEM)) for chosen in range(3)]
    deform = [[gradients[source][target] + (1.0 if target == source else 0.0) for source in range(3)] for target in range(3)]
    strain = [[0.5 * (deform[0][target] * deform[0][source] + deform[1][target] * deform[1][source] + deform[2][target] * deform[2][source]) - (0.5 if target == source else 0.0) for source in range(3)] for target in range(3)]
    trace_strain = strain[0][0] + strain[1][1] + strain[2][2]
    stress = [[2.0 * shear_modulus * strain[target][source] + (lame_lambda * trace_strain if target == source else 0.0) for source in range(3)] for target in range(3)]
    nominal = [[deform[target][0] * stress[0][source] + deform[target][1] * stress[1][source] + deform[target][2] * stress[2][source] for source in range(3)] for target in range(3)]
    coefficient = ELEM * ELEM / 4.0
    forces = []
    for target in range(3):
        summed = cross_pairs(nominal[target][0], 0, -1.0, 0)
        for source in range(1, 3):
            summed = summed + cross_pairs(nominal[target][source], source, -1.0, 0)
        forces.append(-coefficient * summed)
    return jnp.stack(forces)


def spread_all(padded):
    for dimension in range(1, 4):
        padded = interp_axis(padded, dimension, ELEM)
    return padded


def collect_all(volume, squared):
    for dimension in (3, 2, 1):
        volume = collect_axis(volume, dimension, ELEM, squared)
    return volume


def slot_targets(node_map):
    per_slab = NBT * NBT
    slab_index = jnp.arange(SLOTS, dtype=jnp.int32) // per_slab
    return (slab_index * per_slab + node_map).astype(jnp.int32)


def reference(reference_image, deformed_image, roi_mask, displacement, node_map):
    first_padded = jnp.pad(reference_image.astype(jnp.float32), 5)
    second_padded = jnp.pad(deformed_image.astype(jnp.float32), 5)
    derived = derive_fields(first_padded, second_padded)
    contrast = derived[0].astype(jnp.float32)
    slopes = derived[1:].astype(jnp.float32)
    region = jnp.pad(roi_mask, 2).astype(jnp.float32)
    masked_slopes = slopes * region[None]
    curvature = collect_all(masked_slopes * slopes, True) + diagonal_shift
    targets = slot_targets(node_map)
    blocks = jnp.zeros((3, SLOTS, BN), jnp.float32).at[:, targets].set(displacement)
    nodes = blocks.reshape(3, N_GX, N_GY, N_GZ, EX, EY, EZ).transpose(0, 1, 4, 2, 5, 3, 6)
    nodes = nodes.reshape(3, N_GX * EX, N_GY * EY, N_GZ * EZ)
    for iteration in range(ITERS):
        padded = jnp.pad(nodes, ((0, 0), (1, 1), (1, 1), (1, 1)))
        moved = spread_all(padded)
        residual = contrast + slopes[0] * moved[0] + slopes[1] * moved[1] + slopes[2] * moved[2]
        image_part = collect_all(masked_slopes * residual[None], False)
        nodes = nodes - (image_part + elastic_weight * elastic_force(padded)) / curvature
    grid = nodes.reshape(3, N_GX, EX, N_GY, EY, N_GZ, EZ).transpose(0, 1, 3, 5, 2, 4, 6)
    return grid.reshape(3, SLOTS, BN)[:, targets]
```

```python
import jax
import jax.numpy as jnp
from jax import lax
from jax.sharding import PartitionSpec as P

ELEM = 4
ITERS = 2
CAP = 2


binomial = (0.0625, 0.25, 0.375, 0.25, 0.0625)
lame_lambda = 1.0
shear_modulus = 0.5
elastic_weight = 2.0
diagonal_shift = 6.0
highest = lax.Precision.HIGHEST


def with_halo(block, sides, width):
    for axis, dim in sides:
        count = lax.axis_size(axis)
        forward = [(i, i + 1) for i in range(count - 1)]
        backward = [(target, source) for source, target in forward]
        low = lax.ppermute(
            lax.slice_in_dim(block, block.shape[dim] - width, None, axis=dim), axis, forward
        )
        high = lax.ppermute(lax.slice_in_dim(block, 0, width, axis=dim), axis, backward)
        block = jnp.concatenate([low, block, high], axis=dim)
    return block


def smooth_axis(volume, dimension):
    length = volume.shape[dimension] - 4
    summed = binomial[0] * lax.slice_in_dim(volume, 0, length, axis=dimension)
    for offset in range(1, 5):
        summed = summed + binomial[offset] * lax.slice_in_dim(
            volume, offset, offset + length, axis=dimension
        )
    return summed


def derive_fields(first_padded, second_padded):
    first_smooth = first_padded
    second_smooth = second_padded
    for dimension in range(3):
        first_smooth = smooth_axis(first_smooth, dimension)
        second_smooth = smooth_axis(second_smooth, dimension)
    average = (first_smooth + second_smooth) * 0.5
    contrast = (second_smooth - first_smooth)[1:-1, 1:-1, 1:-1].astype(jnp.bfloat16)
    slopes = []
    for dimension in range(3):
        length = average.shape[dimension] - 2
        forward_part = lax.slice_in_dim(average, 2, length + 2, axis=dimension)
        backward_part = lax.slice_in_dim(average, 0, length, axis=dimension)
        gradient = (forward_part - backward_part) * 0.5
        for cropped_dim in range(3):
            if cropped_dim != dimension:
                gradient = lax.slice_in_dim(
                    gradient, 1, gradient.shape[cropped_dim] - 1, axis=cropped_dim
                )
        slopes.append(gradient.astype(jnp.bfloat16))
    return jnp.stack([contrast] + slopes)


def interp_axis(volume, dimension, cells_edge):
    length = volume.shape[dimension]
    before = lax.slice_in_dim(volume, 0, length - 1, axis=dimension)
    after = lax.slice_in_dim(volume, 1, length, axis=dimension)
    shape_one = [1] * (volume.ndim + 1)
    shape_one[dimension + 1] = cells_edge
    fraction = (jnp.arange(cells_edge, dtype=jnp.float32) / cells_edge).reshape(shape_one)
    merged = (
        jnp.expand_dims(before, dimension + 1) * (1.0 - fraction)
        + jnp.expand_dims(after, dimension + 1) * fraction
    )
    new_shape = list(volume.shape)
    new_shape[dimension] = (length - 1) * cells_edge
    return merged.reshape(new_shape)


def collect_axis(volume, dimension, cells_edge, squared):
    elements = volume.shape[dimension] // cells_edge
    split_shape = (
        list(volume.shape[:dimension])
        + [elements, cells_edge]
        + list(volume.shape[dimension + 1 :])
    )
    pieces = volume.reshape(split_shape)
    shape_one = [1] * len(split_shape)
    shape_one[dimension + 1] = cells_edge
    fraction = (jnp.arange(cells_edge, dtype=jnp.float32) / cells_edge).reshape(shape_one)
    weight_low = 1.0 - fraction
    weight_high = fraction
    if squared:
        weight_low = weight_low * weight_low
        weight_high = weight_high * weight_high
    low_side = jnp.sum(pieces * weight_low, axis=dimension + 1)
    high_side = jnp.sum(pieces * weight_high, axis=dimension + 1)
    return lax.slice_in_dim(low_side, 1, elements, axis=dimension) + lax.slice_in_dim(
        high_side, 0, elements - 1, axis=dimension
    )


def pair_op(volume, dimension, factor):
    length = volume.shape[dimension]
    return lax.slice_in_dim(volume, 1, length, axis=dimension) + factor * lax.slice_in_dim(
        volume, 0, length - 1, axis=dimension
    )


def cross_pairs(volume, chosen, factor, offset):
    for dimension in range(3):
        volume = pair_op(volume, dimension + offset, factor if dimension == chosen else 1.0)
    return volume


def elastic_force(padded):
    gradients = [cross_pairs(padded, chosen, -1.0, 1) * (1.0 / (4.0 * ELEM)) for chosen in range(3)]
    deform = [
        [gradients[source][target] + (1.0 if target == source else 0.0) for source in range(3)]
        for target in range(3)
    ]
    strain = [
        [
            0.5
            * (
                deform[0][target] * deform[0][source]
                + deform[1][target] * deform[1][source]
                + deform[2][target] * deform[2][source]
            )
            - (0.5 if target == source else 0.0)
            for source in range(3)
        ]
        for target in range(3)
    ]
    trace_strain = strain[0][0] + strain[1][1] + strain[2][2]
    stress = [
        [
            2.0 * shear_modulus * strain[target][source]
            + (lame_lambda * trace_strain if target == source else 0.0)
            for source in range(3)
        ]
        for target in range(3)
    ]
    nominal = [
        [
            deform[target][0] * stress[0][source]
            + deform[target][1] * stress[1][source]
            + deform[target][2] * stress[2][source]
            for source in range(3)
        ]
        for target in range(3)
    ]
    coefficient = ELEM * ELEM / 4.0
    forces = []
    for target in range(3):
        summed = cross_pairs(nominal[target][0], 0, -1.0, 0)
        for source in range(1, 3):
            summed = summed + cross_pairs(nominal[target][source], source, -1.0, 0)
        forces.append(-coefficient * summed)
    return jnp.stack(forces)


def axis_table(nodes_len, cells_edge, squared):
    voxels = (nodes_len - 1) * cells_edge
    column = jnp.arange(voxels, dtype=jnp.int32)
    element = column // cells_edge
    fraction = (column % cells_edge).astype(jnp.float32) / cells_edge
    weight_low = 1.0 - fraction
    weight_high = fraction
    if squared:
        weight_low = weight_low * weight_low
        weight_high = weight_high * weight_high
    node_row = jnp.arange(nodes_len, dtype=jnp.int32)[:, None]
    return jnp.where(node_row == element[None, :], weight_low[None, :], 0.0) + jnp.where(
        node_row == element[None, :] + 1, weight_high[None, :], 0.0
    )


def spread(padded, weights_table):
    shape_all = padded.shape
    stretched = jnp.dot(padded.reshape(-1, shape_all[3]), weights_table, precision=highest)
    stretched = stretched.reshape(shape_all[0], shape_all[1], shape_all[2], weights_table.shape[1])
    stretched = interp_axis(stretched, 1, ELEM)
    return interp_axis(stretched, 2, ELEM)


def collect(volume, table_back, squared):
    shape_all = volume.shape
    reduced = jnp.dot(volume.reshape(-1, shape_all[3]), table_back, precision=highest)
    reduced = reduced.reshape(shape_all[0], shape_all[1], shape_all[2], table_back.shape[1])
    reduced = collect_axis(reduced, 2, ELEM, squared)
    return collect_axis(reduced, 1, ELEM, squared)


def per_device(reference_image, deformed_image, roi_mask, displacement, node_map):
    mask_half = roi_mask.astype(jnp.bfloat16)
    stacked = jnp.stack([reference_image, deformed_image, mask_half])
    padded_images = with_halo(stacked, (("gx", 1), ("gy", 2), ("gz", 3)), 5)
    derived = derive_fields(
        padded_images[0].astype(jnp.float32), padded_images[1].astype(jnp.float32)
    )
    region = padded_images[2][3:-3, 3:-3, 3:-3].astype(jnp.float32)
    contrast = derived[0].astype(jnp.float32)
    slopes = derived[1:].astype(jnp.float32)
    masked_slopes = slopes * region[None]
    nodes_shape = (
        3,
        reference_image.shape[0] // ELEM,
        reference_image.shape[1] // ELEM,
        reference_image.shape[2] // ELEM,
    )
    weights_table = axis_table(nodes_shape[3] + 2, ELEM, False)
    table_back = weights_table[1:-1].T
    table_square = axis_table(nodes_shape[3] + 2, ELEM, True)[1:-1].T
    curvature = collect(masked_slopes * slopes, table_square, True) + diagonal_shift
    members = lax.axis_size(("gy", "gz"))
    blocks = node_map.shape[0]
    block_nodes = displacement.shape[2]
    owner_tile = node_map // blocks
    tile_block = node_map % blocks
    position = jnp.arange(blocks, dtype=jnp.int32)
    earlier = (owner_tile[:, None] == owner_tile[None, :]) & (position[None, :] < position[:, None])
    ranking = jnp.sum(earlier.astype(jnp.int32), axis=1)
    target_slot = owner_tile * CAP + ranking
    packing = (target_slot[:, None] == jnp.arange(members * CAP, dtype=jnp.int32)[None, :]).astype(
        jnp.float32
    )
    labelled = jnp.concatenate(
        [
            displacement,
            jnp.broadcast_to(
                (tile_block + 1).astype(jnp.float32)[None, :, None], (1, blocks, block_nodes)
            ),
        ]
    )
    send_channels = labelled.shape[0]
    send_outgoing = jnp.einsum("cjn,jp->cpn", labelled, packing, precision=highest).reshape(
        send_channels, -1
    )
    send_incoming = lax.all_to_all(
        send_outgoing, ("gy", "gz"), split_axis=1, concat_axis=1, tiled=True
    ).reshape(send_channels, members * CAP, block_nodes)
    received_labels = send_incoming[3, :, 0]
    send_placing = (
        received_labels[:, None] == (position + 1).astype(jnp.float32)[None, :]
    ).astype(jnp.float32)
    tile_values = jnp.einsum(
        "cpn,pk->ckn", send_incoming[:3], send_placing, precision=highest
    ).reshape(nodes_shape)
    for iteration in range(ITERS):
        padded = with_halo(tile_values, (("gx", 1), ("gy", 2), ("gz", 3)), 1)
        moved = spread(padded, weights_table)
        residual = contrast + slopes[0] * moved[0] + slopes[1] * moved[1] + slopes[2] * moved[2]
        image_part = collect(masked_slopes * residual[None], table_back, False)
        force_total = image_part + elastic_weight * elastic_force(padded)
        tile_values = tile_values - force_total / curvature
    final_blocks = tile_values.reshape(3, blocks, block_nodes)
    outgoing = jnp.einsum("ckn,pk->cpn", final_blocks, send_placing, precision=highest).reshape(
        3, -1
    )
    incoming = lax.all_to_all(outgoing, ("gy", "gz"), split_axis=1, concat_axis=1, tiled=True)
    return jnp.einsum(
        "cpn,jp->cjn", incoming.reshape(3, members * CAP, -1), packing, precision=highest
    )


def solution(mesh):
    in_specs = (
        P("gx", "gy", "gz"),
        P("gx", "gy", "gz"),
        P("gx", "gy", "gz"),
        P(None, ("gx", "gy", "gz"), None),
        P(("gx", "gy", "gz")),
    )
    out_specs = P(None, ("gx", "gy", "gz"), None)
    return jax.shard_map(
        per_device, mesh=mesh, in_specs=in_specs, out_specs=out_specs, check_vma=False
    )
```

```python
import jax
import jax.numpy as jnp
from jax import lax
from jax.sharding import PartitionSpec as P

ELEM = 4
ITERS = 2
CAP = 2


binomial = (0.0625, 0.25, 0.375, 0.25, 0.0625)
lame_lambda = 1.0
shear_modulus = 0.5
elastic_weight = 2.0
diagonal_shift = 6.0
highest = lax.Precision.HIGHEST


def with_halo(block, sides, width):
    for axis, dim in sides:
        count = lax.axis_size(axis)
        forward = [(i, i + 1) for i in range(count - 1)]
        backward = [(target, source) for source, target in forward]
        low = lax.ppermute(
            lax.slice_in_dim(block, block.shape[dim] - width, None, axis=dim), axis, forward
        )
        high = lax.ppermute(lax.slice_in_dim(block, 0, width, axis=dim), axis, backward)
        block = jnp.concatenate([low, block, high], axis=dim)
    return block


def with_halo_pair(first, second, sides, widths):
    for axis, first_dim, second_dim in sides:
        count = lax.axis_size(axis)
        forward = [(i, i + 1) for i in range(count - 1)]
        backward = [(target, source) for source, target in forward]
        parts = []
        for block, dim, width in ((first, first_dim, widths[0]), (second, second_dim, widths[1])):
            parts.append(
                (
                    lax.slice_in_dim(block, block.shape[dim] - width, None, axis=dim),
                    lax.slice_in_dim(block, 0, width, axis=dim),
                )
            )
        low_flat = jnp.concatenate([p[0].reshape(-1) for p in parts])
        high_flat = jnp.concatenate([p[1].reshape(-1) for p in parts])
        low_flat = lax.ppermute(low_flat, axis, forward)
        high_flat = lax.ppermute(high_flat, axis, backward)
        split = parts[0][0].size
        pieces = []
        for index, (block, dim) in enumerate(((first, first_dim), (second, second_dim))):
            shape = parts[index][0].shape
            begin, end = (0, split) if index == 0 else (split, low_flat.shape[0])
            low = low_flat[begin:end].reshape(shape)
            high = high_flat[begin:end].reshape(shape)
            pieces.append(jnp.concatenate([low, block, high], axis=dim))
        first, second = pieces
    return first, second


def smooth_axis(volume, dimension):
    length = volume.shape[dimension] - 4
    summed = binomial[0] * lax.slice_in_dim(volume, 0, length, axis=dimension)
    for offset in range(1, 5):
        summed = summed + binomial[offset] * lax.slice_in_dim(
            volume, offset, offset + length, axis=dimension
        )
    return summed


def derive_fields(first_padded, second_padded):
    first_smooth = first_padded
    second_smooth = second_padded
    for dimension in range(3):
        first_smooth = smooth_axis(first_smooth, dimension)
        second_smooth = smooth_axis(second_smooth, dimension)
    average = (first_smooth + second_smooth) * 0.5
    contrast = (second_smooth - first_smooth)[1:-1, 1:-1, 1:-1].astype(jnp.bfloat16)
    slopes = []
    for dimension in range(3):
        length = average.shape[dimension] - 2
        forward_part = lax.slice_in_dim(average, 2, length + 2, axis=dimension)
        backward_part = lax.slice_in_dim(average, 0, length, axis=dimension)
        gradient = (forward_part - backward_part) * 0.5
        for cropped_dim in range(3):
            if cropped_dim != dimension:
                gradient = lax.slice_in_dim(
                    gradient, 1, gradient.shape[cropped_dim] - 1, axis=cropped_dim
                )
        slopes.append(gradient.astype(jnp.bfloat16))
    return jnp.stack([contrast] + slopes)


def interp_axis(volume, dimension, cells_edge):
    length = volume.shape[dimension]
    before = lax.slice_in_dim(volume, 0, length - 1, axis=dimension)
    after = lax.slice_in_dim(volume, 1, length, axis=dimension)
    shape_one = [1] * (volume.ndim + 1)
    shape_one[dimension + 1] = cells_edge
    fraction = (jnp.arange(cells_edge, dtype=jnp.float32) / cells_edge).reshape(shape_one)
    merged = (
        jnp.expand_dims(before, dimension + 1) * (1.0 - fraction)
        + jnp.expand_dims(after, dimension + 1) * fraction
    )
    new_shape = list(volume.shape)
    new_shape[dimension] = (length - 1) * cells_edge
    return merged.reshape(new_shape)


def collect_axis(volume, dimension, cells_edge, squared):
    elements = volume.shape[dimension] // cells_edge
    split_shape = (
        list(volume.shape[:dimension])
        + [elements, cells_edge]
        + list(volume.shape[dimension + 1 :])
    )
    pieces = volume.reshape(split_shape)
    shape_one = [1] * len(split_shape)
    shape_one[dimension + 1] = cells_edge
    fraction = (jnp.arange(cells_edge, dtype=jnp.float32) / cells_edge).reshape(shape_one)
    weight_low = 1.0 - fraction
    weight_high = fraction
    if squared:
        weight_low = weight_low * weight_low
        weight_high = weight_high * weight_high
    low_side = jnp.sum(pieces * weight_low, axis=dimension + 1)
    high_side = jnp.sum(pieces * weight_high, axis=dimension + 1)
    return lax.slice_in_dim(low_side, 1, elements, axis=dimension) + lax.slice_in_dim(
        high_side, 0, elements - 1, axis=dimension
    )


def pair_op(volume, dimension, factor):
    length = volume.shape[dimension]
    return lax.slice_in_dim(volume, 1, length, axis=dimension) + factor * lax.slice_in_dim(
        volume, 0, length - 1, axis=dimension
    )


def cross_pairs(volume, chosen, factor, offset):
    for dimension in range(3):
        volume = pair_op(volume, dimension + offset, factor if dimension == chosen else 1.0)
    return volume


def elastic_force(padded):
    gradients = [cross_pairs(padded, chosen, -1.0, 1) * (1.0 / (4.0 * ELEM)) for chosen in range(3)]
    deform = [
        [gradients[source][target] + (1.0 if target == source else 0.0) for source in range(3)]
        for target in range(3)
    ]
    strain = [
        [
            0.5
            * (
                deform[0][target] * deform[0][source]
                + deform[1][target] * deform[1][source]
                + deform[2][target] * deform[2][source]
            )
            - (0.5 if target == source else 0.0)
            for source in range(3)
        ]
        for target in range(3)
    ]
    trace_strain = strain[0][0] + strain[1][1] + strain[2][2]
    stress = [
        [
            2.0 * shear_modulus * strain[target][source]
            + (lame_lambda * trace_strain if target == source else 0.0)
            for source in range(3)
        ]
        for target in range(3)
    ]
    nominal = [
        [
            deform[target][0] * stress[0][source]
            + deform[target][1] * stress[1][source]
            + deform[target][2] * stress[2][source]
            for source in range(3)
        ]
        for target in range(3)
    ]
    coefficient = ELEM * ELEM / 4.0
    forces = []
    for target in range(3):
        summed = cross_pairs(nominal[target][0], 0, -1.0, 0)
        for source in range(1, 3):
            summed = summed + cross_pairs(nominal[target][source], source, -1.0, 0)
        forces.append(-coefficient * summed)
    return jnp.stack(forces)


def axis_table(nodes_len, cells_edge, squared):
    voxels = (nodes_len - 1) * cells_edge
    column = jnp.arange(voxels, dtype=jnp.int32)
    element = column // cells_edge
    fraction = (column % cells_edge).astype(jnp.float32) / cells_edge
    weight_low = 1.0 - fraction
    weight_high = fraction
    if squared:
        weight_low = weight_low * weight_low
        weight_high = weight_high * weight_high
    node_row = jnp.arange(nodes_len, dtype=jnp.int32)[:, None]
    return jnp.where(node_row == element[None, :], weight_low[None, :], 0.0) + jnp.where(
        node_row == element[None, :] + 1, weight_high[None, :], 0.0
    )


def spread(padded, weights_table):
    shape_all = padded.shape
    stretched = jnp.dot(padded.reshape(-1, shape_all[3]), weights_table, precision=highest)
    stretched = stretched.reshape(shape_all[0], shape_all[1], shape_all[2], weights_table.shape[1])
    stretched = interp_axis(stretched, 1, ELEM)
    return interp_axis(stretched, 2, ELEM)


def collect(volume, table_back, squared):
    shape_all = volume.shape
    reduced = jnp.dot(volume.reshape(-1, shape_all[3]), table_back, precision=highest)
    reduced = reduced.reshape(shape_all[0], shape_all[1], shape_all[2], table_back.shape[1])
    reduced = collect_axis(reduced, 2, ELEM, squared)
    return collect_axis(reduced, 1, ELEM, squared)


def per_device(reference_image, deformed_image, roi_mask, displacement, node_map):
    stacked = jnp.stack(
        [
            reference_image.astype(jnp.float32),
            deformed_image.astype(jnp.float32),
            roi_mask.astype(jnp.float32),
        ]
    )
    nodes_shape = (
        3,
        reference_image.shape[0] // ELEM,
        reference_image.shape[1] // ELEM,
        reference_image.shape[2] // ELEM,
    )
    weights_table = axis_table(nodes_shape[3] + 2, ELEM, False)
    table_back = weights_table[1:-1].T
    table_square = axis_table(nodes_shape[3] + 2, ELEM, True)[1:-1].T
    members = lax.axis_size(("gy", "gz"))
    blocks = node_map.shape[0]
    block_nodes = displacement.shape[2]
    owner_tile = node_map // blocks
    tile_block = node_map % blocks
    position = jnp.arange(blocks, dtype=jnp.int32)
    earlier = (owner_tile[:, None] == owner_tile[None, :]) & (position[None, :] < position[:, None])
    ranking = jnp.sum(earlier.astype(jnp.int32), axis=1)
    target_slot = owner_tile * CAP + ranking
    packing = (target_slot[:, None] == jnp.arange(members * CAP, dtype=jnp.int32)[None, :]).astype(
        jnp.float32
    )
    labelled = jnp.concatenate(
        [
            displacement,
            jnp.broadcast_to(
                (tile_block + 1).astype(jnp.float32)[None, :, None], (1, blocks, block_nodes)
            ),
        ]
    )
    send_channels = labelled.shape[0]
    send_outgoing = jnp.einsum("cjn,jp->cpn", labelled, packing, precision=highest).reshape(
        send_channels, -1
    )
    send_incoming = lax.all_to_all(
        send_outgoing, ("gy", "gz"), split_axis=1, concat_axis=1, tiled=True
    ).reshape(send_channels, members * CAP, block_nodes)
    received_labels = send_incoming[3, :, 0]
    send_placing = (
        received_labels[:, None] == (position + 1).astype(jnp.float32)[None, :]
    ).astype(jnp.float32)
    tile_values = jnp.einsum(
        "cpn,pk->ckn", send_incoming[:3], send_placing, precision=highest
    ).reshape(nodes_shape)
    padded_images, first_padded = with_halo_pair(
        stacked, tile_values, (("gx", 1, 1), ("gy", 2, 2), ("gz", 3, 3)), (5, 1)
    )
    derived = derive_fields(padded_images[0], padded_images[1])
    region = padded_images[2][3:-3, 3:-3, 3:-3]
    contrast = derived[0].astype(jnp.float32)
    slopes = derived[1:].astype(jnp.float32)
    masked_slopes = slopes * region[None]
    curvature = collect(masked_slopes * slopes, table_square, True) + diagonal_shift
    for iteration in range(ITERS):
        if iteration == 0:
            padded = first_padded
        else:
            padded = with_halo(tile_values, (("gx", 1), ("gy", 2), ("gz", 3)), 1)
        moved = spread(padded, weights_table)
        residual = contrast + slopes[0] * moved[0] + slopes[1] * moved[1] + slopes[2] * moved[2]
        image_part = collect(masked_slopes * residual[None], table_back, False)
        force_total = image_part + elastic_weight * elastic_force(padded)
        tile_values = tile_values - force_total / curvature
    final_blocks = tile_values.reshape(3, blocks, block_nodes)
    outgoing = jnp.einsum("ckn,pk->cpn", final_blocks, send_placing, precision=highest).reshape(
        3, -1
    )
    incoming = lax.all_to_all(outgoing, ("gy", "gz"), split_axis=1, concat_axis=1, tiled=True)
    return jnp.einsum(
        "cpn,jp->cjn", incoming.reshape(3, members * CAP, -1), packing, precision=highest
    )


def solution(mesh):
    in_specs = (
        P("gx", "gy", "gz"),
        P("gx", "gy", "gz"),
        P("gx", "gy", "gz"),
        P(None, ("gx", "gy", "gz"), None),
        P(("gx", "gy", "gz")),
    )
    out_specs = P(None, ("gx", "gy", "gz"), None)
    return jax.shard_map(
        per_device, mesh=mesh, in_specs=in_specs, out_specs=out_specs, check_vma=False
    )
```

```python
import jax
import jax.numpy as jnp
from jax import lax
from jax.sharding import PartitionSpec as P

ELEM = 4
ITERS = 2
CAP = 2


binomial = (0.0625, 0.25, 0.375, 0.25, 0.0625)
lame_lambda = 1.0
shear_modulus = 0.5
elastic_weight = 2.0
diagonal_shift = 6.0
highest = lax.Precision.HIGHEST


def with_halo(block, sides, width):
    for axis, dim in sides:
        count = lax.axis_size(axis)
        forward = [(i, i + 1) for i in range(count - 1)]
        backward = [(target, source) for source, target in forward]
        low = lax.ppermute(
            lax.slice_in_dim(block, block.shape[dim] - width, None, axis=dim), axis, forward
        )
        high = lax.ppermute(lax.slice_in_dim(block, 0, width, axis=dim), axis, backward)
        block = jnp.concatenate([low, block, high], axis=dim)
    return block


def with_halo_pair(first, second, sides, widths):
    for axis, first_dim, second_dim in sides:
        count = lax.axis_size(axis)
        forward = [(i, i + 1) for i in range(count - 1)]
        backward = [(target, source) for source, target in forward]
        parts = []
        for block, dim, width in ((first, first_dim, widths[0]), (second, second_dim, widths[1])):
            parts.append(
                (
                    lax.slice_in_dim(block, block.shape[dim] - width, None, axis=dim),
                    lax.slice_in_dim(block, 0, width, axis=dim),
                )
            )
        low_flat = jnp.concatenate([p[0].reshape(-1) for p in parts])
        high_flat = jnp.concatenate([p[1].reshape(-1) for p in parts])
        low_flat = lax.ppermute(low_flat, axis, forward)
        high_flat = lax.ppermute(high_flat, axis, backward)
        split = parts[0][0].size
        pieces = []
        for index, (block, dim) in enumerate(((first, first_dim), (second, second_dim))):
            shape = parts[index][0].shape
            begin, end = (0, split) if index == 0 else (split, low_flat.shape[0])
            low = low_flat[begin:end].reshape(shape)
            high = high_flat[begin:end].reshape(shape)
            pieces.append(jnp.concatenate([low, block, high], axis=dim))
        first, second = pieces
    return first, second


def smooth_axis(volume, dimension):
    length = volume.shape[dimension] - 4
    summed = binomial[0] * lax.slice_in_dim(volume, 0, length, axis=dimension)
    for offset in range(1, 5):
        summed = summed + binomial[offset] * lax.slice_in_dim(
            volume, offset, offset + length, axis=dimension
        )
    return summed


def derive_fields(first_padded, second_padded):
    first_smooth = first_padded
    second_smooth = second_padded
    for dimension in range(3):
        first_smooth = smooth_axis(first_smooth, dimension)
        second_smooth = smooth_axis(second_smooth, dimension)
    average = (first_smooth + second_smooth) * 0.5
    contrast = (second_smooth - first_smooth)[1:-1, 1:-1, 1:-1].astype(jnp.bfloat16)
    slopes = []
    for dimension in range(3):
        length = average.shape[dimension] - 2
        forward_part = lax.slice_in_dim(average, 2, length + 2, axis=dimension)
        backward_part = lax.slice_in_dim(average, 0, length, axis=dimension)
        gradient = (forward_part - backward_part) * 0.5
        for cropped_dim in range(3):
            if cropped_dim != dimension:
                gradient = lax.slice_in_dim(
                    gradient, 1, gradient.shape[cropped_dim] - 1, axis=cropped_dim
                )
        slopes.append(gradient.astype(jnp.bfloat16))
    return jnp.stack([contrast] + slopes)


def interp_axis(volume, dimension, cells_edge):
    length = volume.shape[dimension]
    before = lax.slice_in_dim(volume, 0, length - 1, axis=dimension)
    after = lax.slice_in_dim(volume, 1, length, axis=dimension)
    shape_one = [1] * (volume.ndim + 1)
    shape_one[dimension + 1] = cells_edge
    fraction = (jnp.arange(cells_edge, dtype=jnp.float32) / cells_edge).reshape(shape_one)
    merged = (
        jnp.expand_dims(before, dimension + 1) * (1.0 - fraction)
        + jnp.expand_dims(after, dimension + 1) * fraction
    )
    new_shape = list(volume.shape)
    new_shape[dimension] = (length - 1) * cells_edge
    return merged.reshape(new_shape)


def collect_axis(volume, dimension, cells_edge, squared):
    elements = volume.shape[dimension] // cells_edge
    split_shape = (
        list(volume.shape[:dimension])
        + [elements, cells_edge]
        + list(volume.shape[dimension + 1 :])
    )
    pieces = volume.reshape(split_shape)
    shape_one = [1] * len(split_shape)
    shape_one[dimension + 1] = cells_edge
    fraction = (jnp.arange(cells_edge, dtype=jnp.float32) / cells_edge).reshape(shape_one)
    weight_low = 1.0 - fraction
    weight_high = fraction
    if squared:
        weight_low = weight_low * weight_low
        weight_high = weight_high * weight_high
    low_side = jnp.sum(pieces * weight_low, axis=dimension + 1)
    high_side = jnp.sum(pieces * weight_high, axis=dimension + 1)
    return lax.slice_in_dim(low_side, 1, elements, axis=dimension) + lax.slice_in_dim(
        high_side, 0, elements - 1, axis=dimension
    )


def pair_op(volume, dimension, factor):
    length = volume.shape[dimension]
    return lax.slice_in_dim(volume, 1, length, axis=dimension) + factor * lax.slice_in_dim(
        volume, 0, length - 1, axis=dimension
    )


def cross_pairs(volume, chosen, factor, offset):
    for dimension in range(3):
        volume = pair_op(volume, dimension + offset, factor if dimension == chosen else 1.0)
    return volume


def elastic_force(padded):
    gradients = [cross_pairs(padded, chosen, -1.0, 1) * (1.0 / (4.0 * ELEM)) for chosen in range(3)]
    deform = [
        [gradients[source][target] + (1.0 if target == source else 0.0) for source in range(3)]
        for target in range(3)
    ]
    strain = [
        [
            0.5
            * (
                deform[0][target] * deform[0][source]
                + deform[1][target] * deform[1][source]
                + deform[2][target] * deform[2][source]
            )
            - (0.5 if target == source else 0.0)
            for source in range(3)
        ]
        for target in range(3)
    ]
    trace_strain = strain[0][0] + strain[1][1] + strain[2][2]
    stress = [
        [
            2.0 * shear_modulus * strain[target][source]
            + (lame_lambda * trace_strain if target == source else 0.0)
            for source in range(3)
        ]
        for target in range(3)
    ]
    nominal = [
        [
            deform[target][0] * stress[0][source]
            + deform[target][1] * stress[1][source]
            + deform[target][2] * stress[2][source]
            for source in range(3)
        ]
        for target in range(3)
    ]
    coefficient = ELEM * ELEM / 4.0
    forces = []
    for target in range(3):
        summed = cross_pairs(nominal[target][0], 0, -1.0, 0)
        for source in range(1, 3):
            summed = summed + cross_pairs(nominal[target][source], source, -1.0, 0)
        forces.append(-coefficient * summed)
    return jnp.stack(forces)


def axis_table(nodes_len, cells_edge, squared):
    voxels = (nodes_len - 1) * cells_edge
    column = jnp.arange(voxels, dtype=jnp.int32)
    element = column // cells_edge
    fraction = (column % cells_edge).astype(jnp.float32) / cells_edge
    weight_low = 1.0 - fraction
    weight_high = fraction
    if squared:
        weight_low = weight_low * weight_low
        weight_high = weight_high * weight_high
    node_row = jnp.arange(nodes_len, dtype=jnp.int32)[:, None]
    return jnp.where(node_row == element[None, :], weight_low[None, :], 0.0) + jnp.where(
        node_row == element[None, :] + 1, weight_high[None, :], 0.0
    )


def spread(padded, weights_table):
    shape_all = padded.shape
    stretched = jnp.dot(padded.reshape(-1, shape_all[3]), weights_table, precision=highest)
    stretched = stretched.reshape(shape_all[0], shape_all[1], shape_all[2], weights_table.shape[1])
    stretched = interp_axis(stretched, 1, ELEM)
    return interp_axis(stretched, 2, ELEM)


def collect(volume, table_back, squared):
    shape_all = volume.shape
    reduced = jnp.dot(volume.reshape(-1, shape_all[3]), table_back, precision=highest)
    reduced = reduced.reshape(shape_all[0], shape_all[1], shape_all[2], table_back.shape[1])
    reduced = collect_axis(reduced, 2, ELEM, squared)
    return collect_axis(reduced, 1, ELEM, squared)


NEIGHBOURS = [(0, 0)] + [(ry, rz) for ry in (-1, 0, 1) for rz in (-1, 0, 1) if (ry, rz) != (0, 0)]
HALO_CAP = 10


def per_device(reference_image, deformed_image, roi_mask, displacement, node_map):
    stacked = jnp.stack([reference_image, deformed_image, roi_mask.astype(jnp.bfloat16)])
    stacked = with_halo(stacked, (("gy", 2), ("gz", 3)), 5).astype(jnp.float32)
    nodes_shape = (
        3,
        reference_image.shape[0] // ELEM,
        reference_image.shape[1] // ELEM,
        reference_image.shape[2] // ELEM,
    )
    _, ex, ey, ez = nodes_shape
    weights_table = axis_table(ez + 2, ELEM, False)
    table_back = weights_table[1:-1].T
    table_square = axis_table(ez + 2, ELEM, True)[1:-1].T
    size_y = lax.axis_size("gy")
    size_z = lax.axis_size("gz")
    members = size_y * size_z
    blocks = node_map.shape[0]
    block_nodes = displacement.shape[2]
    zchunks = ez // block_nodes
    owner_tile = node_map // blocks
    tile_block = node_map % blocks
    tile_y = owner_tile // size_z
    tile_z = owner_tile % size_z
    block_y = (tile_block // zchunks) % ey
    block_zc = tile_block % zchunks
    dests, valids, labels = [], [], []
    for index, (ry, rz) in enumerate(NEIGHBOURS):
        dest_y = tile_y - ry
        dest_z = tile_z - rz
        valid = (dest_y >= 0) & (dest_y < size_y) & (dest_z >= 0) & (dest_z < size_z)
        if ry == -1:
            valid = valid & (block_y == ey - 1)
        elif ry == 1:
            valid = valid & (block_y == 0)
        if rz == -1:
            valid = valid & (block_zc == zchunks - 1)
        elif rz == 1:
            valid = valid & (block_zc == 0)
        dests.append(dest_y * size_z + dest_z)
        valids.append(valid)
        labels.append(index * blocks + tile_block + 1)
    cand_dest = jnp.concatenate(dests)
    cand_valid = jnp.concatenate(valids)
    cand_label = jnp.concatenate(labels).astype(jnp.float32)
    count = cand_dest.shape[0]
    order = jnp.arange(count, dtype=jnp.int32)
    earlier = (
        (cand_dest[:, None] == cand_dest[None, :])
        & cand_valid[None, :]
        & (order[None, :] < order[:, None])
    )
    ranking = jnp.sum(earlier.astype(jnp.int32), axis=1)
    target_slot = jnp.where(cand_valid, cand_dest * HALO_CAP + ranking, -1)
    packing = (
        target_slot[:, None] == jnp.arange(members * HALO_CAP, dtype=jnp.int32)[None, :]
    ).astype(jnp.float32)
    cand_data = jnp.concatenate(
        [
            jnp.concatenate([displacement] * len(NEIGHBOURS), axis=1),
            jnp.broadcast_to(cand_label[None, :, None], (1, count, block_nodes)),
        ]
    )
    send_channels = cand_data.shape[0]
    send_outgoing = jnp.einsum("cjn,jp->cpn", cand_data, packing, precision=highest).reshape(
        send_channels, -1
    )
    send_incoming = lax.all_to_all(
        send_outgoing, ("gy", "gz"), split_axis=1, concat_axis=1, tiled=True
    ).reshape(send_channels, members * HALO_CAP, block_nodes)
    received_labels = send_incoming[3, :, 0]
    placing = (
        received_labels[:, None] == jnp.arange(1, count + 1, dtype=jnp.float32)[None, :]
    ).astype(jnp.float32)
    around = jnp.einsum("cpn,pk->ckn", send_incoming[:3], placing, precision=highest).reshape(
        3, len(NEIGHBOURS), ex, ey, ez
    )

    def near(ry, rz):
        return around[:, NEIGHBOURS.index((ry, rz))]

    tile_values = near(0, 0)
    middle = jnp.concatenate(
        [near(0, -1)[..., ez - 1 :], tile_values, near(0, 1)[..., :1]], axis=3
    )
    low_row = jnp.concatenate(
        [
            near(-1, -1)[:, :, ey - 1 :, ez - 1 :],
            near(-1, 0)[:, :, ey - 1 :, :],
            near(-1, 1)[:, :, ey - 1 :, :1],
        ],
        axis=3,
    )
    high_row = jnp.concatenate(
        [near(1, -1)[:, :, :1, ez - 1 :], near(1, 0)[:, :, :1, :], near(1, 1)[:, :, :1, :1]],
        axis=3,
    )
    extended = jnp.concatenate([low_row, middle, high_row], axis=2)
    padded_images, first_padded = with_halo_pair(stacked, extended, (("gx", 1, 1),), (5, 1))
    derived = derive_fields(padded_images[0], padded_images[1])
    region = padded_images[2][3:-3, 3:-3, 3:-3]
    contrast = derived[0].astype(jnp.float32)
    slopes = derived[1:].astype(jnp.float32)
    masked_slopes = slopes * region[None]
    curvature = collect(masked_slopes * slopes, table_square, True) + diagonal_shift
    for iteration in range(ITERS):
        if iteration == 0:
            padded = first_padded
        else:
            padded = with_halo(tile_values, (("gx", 1), ("gy", 2), ("gz", 3)), 1)
        moved = spread(padded, weights_table)
        residual = contrast + slopes[0] * moved[0] + slopes[1] * moved[1] + slopes[2] * moved[2]
        image_part = collect(masked_slopes * residual[None], table_back, False)
        force_total = image_part + elastic_weight * elastic_force(padded)
        tile_values = tile_values - force_total / curvature
    final_blocks = tile_values.reshape(3, blocks, block_nodes)
    own_labels = received_labels.reshape(members, HALO_CAP)[:, :CAP].reshape(-1)
    position = jnp.arange(blocks, dtype=jnp.int32)
    back_placing = (own_labels[:, None] == (position + 1).astype(jnp.float32)[None, :]).astype(
        jnp.float32
    )
    outgoing = jnp.einsum("ckn,pk->cpn", final_blocks, back_placing, precision=highest).reshape(
        3, -1
    )
    incoming = lax.all_to_all(outgoing, ("gy", "gz"), split_axis=1, concat_axis=1, tiled=True)
    own_slot = owner_tile * CAP + ranking[:blocks]
    back_packing = (
        own_slot[:, None] == jnp.arange(members * CAP, dtype=jnp.int32)[None, :]
    ).astype(jnp.float32)
    return jnp.einsum(
        "cpn,jp->cjn", incoming.reshape(3, members * CAP, -1), back_packing, precision=highest
    )


def solution(mesh):
    in_specs = (
        P("gx", "gy", "gz"),
        P("gx", "gy", "gz"),
        P("gx", "gy", "gz"),
        P(None, ("gx", "gy", "gz"), None),
        P(("gx", "gy", "gz")),
    )
    out_specs = P(None, ("gx", "gy", "gz"), None)
    return jax.shard_map(
        per_device, mesh=mesh, in_specs=in_specs, out_specs=out_specs, check_vma=False
    )
```

```python
import jax
import jax.numpy as jnp
from jax import lax
from jax.sharding import PartitionSpec as P

ELEM = 4
ITERS = 2
CAP = 2


binomial = (0.0625, 0.25, 0.375, 0.25, 0.0625)
lame_lambda = 1.0
shear_modulus = 0.5
elastic_weight = 2.0
diagonal_shift = 6.0
highest = lax.Precision.HIGHEST


def with_halo(block, sides, width):
    for axis, dim in sides:
        count = lax.axis_size(axis)
        forward = [(i, i + 1) for i in range(count - 1)]
        backward = [(target, source) for source, target in forward]
        low = lax.ppermute(
            lax.slice_in_dim(block, block.shape[dim] - width, None, axis=dim), axis, forward
        )
        high = lax.ppermute(lax.slice_in_dim(block, 0, width, axis=dim), axis, backward)
        block = jnp.concatenate([low, block, high], axis=dim)
    return block


def with_halo_pair(first, second, sides, widths):
    for axis, first_dim, second_dim in sides:
        count = lax.axis_size(axis)
        forward = [(i, i + 1) for i in range(count - 1)]
        backward = [(target, source) for source, target in forward]
        parts = []
        for block, dim, width in ((first, first_dim, widths[0]), (second, second_dim, widths[1])):
            parts.append(
                (
                    lax.slice_in_dim(block, block.shape[dim] - width, None, axis=dim),
                    lax.slice_in_dim(block, 0, width, axis=dim),
                )
            )
        low_flat = jnp.concatenate([p[0].reshape(-1) for p in parts])
        high_flat = jnp.concatenate([p[1].reshape(-1) for p in parts])
        low_flat = lax.ppermute(low_flat, axis, forward)
        high_flat = lax.ppermute(high_flat, axis, backward)
        split = parts[0][0].size
        pieces = []
        for index, (block, dim) in enumerate(((first, first_dim), (second, second_dim))):
            shape = parts[index][0].shape
            begin, end = (0, split) if index == 0 else (split, low_flat.shape[0])
            low = low_flat[begin:end].reshape(shape)
            high = high_flat[begin:end].reshape(shape)
            pieces.append(jnp.concatenate([low, block, high], axis=dim))
        first, second = pieces
    return first, second


def smooth_axis(volume, dimension):
    length = volume.shape[dimension] - 4
    summed = binomial[0] * lax.slice_in_dim(volume, 0, length, axis=dimension)
    for offset in range(1, 5):
        summed = summed + binomial[offset] * lax.slice_in_dim(
            volume, offset, offset + length, axis=dimension
        )
    return summed


def derive_fields(first_padded, second_padded):
    first_smooth = first_padded
    second_smooth = second_padded
    for dimension in range(3):
        first_smooth = smooth_axis(first_smooth, dimension)
        second_smooth = smooth_axis(second_smooth, dimension)
    average = (first_smooth + second_smooth) * 0.5
    contrast = (second_smooth - first_smooth)[1:-1, 1:-1, 1:-1].astype(jnp.bfloat16)
    slopes = []
    for dimension in range(3):
        length = average.shape[dimension] - 2
        forward_part = lax.slice_in_dim(average, 2, length + 2, axis=dimension)
        backward_part = lax.slice_in_dim(average, 0, length, axis=dimension)
        gradient = (forward_part - backward_part) * 0.5
        for cropped_dim in range(3):
            if cropped_dim != dimension:
                gradient = lax.slice_in_dim(
                    gradient, 1, gradient.shape[cropped_dim] - 1, axis=cropped_dim
                )
        slopes.append(gradient.astype(jnp.bfloat16))
    return jnp.stack([contrast] + slopes)


def interp_axis(volume, dimension, cells_edge):
    length = volume.shape[dimension]
    before = lax.slice_in_dim(volume, 0, length - 1, axis=dimension)
    after = lax.slice_in_dim(volume, 1, length, axis=dimension)
    shape_one = [1] * (volume.ndim + 1)
    shape_one[dimension + 1] = cells_edge
    fraction = (jnp.arange(cells_edge, dtype=jnp.float32) / cells_edge).reshape(shape_one)
    merged = (
        jnp.expand_dims(before, dimension + 1) * (1.0 - fraction)
        + jnp.expand_dims(after, dimension + 1) * fraction
    )
    new_shape = list(volume.shape)
    new_shape[dimension] = (length - 1) * cells_edge
    return merged.reshape(new_shape)


def collect_axis(volume, dimension, cells_edge, squared):
    elements = volume.shape[dimension] // cells_edge
    split_shape = (
        list(volume.shape[:dimension])
        + [elements, cells_edge]
        + list(volume.shape[dimension + 1 :])
    )
    pieces = volume.reshape(split_shape)
    shape_one = [1] * len(split_shape)
    shape_one[dimension + 1] = cells_edge
    fraction = (jnp.arange(cells_edge, dtype=jnp.float32) / cells_edge).reshape(shape_one)
    weight_low = 1.0 - fraction
    weight_high = fraction
    if squared:
        weight_low = weight_low * weight_low
        weight_high = weight_high * weight_high
    low_side = jnp.sum(pieces * weight_low, axis=dimension + 1)
    high_side = jnp.sum(pieces * weight_high, axis=dimension + 1)
    return lax.slice_in_dim(low_side, 1, elements, axis=dimension) + lax.slice_in_dim(
        high_side, 0, elements - 1, axis=dimension
    )


def pair_op(volume, dimension, factor):
    length = volume.shape[dimension]
    return lax.slice_in_dim(volume, 1, length, axis=dimension) + factor * lax.slice_in_dim(
        volume, 0, length - 1, axis=dimension
    )


def cross_pairs(volume, chosen, factor, offset):
    for dimension in range(3):
        volume = pair_op(volume, dimension + offset, factor if dimension == chosen else 1.0)
    return volume


def elastic_force(padded):
    gradients = [cross_pairs(padded, chosen, -1.0, 1) * (1.0 / (4.0 * ELEM)) for chosen in range(3)]
    deform = [
        [gradients[source][target] + (1.0 if target == source else 0.0) for source in range(3)]
        for target in range(3)
    ]
    strain = [
        [
            0.5
            * (
                deform[0][target] * deform[0][source]
                + deform[1][target] * deform[1][source]
                + deform[2][target] * deform[2][source]
            )
            - (0.5 if target == source else 0.0)
            for source in range(3)
        ]
        for target in range(3)
    ]
    trace_strain = strain[0][0] + strain[1][1] + strain[2][2]
    stress = [
        [
            2.0 * shear_modulus * strain[target][source]
            + (lame_lambda * trace_strain if target == source else 0.0)
            for source in range(3)
        ]
        for target in range(3)
    ]
    nominal = [
        [
            deform[target][0] * stress[0][source]
            + deform[target][1] * stress[1][source]
            + deform[target][2] * stress[2][source]
            for source in range(3)
        ]
        for target in range(3)
    ]
    coefficient = ELEM * ELEM / 4.0
    forces = []
    for target in range(3):
        summed = cross_pairs(nominal[target][0], 0, -1.0, 0)
        for source in range(1, 3):
            summed = summed + cross_pairs(nominal[target][source], source, -1.0, 0)
        forces.append(-coefficient * summed)
    return jnp.stack(forces)


def axis_table(nodes_len, cells_edge, squared):
    voxels = (nodes_len - 1) * cells_edge
    column = jnp.arange(voxels, dtype=jnp.int32)
    element = column // cells_edge
    fraction = (column % cells_edge).astype(jnp.float32) / cells_edge
    weight_low = 1.0 - fraction
    weight_high = fraction
    if squared:
        weight_low = weight_low * weight_low
        weight_high = weight_high * weight_high
    node_row = jnp.arange(nodes_len, dtype=jnp.int32)[:, None]
    return jnp.where(node_row == element[None, :], weight_low[None, :], 0.0) + jnp.where(
        node_row == element[None, :] + 1, weight_high[None, :], 0.0
    )


def spread(padded, weights_table):
    shape_all = padded.shape
    stretched = jnp.dot(padded.reshape(-1, shape_all[3]), weights_table, precision=highest)
    stretched = stretched.reshape(shape_all[0], shape_all[1], shape_all[2], weights_table.shape[1])
    stretched = interp_axis(stretched, 1, ELEM)
    return interp_axis(stretched, 2, ELEM)


def collect(volume, table_back, squared):
    shape_all = volume.shape
    reduced = jnp.dot(volume.reshape(-1, shape_all[3]), table_back, precision=highest)
    reduced = reduced.reshape(shape_all[0], shape_all[1], shape_all[2], table_back.shape[1])
    reduced = collect_axis(reduced, 2, ELEM, squared)
    return collect_axis(reduced, 1, ELEM, squared)


NEIGHBOURS = [(0, 0)] + [(ry, rz) for ry in (-1, 0, 1) for rz in (-1, 0, 1) if (ry, rz) != (0, 0)]
HALO_CAP = 10


def per_device(reference_image, deformed_image, roi_mask, displacement, node_map):
    stacked = jnp.stack([reference_image, deformed_image, roi_mask.astype(jnp.bfloat16)])
    padded_images = with_halo(stacked, (("gy", 2), ("gz", 3), ("gx", 1)), 5).astype(jnp.float32)
    nodes_shape = (
        3,
        reference_image.shape[0] // ELEM,
        reference_image.shape[1] // ELEM,
        reference_image.shape[2] // ELEM,
    )
    _, ex, ey, ez = nodes_shape
    weights_table = axis_table(ez + 2, ELEM, False)
    table_back = weights_table[1:-1].T
    table_square = axis_table(ez + 2, ELEM, True)[1:-1].T
    size_y = lax.axis_size("gy")
    size_z = lax.axis_size("gz")
    members = size_y * size_z
    blocks = node_map.shape[0]
    block_nodes = displacement.shape[2]
    zchunks = ez // block_nodes
    owner_tile = node_map // blocks
    tile_block = node_map % blocks
    tile_y = owner_tile // size_z
    tile_z = owner_tile % size_z
    block_y = (tile_block // zchunks) % ey
    block_zc = tile_block % zchunks
    dests, valids, labels = [], [], []
    for index, (ry, rz) in enumerate(NEIGHBOURS):
        dest_y = tile_y - ry
        dest_z = tile_z - rz
        valid = (dest_y >= 0) & (dest_y < size_y) & (dest_z >= 0) & (dest_z < size_z)
        if ry == -1:
            valid = valid & (block_y == ey - 1)
        elif ry == 1:
            valid = valid & (block_y == 0)
        if rz == -1:
            valid = valid & (block_zc == zchunks - 1)
        elif rz == 1:
            valid = valid & (block_zc == 0)
        dests.append(dest_y * size_z + dest_z)
        valids.append(valid)
        labels.append(index * blocks + tile_block + 1)
    cand_dest = jnp.concatenate(dests)
    cand_valid = jnp.concatenate(valids)
    cand_label = jnp.concatenate(labels).astype(jnp.float32)
    count = cand_dest.shape[0]
    order = jnp.arange(count, dtype=jnp.int32)
    earlier = (
        (cand_dest[:, None] == cand_dest[None, :])
        & cand_valid[None, :]
        & (order[None, :] < order[:, None])
    )
    ranking = jnp.sum(earlier.astype(jnp.int32), axis=1)
    target_slot = jnp.where(cand_valid, cand_dest * HALO_CAP + ranking, -1)
    packing = (
        target_slot[:, None] == jnp.arange(members * HALO_CAP, dtype=jnp.int32)[None, :]
    ).astype(jnp.float32)
    cand_data = jnp.concatenate(
        [
            jnp.concatenate([displacement] * len(NEIGHBOURS), axis=1),
            jnp.broadcast_to(cand_label[None, :, None], (1, count, block_nodes)),
        ]
    )
    send_channels = cand_data.shape[0]
    send_outgoing = jnp.einsum("cjn,jp->cpn", cand_data, packing, precision=highest).reshape(
        send_channels, -1
    )
    send_incoming = lax.all_to_all(
        send_outgoing, ("gy", "gz"), split_axis=1, concat_axis=1, tiled=True
    ).reshape(send_channels, members * HALO_CAP, block_nodes)
    received_labels = send_incoming[3, :, 0]
    placing = (
        received_labels[:, None] == jnp.arange(1, count + 1, dtype=jnp.float32)[None, :]
    ).astype(jnp.float32)
    around = jnp.einsum("cpn,pk->ckn", send_incoming[:3], placing, precision=highest).reshape(
        3, len(NEIGHBOURS), ex, ey, ez
    )

    def near(ry, rz):
        return around[:, NEIGHBOURS.index((ry, rz))]

    tile_values = near(0, 0)
    middle = jnp.concatenate(
        [near(0, -1)[..., ez - 1 :], tile_values, near(0, 1)[..., :1]], axis=3
    )
    low_row = jnp.concatenate(
        [
            near(-1, -1)[:, :, ey - 1 :, ez - 1 :],
            near(-1, 0)[:, :, ey - 1 :, :],
            near(-1, 1)[:, :, ey - 1 :, :1],
        ],
        axis=3,
    )
    high_row = jnp.concatenate(
        [near(1, -1)[:, :, :1, ez - 1 :], near(1, 0)[:, :, :1, :], near(1, 1)[:, :, :1, :1]],
        axis=3,
    )
    extended = jnp.concatenate([low_row, middle, high_row], axis=2)
    first_padded = with_halo(extended, (("gx", 1),), 1)
    derived = derive_fields(padded_images[0], padded_images[1])
    region = padded_images[2][3:-3, 3:-3, 3:-3]
    contrast = derived[0].astype(jnp.float32)
    slopes = derived[1:].astype(jnp.float32)
    masked_slopes = slopes * region[None]
    curvature = collect(masked_slopes * slopes, table_square, True) + diagonal_shift
    for iteration in range(ITERS):
        if iteration == 0:
            padded = first_padded
        else:
            padded = with_halo(tile_values, (("gx", 1), ("gy", 2), ("gz", 3)), 1)
        moved = spread(padded, weights_table)
        residual = contrast + slopes[0] * moved[0] + slopes[1] * moved[1] + slopes[2] * moved[2]
        image_part = collect(masked_slopes * residual[None], table_back, False)
        force_total = image_part + elastic_weight * elastic_force(padded)
        tile_values = tile_values - force_total / curvature
    final_blocks = tile_values.reshape(3, blocks, block_nodes)
    own_labels = received_labels.reshape(members, HALO_CAP)[:, :CAP].reshape(-1)
    position = jnp.arange(blocks, dtype=jnp.int32)
    back_placing = (own_labels[:, None] == (position + 1).astype(jnp.float32)[None, :]).astype(
        jnp.float32
    )
    outgoing = jnp.einsum("ckn,pk->cpn", final_blocks, back_placing, precision=highest).reshape(
        3, -1
    )
    incoming = lax.all_to_all(outgoing, ("gy", "gz"), split_axis=1, concat_axis=1, tiled=True)
    own_slot = owner_tile * CAP + ranking[:blocks]
    back_packing = (
        own_slot[:, None] == jnp.arange(members * CAP, dtype=jnp.int32)[None, :]
    ).astype(jnp.float32)
    return jnp.einsum(
        "cpn,jp->cjn", incoming.reshape(3, members * CAP, -1), back_packing, precision=highest
    )


def solution(mesh):
    in_specs = (
        P("gx", "gy", "gz"),
        P("gx", "gy", "gz"),
        P("gx", "gy", "gz"),
        P(None, ("gx", "gy", "gz"), None),
        P(("gx", "gy", "gz")),
    )
    out_specs = P(None, ("gx", "gy", "gz"), None)
    return jax.shard_map(
        per_device, mesh=mesh, in_specs=in_specs, out_specs=out_specs, check_vma=False
    )
```

```python
import jax
import jax.numpy as jnp
from jax import lax
from jax.sharding import PartitionSpec as P

ELEM = 4
ITERS = 2
CAP = 2


binomial = (0.0625, 0.25, 0.375, 0.25, 0.0625)
lame_lambda = 1.0
shear_modulus = 0.5
elastic_weight = 2.0
diagonal_shift = 6.0
highest = lax.Precision.HIGHEST


def with_halo(block, sides, width):
    for axis, dim in sides:
        count = lax.axis_size(axis)
        forward = [(i, i + 1) for i in range(count - 1)]
        backward = [(target, source) for source, target in forward]
        low = lax.ppermute(
            lax.slice_in_dim(block, block.shape[dim] - width, None, axis=dim), axis, forward
        )
        high = lax.ppermute(lax.slice_in_dim(block, 0, width, axis=dim), axis, backward)
        block = jnp.concatenate([low, block, high], axis=dim)
    return block


def with_halo_pair(first, second, sides, widths):
    for axis, first_dim, second_dim in sides:
        count = lax.axis_size(axis)
        forward = [(i, i + 1) for i in range(count - 1)]
        backward = [(target, source) for source, target in forward]
        parts = []
        for block, dim, width in ((first, first_dim, widths[0]), (second, second_dim, widths[1])):
            parts.append(
                (
                    lax.slice_in_dim(block, block.shape[dim] - width, None, axis=dim),
                    lax.slice_in_dim(block, 0, width, axis=dim),
                )
            )
        low_flat = jnp.concatenate([p[0].reshape(-1) for p in parts])
        high_flat = jnp.concatenate([p[1].reshape(-1) for p in parts])
        low_flat = lax.ppermute(low_flat, axis, forward)
        high_flat = lax.ppermute(high_flat, axis, backward)
        split = parts[0][0].size
        pieces = []
        for index, (block, dim) in enumerate(((first, first_dim), (second, second_dim))):
            shape = parts[index][0].shape
            begin, end = (0, split) if index == 0 else (split, low_flat.shape[0])
            low = low_flat[begin:end].reshape(shape)
            high = high_flat[begin:end].reshape(shape)
            pieces.append(jnp.concatenate([low, block, high], axis=dim))
        first, second = pieces
    return first, second


def smooth_axis(volume, dimension):
    length = volume.shape[dimension] - 4
    summed = binomial[0] * lax.slice_in_dim(volume, 0, length, axis=dimension)
    for offset in range(1, 5):
        summed = summed + binomial[offset] * lax.slice_in_dim(
            volume, offset, offset + length, axis=dimension
        )
    return summed


def derive_fields(first_padded, second_padded):
    first_smooth = first_padded
    second_smooth = second_padded
    for dimension in range(3):
        first_smooth = smooth_axis(first_smooth, dimension)
        second_smooth = smooth_axis(second_smooth, dimension)
    average = (first_smooth + second_smooth) * 0.5
    contrast = (second_smooth - first_smooth)[1:-1, 1:-1, 1:-1].astype(jnp.bfloat16)
    slopes = []
    for dimension in range(3):
        length = average.shape[dimension] - 2
        forward_part = lax.slice_in_dim(average, 2, length + 2, axis=dimension)
        backward_part = lax.slice_in_dim(average, 0, length, axis=dimension)
        gradient = (forward_part - backward_part) * 0.5
        for cropped_dim in range(3):
            if cropped_dim != dimension:
                gradient = lax.slice_in_dim(
                    gradient, 1, gradient.shape[cropped_dim] - 1, axis=cropped_dim
                )
        slopes.append(gradient.astype(jnp.bfloat16))
    return jnp.stack([contrast] + slopes)


def interp_axis(volume, dimension, cells_edge):
    length = volume.shape[dimension]
    before = lax.slice_in_dim(volume, 0, length - 1, axis=dimension)
    after = lax.slice_in_dim(volume, 1, length, axis=dimension)
    shape_one = [1] * (volume.ndim + 1)
    shape_one[dimension + 1] = cells_edge
    fraction = (jnp.arange(cells_edge, dtype=jnp.float32) / cells_edge).reshape(shape_one)
    merged = (
        jnp.expand_dims(before, dimension + 1) * (1.0 - fraction)
        + jnp.expand_dims(after, dimension + 1) * fraction
    )
    new_shape = list(volume.shape)
    new_shape[dimension] = (length - 1) * cells_edge
    return merged.reshape(new_shape)


def collect_axis(volume, dimension, cells_edge, squared):
    elements = volume.shape[dimension] // cells_edge
    split_shape = (
        list(volume.shape[:dimension])
        + [elements, cells_edge]
        + list(volume.shape[dimension + 1 :])
    )
    pieces = volume.reshape(split_shape)
    shape_one = [1] * len(split_shape)
    shape_one[dimension + 1] = cells_edge
    fraction = (jnp.arange(cells_edge, dtype=jnp.float32) / cells_edge).reshape(shape_one)
    weight_low = 1.0 - fraction
    weight_high = fraction
    if squared:
        weight_low = weight_low * weight_low
        weight_high = weight_high * weight_high
    low_side = jnp.sum(pieces * weight_low, axis=dimension + 1)
    high_side = jnp.sum(pieces * weight_high, axis=dimension + 1)
    return lax.slice_in_dim(low_side, 1, elements, axis=dimension) + lax.slice_in_dim(
        high_side, 0, elements - 1, axis=dimension
    )


def pair_op(volume, dimension, factor):
    length = volume.shape[dimension]
    return lax.slice_in_dim(volume, 1, length, axis=dimension) + factor * lax.slice_in_dim(
        volume, 0, length - 1, axis=dimension
    )


def cross_pairs(volume, chosen, factor, offset):
    for dimension in range(3):
        volume = pair_op(volume, dimension + offset, factor if dimension == chosen else 1.0)
    return volume


def elastic_force(padded):
    gradients = [cross_pairs(padded, chosen, -1.0, 1) * (1.0 / (4.0 * ELEM)) for chosen in range(3)]
    deform = [
        [gradients[source][target] + (1.0 if target == source else 0.0) for source in range(3)]
        for target in range(3)
    ]
    strain = [
        [
            0.5
            * (
                deform[0][target] * deform[0][source]
                + deform[1][target] * deform[1][source]
                + deform[2][target] * deform[2][source]
            )
            - (0.5 if target == source else 0.0)
            for source in range(3)
        ]
        for target in range(3)
    ]
    trace_strain = strain[0][0] + strain[1][1] + strain[2][2]
    stress = [
        [
            2.0 * shear_modulus * strain[target][source]
            + (lame_lambda * trace_strain if target == source else 0.0)
            for source in range(3)
        ]
        for target in range(3)
    ]
    nominal = [
        [
            deform[target][0] * stress[0][source]
            + deform[target][1] * stress[1][source]
            + deform[target][2] * stress[2][source]
            for source in range(3)
        ]
        for target in range(3)
    ]
    coefficient = ELEM * ELEM / 4.0
    forces = []
    for target in range(3):
        summed = cross_pairs(nominal[target][0], 0, -1.0, 0)
        for source in range(1, 3):
            summed = summed + cross_pairs(nominal[target][source], source, -1.0, 0)
        forces.append(-coefficient * summed)
    return jnp.stack(forces)


def axis_table(nodes_len, cells_edge, squared):
    voxels = (nodes_len - 1) * cells_edge
    column = jnp.arange(voxels, dtype=jnp.int32)
    element = column // cells_edge
    fraction = (column % cells_edge).astype(jnp.float32) / cells_edge
    weight_low = 1.0 - fraction
    weight_high = fraction
    if squared:
        weight_low = weight_low * weight_low
        weight_high = weight_high * weight_high
    node_row = jnp.arange(nodes_len, dtype=jnp.int32)[:, None]
    return jnp.where(node_row == element[None, :], weight_low[None, :], 0.0) + jnp.where(
        node_row == element[None, :] + 1, weight_high[None, :], 0.0
    )


def spread(padded, weights_table):
    shape_all = padded.shape
    stretched = jnp.dot(padded.reshape(-1, shape_all[3]), weights_table, precision=highest)
    stretched = stretched.reshape(shape_all[0], shape_all[1], shape_all[2], weights_table.shape[1])
    stretched = interp_axis(stretched, 1, ELEM)
    return interp_axis(stretched, 2, ELEM)


def collect(volume, table_back, squared):
    shape_all = volume.shape
    reduced = jnp.dot(volume.reshape(-1, shape_all[3]), table_back, precision=highest)
    reduced = reduced.reshape(shape_all[0], shape_all[1], shape_all[2], table_back.shape[1])
    reduced = collect_axis(reduced, 2, ELEM, squared)
    return collect_axis(reduced, 1, ELEM, squared)


NEIGHBOURS = [(0, 0)] + [(ry, rz) for ry in (-1, 0, 1) for rz in (-1, 0, 1) if (ry, rz) != (0, 0)]
HALO_CAP = 10


def per_device(reference_image, deformed_image, roi_mask, displacement, node_map):
    stacked = jnp.stack([reference_image, deformed_image, roi_mask.astype(jnp.bfloat16)])
    stacked = with_halo(stacked, (("gy", 2),), 5)
    stacked = with_halo(stacked, (("gz", 3),), 5 + ELEM)
    padded_images = with_halo(stacked, (("gx", 1),), 5).astype(jnp.float32)
    nodes_shape = (
        3,
        reference_image.shape[0] // ELEM,
        reference_image.shape[1] // ELEM,
        reference_image.shape[2] // ELEM,
    )
    _, ex, ey, ez = nodes_shape
    weights_table = axis_table(ez + 2, ELEM, False)
    table_back = weights_table[1:-1].T
    wide_table = axis_table(ez + 4, ELEM, False)
    wide_back = wide_table[1:-1].T
    wide_square = axis_table(ez + 4, ELEM, True)[1:-1].T
    size_y = lax.axis_size("gy")
    size_z = lax.axis_size("gz")
    members = size_y * size_z
    blocks = node_map.shape[0]
    block_nodes = displacement.shape[2]
    zchunks = ez // block_nodes
    owner_tile = node_map // blocks
    tile_block = node_map % blocks
    tile_y = owner_tile // size_z
    tile_z = owner_tile % size_z
    block_y = (tile_block // zchunks) % ey
    block_zc = tile_block % zchunks
    dests, valids, labels = [], [], []
    for index, (ry, rz) in enumerate(NEIGHBOURS):
        dest_y = tile_y - ry
        dest_z = tile_z - rz
        valid = (dest_y >= 0) & (dest_y < size_y) & (dest_z >= 0) & (dest_z < size_z)
        if ry == -1:
            valid = valid & (block_y == ey - 1)
        elif ry == 1:
            valid = valid & (block_y == 0)
        if rz == -1:
            valid = valid & (block_zc == zchunks - 1)
        elif rz == 1:
            valid = valid & (block_zc == 0)
        dests.append(dest_y * size_z + dest_z)
        valids.append(valid)
        labels.append(index * blocks + tile_block + 1)
    cand_dest = jnp.concatenate(dests)
    cand_valid = jnp.concatenate(valids)
    cand_label = jnp.concatenate(labels).astype(jnp.float32)
    count = cand_dest.shape[0]
    order = jnp.arange(count, dtype=jnp.int32)
    earlier = (
        (cand_dest[:, None] == cand_dest[None, :])
        & cand_valid[None, :]
        & (order[None, :] < order[:, None])
    )
    ranking = jnp.sum(earlier.astype(jnp.int32), axis=1)
    target_slot = jnp.where(cand_valid, cand_dest * HALO_CAP + ranking, -1)
    packing = (
        target_slot[:, None] == jnp.arange(members * HALO_CAP, dtype=jnp.int32)[None, :]
    ).astype(jnp.float32)
    cand_data = jnp.concatenate(
        [
            jnp.concatenate([displacement] * len(NEIGHBOURS), axis=1),
            jnp.broadcast_to(cand_label[None, :, None], (1, count, block_nodes)),
        ]
    )
    send_channels = cand_data.shape[0]
    send_outgoing = jnp.einsum("cjn,jp->cpn", cand_data, packing, precision=highest).reshape(
        send_channels, -1
    )
    send_incoming = lax.all_to_all(
        send_outgoing, ("gy", "gz"), split_axis=1, concat_axis=1, tiled=True
    ).reshape(send_channels, members * HALO_CAP, block_nodes)
    received_labels = send_incoming[3, :, 0]
    placing = (
        received_labels[:, None] == jnp.arange(1, count + 1, dtype=jnp.float32)[None, :]
    ).astype(jnp.float32)
    around = jnp.einsum("cpn,pk->ckn", send_incoming[:3], placing, precision=highest).reshape(
        3, len(NEIGHBOURS), ex, ey, ez
    )

    def near(ry, rz):
        return around[:, NEIGHBOURS.index((ry, rz))]

    centre = near(0, 0)
    middle = jnp.concatenate(
        [near(0, -1)[..., ez - 2 :], centre, near(0, 1)[..., :2]], axis=3
    )
    low_row = jnp.concatenate(
        [
            near(-1, -1)[:, :, ey - 1 :, ez - 2 :],
            near(-1, 0)[:, :, ey - 1 :, :],
            near(-1, 1)[:, :, ey - 1 :, :2],
        ],
        axis=3,
    )
    high_row = jnp.concatenate(
        [near(1, -1)[:, :, :1, ez - 2 :], near(1, 0)[:, :, :1, :], near(1, 1)[:, :, :1, :2]],
        axis=3,
    )
    extended = jnp.concatenate([low_row, middle, high_row], axis=2)
    first_padded = with_halo(extended, (("gx", 1),), 1)
    derived = derive_fields(padded_images[0], padded_images[1])
    region = padded_images[2][3:-3, 3:-3, 3:-3]
    contrast = derived[0].astype(jnp.float32)
    slopes = derived[1:].astype(jnp.float32)
    masked_slopes = slopes * region[None]
    wide_curvature = collect(masked_slopes * slopes, wide_square, True) + diagonal_shift
    moved = spread(first_padded, wide_table)
    residual = contrast + slopes[0] * moved[0] + slopes[1] * moved[1] + slopes[2] * moved[2]
    image_part = collect(masked_slopes * residual[None], wide_back, False)
    force_total = image_part + elastic_weight * elastic_force(first_padded)
    wide_values = first_padded[:, 1:-1, 1:-1, 1:-1] - force_total / wide_curvature
    column = jnp.arange(ez + 2, dtype=jnp.int32)
    ghost = ((column == 0) & (lax.axis_index("gz") == 0)) | (
        (column == ez + 1) & (lax.axis_index("gz") == size_z - 1)
    )
    wide_values = jnp.where(ghost, 0.0, wide_values)
    tile_values = wide_values[..., 1:-1]
    curvature = wide_curvature[..., 1:-1]
    contrast = contrast[..., ELEM:-ELEM]
    slopes = slopes[..., ELEM:-ELEM]
    masked_slopes = masked_slopes[..., ELEM:-ELEM]
    padded = with_halo(wide_values, (("gx", 1), ("gy", 2)), 1)
    moved = spread(padded, weights_table)
    residual = contrast + slopes[0] * moved[0] + slopes[1] * moved[1] + slopes[2] * moved[2]
    image_part = collect(masked_slopes * residual[None], table_back, False)
    force_total = image_part + elastic_weight * elastic_force(padded)
    tile_values = tile_values - force_total / curvature
    final_blocks = tile_values.reshape(3, blocks, block_nodes)
    own_labels = received_labels.reshape(members, HALO_CAP)[:, :CAP].reshape(-1)
    position = jnp.arange(blocks, dtype=jnp.int32)
    back_placing = (own_labels[:, None] == (position + 1).astype(jnp.float32)[None, :]).astype(
        jnp.float32
    )
    outgoing = jnp.einsum("ckn,pk->cpn", final_blocks, back_placing, precision=highest).reshape(
        3, -1
    )
    incoming = lax.all_to_all(outgoing, ("gy", "gz"), split_axis=1, concat_axis=1, tiled=True)
    own_slot = owner_tile * CAP + ranking[:blocks]
    back_packing = (
        own_slot[:, None] == jnp.arange(members * CAP, dtype=jnp.int32)[None, :]
    ).astype(jnp.float32)
    return jnp.einsum(
        "cpn,jp->cjn", incoming.reshape(3, members * CAP, -1), back_packing, precision=highest
    )


def solution(mesh):
    in_specs = (
        P("gx", "gy", "gz"),
        P("gx", "gy", "gz"),
        P("gx", "gy", "gz"),
        P(None, ("gx", "gy", "gz"), None),
        P(("gx", "gy", "gz")),
    )
    out_specs = P(None, ("gx", "gy", "gz"), None)
    return jax.shard_map(
        per_device, mesh=mesh, in_specs=in_specs, out_specs=out_specs, check_vma=False
    )
```

```python
import jax
import jax.numpy as jnp
from jax import lax
from jax.sharding import PartitionSpec as P

ELEM = 4
ITERS = 2
CAP = 2


binomial = (0.0625, 0.25, 0.375, 0.25, 0.0625)
lame_lambda = 1.0
shear_modulus = 0.5
elastic_weight = 2.0
diagonal_shift = 6.0
highest = lax.Precision.HIGHEST


def with_halo(block, sides, width):
    for axis, dim in sides:
        count = lax.axis_size(axis)
        forward = [(i, i + 1) for i in range(count - 1)]
        backward = [(target, source) for source, target in forward]
        low = lax.ppermute(
            lax.slice_in_dim(block, block.shape[dim] - width, None, axis=dim), axis, forward
        )
        high = lax.ppermute(lax.slice_in_dim(block, 0, width, axis=dim), axis, backward)
        block = jnp.concatenate([low, block, high], axis=dim)
    return block


def with_halo_pair(first, second, sides, widths):
    for axis, first_dim, second_dim in sides:
        count = lax.axis_size(axis)
        forward = [(i, i + 1) for i in range(count - 1)]
        backward = [(target, source) for source, target in forward]
        parts = []
        for block, dim, width in ((first, first_dim, widths[0]), (second, second_dim, widths[1])):
            parts.append(
                (
                    lax.slice_in_dim(block, block.shape[dim] - width, None, axis=dim),
                    lax.slice_in_dim(block, 0, width, axis=dim),
                )
            )
        low_flat = jnp.concatenate([p[0].reshape(-1) for p in parts])
        high_flat = jnp.concatenate([p[1].reshape(-1) for p in parts])
        low_flat = lax.ppermute(low_flat, axis, forward)
        high_flat = lax.ppermute(high_flat, axis, backward)
        split = parts[0][0].size
        pieces = []
        for index, (block, dim) in enumerate(((first, first_dim), (second, second_dim))):
            shape = parts[index][0].shape
            begin, end = (0, split) if index == 0 else (split, low_flat.shape[0])
            low = low_flat[begin:end].reshape(shape)
            high = high_flat[begin:end].reshape(shape)
            pieces.append(jnp.concatenate([low, block, high], axis=dim))
        first, second = pieces
    return first, second


def smooth_axis(volume, dimension):
    length = volume.shape[dimension] - 4
    summed = binomial[0] * lax.slice_in_dim(volume, 0, length, axis=dimension)
    for offset in range(1, 5):
        summed = summed + binomial[offset] * lax.slice_in_dim(
            volume, offset, offset + length, axis=dimension
        )
    return summed


def derive_fields(first_padded, second_padded):
    first_smooth = first_padded
    second_smooth = second_padded
    for dimension in range(3):
        first_smooth = smooth_axis(first_smooth, dimension)
        second_smooth = smooth_axis(second_smooth, dimension)
    average = (first_smooth + second_smooth) * 0.5
    contrast = (second_smooth - first_smooth)[1:-1, 1:-1, 1:-1].astype(jnp.bfloat16)
    slopes = []
    for dimension in range(3):
        length = average.shape[dimension] - 2
        forward_part = lax.slice_in_dim(average, 2, length + 2, axis=dimension)
        backward_part = lax.slice_in_dim(average, 0, length, axis=dimension)
        gradient = (forward_part - backward_part) * 0.5
        for cropped_dim in range(3):
            if cropped_dim != dimension:
                gradient = lax.slice_in_dim(
                    gradient, 1, gradient.shape[cropped_dim] - 1, axis=cropped_dim
                )
        slopes.append(gradient.astype(jnp.bfloat16))
    return jnp.stack([contrast] + slopes)


def interp_axis(volume, dimension, cells_edge):
    length = volume.shape[dimension]
    before = lax.slice_in_dim(volume, 0, length - 1, axis=dimension)
    after = lax.slice_in_dim(volume, 1, length, axis=dimension)
    shape_one = [1] * (volume.ndim + 1)
    shape_one[dimension + 1] = cells_edge
    fraction = (jnp.arange(cells_edge, dtype=jnp.float32) / cells_edge).reshape(shape_one)
    merged = (
        jnp.expand_dims(before, dimension + 1) * (1.0 - fraction)
        + jnp.expand_dims(after, dimension + 1) * fraction
    )
    new_shape = list(volume.shape)
    new_shape[dimension] = (length - 1) * cells_edge
    return merged.reshape(new_shape)


def collect_axis(volume, dimension, cells_edge, squared):
    elements = volume.shape[dimension] // cells_edge
    split_shape = (
        list(volume.shape[:dimension])
        + [elements, cells_edge]
        + list(volume.shape[dimension + 1 :])
    )
    pieces = volume.reshape(split_shape)
    shape_one = [1] * len(split_shape)
    shape_one[dimension + 1] = cells_edge
    fraction = (jnp.arange(cells_edge, dtype=jnp.float32) / cells_edge).reshape(shape_one)
    weight_low = 1.0 - fraction
    weight_high = fraction
    if squared:
        weight_low = weight_low * weight_low
        weight_high = weight_high * weight_high
    low_side = jnp.sum(pieces * weight_low, axis=dimension + 1)
    high_side = jnp.sum(pieces * weight_high, axis=dimension + 1)
    return lax.slice_in_dim(low_side, 1, elements, axis=dimension) + lax.slice_in_dim(
        high_side, 0, elements - 1, axis=dimension
    )


def pair_op(volume, dimension, factor):
    length = volume.shape[dimension]
    return lax.slice_in_dim(volume, 1, length, axis=dimension) + factor * lax.slice_in_dim(
        volume, 0, length - 1, axis=dimension
    )


def cross_pairs(volume, chosen, factor, offset):
    for dimension in range(3):
        volume = pair_op(volume, dimension + offset, factor if dimension == chosen else 1.0)
    return volume


def elastic_force(padded):
    gradients = [cross_pairs(padded, chosen, -1.0, 1) * (1.0 / (4.0 * ELEM)) for chosen in range(3)]
    deform = [
        [gradients[source][target] + (1.0 if target == source else 0.0) for source in range(3)]
        for target in range(3)
    ]
    strain = [
        [
            0.5
            * (
                deform[0][target] * deform[0][source]
                + deform[1][target] * deform[1][source]
                + deform[2][target] * deform[2][source]
            )
            - (0.5 if target == source else 0.0)
            for source in range(3)
        ]
        for target in range(3)
    ]
    trace_strain = strain[0][0] + strain[1][1] + strain[2][2]
    stress = [
        [
            2.0 * shear_modulus * strain[target][source]
            + (lame_lambda * trace_strain if target == source else 0.0)
            for source in range(3)
        ]
        for target in range(3)
    ]
    nominal = [
        [
            deform[target][0] * stress[0][source]
            + deform[target][1] * stress[1][source]
            + deform[target][2] * stress[2][source]
            for source in range(3)
        ]
        for target in range(3)
    ]
    coefficient = ELEM * ELEM / 4.0
    forces = []
    for target in range(3):
        summed = cross_pairs(nominal[target][0], 0, -1.0, 0)
        for source in range(1, 3):
            summed = summed + cross_pairs(nominal[target][source], source, -1.0, 0)
        forces.append(-coefficient * summed)
    return jnp.stack(forces)


def axis_table(nodes_len, cells_edge, squared):
    voxels = (nodes_len - 1) * cells_edge
    column = jnp.arange(voxels, dtype=jnp.int32)
    element = column // cells_edge
    fraction = (column % cells_edge).astype(jnp.float32) / cells_edge
    weight_low = 1.0 - fraction
    weight_high = fraction
    if squared:
        weight_low = weight_low * weight_low
        weight_high = weight_high * weight_high
    node_row = jnp.arange(nodes_len, dtype=jnp.int32)[:, None]
    return jnp.where(node_row == element[None, :], weight_low[None, :], 0.0) + jnp.where(
        node_row == element[None, :] + 1, weight_high[None, :], 0.0
    )


def spread(padded, weights_table):
    shape_all = padded.shape
    stretched = jnp.dot(padded.reshape(-1, shape_all[3]), weights_table, precision=highest)
    stretched = stretched.reshape(shape_all[0], shape_all[1], shape_all[2], weights_table.shape[1])
    stretched = interp_axis(stretched, 1, ELEM)
    return interp_axis(stretched, 2, ELEM)


def collect(volume, table_back, squared):
    shape_all = volume.shape
    reduced = jnp.dot(volume.reshape(-1, shape_all[3]), table_back, precision=highest)
    reduced = reduced.reshape(shape_all[0], shape_all[1], shape_all[2], table_back.shape[1])
    reduced = collect_axis(reduced, 2, ELEM, squared)
    return collect_axis(reduced, 1, ELEM, squared)


NEIGHBOURS = [(0, 0)] + [(ry, rz) for ry in (-1, 0, 1) for rz in (-1, 0, 1) if (ry, rz) != (0, 0)]
HALO_CAP = 10


def per_device(reference_image, deformed_image, roi_mask, displacement, node_map):
    stacked = jnp.stack([reference_image, deformed_image, roi_mask.astype(jnp.bfloat16)])
    stacked = with_halo(stacked, (("gy", 2),), 5)
    stacked = with_halo(stacked, (("gz", 3),), 5 + ELEM)
    padded_images = with_halo(stacked, (("gx", 1),), 5).astype(jnp.float32)
    nodes_shape = (
        3,
        reference_image.shape[0] // ELEM,
        reference_image.shape[1] // ELEM,
        reference_image.shape[2] // ELEM,
    )
    _, ex, ey, ez = nodes_shape
    wide_table = axis_table(ez + 4, ELEM, False)
    wide_back = wide_table[1:-1].T
    wide_square = axis_table(ez + 4, ELEM, True)[1:-1].T
    size_y = lax.axis_size("gy")
    size_z = lax.axis_size("gz")
    members = size_y * size_z
    blocks = node_map.shape[0]
    block_nodes = displacement.shape[2]
    zchunks = ez // block_nodes
    owner_tile = node_map // blocks
    tile_block = node_map % blocks
    tile_y = owner_tile // size_z
    tile_z = owner_tile % size_z
    block_y = (tile_block // zchunks) % ey
    block_zc = tile_block % zchunks
    dests, valids, labels = [], [], []
    for index, (ry, rz) in enumerate(NEIGHBOURS):
        dest_y = tile_y - ry
        dest_z = tile_z - rz
        valid = (dest_y >= 0) & (dest_y < size_y) & (dest_z >= 0) & (dest_z < size_z)
        if ry == -1:
            valid = valid & (block_y == ey - 1)
        elif ry == 1:
            valid = valid & (block_y == 0)
        if rz == -1:
            valid = valid & (block_zc == zchunks - 1)
        elif rz == 1:
            valid = valid & (block_zc == 0)
        dests.append(dest_y * size_z + dest_z)
        valids.append(valid)
        labels.append(index * blocks + tile_block + 1)
    cand_dest = jnp.concatenate(dests)
    cand_valid = jnp.concatenate(valids)
    cand_label = jnp.concatenate(labels).astype(jnp.float32)
    count = cand_dest.shape[0]
    order = jnp.arange(count, dtype=jnp.int32)
    earlier = (
        (cand_dest[:, None] == cand_dest[None, :])
        & cand_valid[None, :]
        & (order[None, :] < order[:, None])
    )
    ranking = jnp.sum(earlier.astype(jnp.int32), axis=1)
    target_slot = jnp.where(cand_valid, cand_dest * HALO_CAP + ranking, -1)
    packing = (
        target_slot[:, None] == jnp.arange(members * HALO_CAP, dtype=jnp.int32)[None, :]
    ).astype(jnp.float32)
    cand_data = jnp.concatenate(
        [
            jnp.concatenate([displacement] * len(NEIGHBOURS), axis=1),
            jnp.broadcast_to(cand_label[None, :, None], (1, count, block_nodes)),
        ]
    )
    send_channels = cand_data.shape[0]
    send_outgoing = jnp.einsum("cjn,jp->cpn", cand_data, packing, precision=highest).reshape(
        send_channels, -1
    )
    send_incoming = lax.all_to_all(
        send_outgoing, ("gy", "gz"), split_axis=1, concat_axis=1, tiled=True
    ).reshape(send_channels, members * HALO_CAP, block_nodes)
    received_labels = send_incoming[3, :, 0]
    placing = (
        received_labels[:, None] == jnp.arange(1, count + 1, dtype=jnp.float32)[None, :]
    ).astype(jnp.float32)
    around = jnp.einsum("cpn,pk->ckn", send_incoming[:3], placing, precision=highest).reshape(
        3, len(NEIGHBOURS), ex, ey, ez
    )

    def near(ry, rz):
        return around[:, NEIGHBOURS.index((ry, rz))]

    centre = near(0, 0)
    middle = jnp.concatenate(
        [near(0, -1)[..., ez - 2 :], centre, near(0, 1)[..., :2]], axis=3
    )
    low_row = jnp.concatenate(
        [
            near(-1, -1)[:, :, ey - 1 :, ez - 2 :],
            near(-1, 0)[:, :, ey - 1 :, :],
            near(-1, 1)[:, :, ey - 1 :, :2],
        ],
        axis=3,
    )
    high_row = jnp.concatenate(
        [near(1, -1)[:, :, :1, ez - 2 :], near(1, 0)[:, :, :1, :], near(1, 1)[:, :, :1, :2]],
        axis=3,
    )
    extended = jnp.concatenate([low_row, middle, high_row], axis=2)
    first_padded = with_halo(extended, (("gx", 1),), 1)
    derived = derive_fields(padded_images[0], padded_images[1])
    region = padded_images[2][3:-3, 3:-3, 3:-3]
    contrast = derived[0].astype(jnp.float32)
    slopes = derived[1:].astype(jnp.float32)
    masked_slopes = slopes * region[None]
    wide_curvature = collect(masked_slopes * slopes, wide_square, True) + diagonal_shift
    moved = spread(first_padded, wide_table)
    residual = contrast + slopes[0] * moved[0] + slopes[1] * moved[1] + slopes[2] * moved[2]
    image_part = collect(masked_slopes * residual[None], wide_back, False)
    force_total = image_part + elastic_weight * elastic_force(first_padded)
    wide_values = first_padded[:, 1:-1, 1:-1, 1:-1] - force_total / wide_curvature
    column = jnp.arange(ez + 2, dtype=jnp.int32)
    ghost = ((column == 0) & (lax.axis_index("gz") == 0)) | (
        (column == ez + 1) & (lax.axis_index("gz") == size_z - 1)
    )
    wide_values = jnp.where(ghost, 0.0, wide_values)
    padded = with_halo(wide_values, (("gx", 1), ("gy", 2)), 1)
    padded = jnp.pad(padded, ((0, 0), (0, 0), (0, 0), (1, 1)))
    moved = spread(padded, wide_table)
    residual = contrast + slopes[0] * moved[0] + slopes[1] * moved[1] + slopes[2] * moved[2]
    image_part = collect(masked_slopes * residual[None], wide_back, False)
    force_total = image_part + elastic_weight * elastic_force(padded)
    tile_values = (wide_values - force_total / wide_curvature)[..., 1:-1]
    final_blocks = tile_values.reshape(3, blocks, block_nodes)
    own_labels = received_labels.reshape(members, HALO_CAP)[:, :CAP].reshape(-1)
    position = jnp.arange(blocks, dtype=jnp.int32)
    back_placing = (own_labels[:, None] == (position + 1).astype(jnp.float32)[None, :]).astype(
        jnp.float32
    )
    outgoing = jnp.einsum("ckn,pk->cpn", final_blocks, back_placing, precision=highest).reshape(
        3, -1
    )
    incoming = lax.all_to_all(outgoing, ("gy", "gz"), split_axis=1, concat_axis=1, tiled=True)
    own_slot = owner_tile * CAP + ranking[:blocks]
    back_packing = (
        own_slot[:, None] == jnp.arange(members * CAP, dtype=jnp.int32)[None, :]
    ).astype(jnp.float32)
    return jnp.einsum(
        "cpn,jp->cjn", incoming.reshape(3, members * CAP, -1), back_packing, precision=highest
    )


def solution(mesh):
    in_specs = (
        P("gx", "gy", "gz"),
        P("gx", "gy", "gz"),
        P("gx", "gy", "gz"),
        P(None, ("gx", "gy", "gz"), None),
        P(("gx", "gy", "gz")),
    )
    out_specs = P(None, ("gx", "gy", "gz"), None)
    return jax.shard_map(
        per_device, mesh=mesh, in_specs=in_specs, out_specs=out_specs, check_vma=False
    )
```

```python
import jax
import jax.numpy as jnp
from jax import lax
from jax.sharding import PartitionSpec as P

ELEM = 4
ITERS = 2
CAP = 2


binomial = (0.0625, 0.25, 0.375, 0.25, 0.0625)
lame_lambda = 1.0
shear_modulus = 0.5
elastic_weight = 2.0
diagonal_shift = 6.0
highest = lax.Precision.HIGHEST


def with_halo(block, sides, width):
    for axis, dim in sides:
        count = lax.axis_size(axis)
        forward = [(i, i + 1) for i in range(count - 1)]
        backward = [(target, source) for source, target in forward]
        low = lax.ppermute(
            lax.slice_in_dim(block, block.shape[dim] - width, None, axis=dim), axis, forward
        )
        high = lax.ppermute(lax.slice_in_dim(block, 0, width, axis=dim), axis, backward)
        block = jnp.concatenate([low, block, high], axis=dim)
    return block


def with_halo_pair(first, second, sides, widths):
    for axis, first_dim, second_dim in sides:
        count = lax.axis_size(axis)
        forward = [(i, i + 1) for i in range(count - 1)]
        backward = [(target, source) for source, target in forward]
        parts = []
        for block, dim, width in ((first, first_dim, widths[0]), (second, second_dim, widths[1])):
            parts.append(
                (
                    lax.slice_in_dim(block, block.shape[dim] - width, None, axis=dim),
                    lax.slice_in_dim(block, 0, width, axis=dim),
                )
            )
        low_flat = jnp.concatenate([p[0].reshape(-1).astype(jnp.float32) for p in parts])
        high_flat = jnp.concatenate([p[1].reshape(-1).astype(jnp.float32) for p in parts])
        low_flat = lax.ppermute(low_flat, axis, forward)
        high_flat = lax.ppermute(high_flat, axis, backward)
        split = parts[0][0].size
        pieces = []
        for index, (block, dim) in enumerate(((first, first_dim), (second, second_dim))):
            shape = parts[index][0].shape
            begin, end = (0, split) if index == 0 else (split, low_flat.shape[0])
            low = low_flat[begin:end].reshape(shape).astype(block.dtype)
            high = high_flat[begin:end].reshape(shape).astype(block.dtype)
            pieces.append(jnp.concatenate([low, block, high], axis=dim))
        first, second = pieces
    return first, second


def smooth_axis(volume, dimension):
    length = volume.shape[dimension] - 4
    summed = binomial[0] * lax.slice_in_dim(volume, 0, length, axis=dimension)
    for offset in range(1, 5):
        summed = summed + binomial[offset] * lax.slice_in_dim(
            volume, offset, offset + length, axis=dimension
        )
    return summed


def derive_fields(first_padded, second_padded):
    first_smooth = first_padded
    second_smooth = second_padded
    for dimension in range(3):
        first_smooth = smooth_axis(first_smooth, dimension)
        second_smooth = smooth_axis(second_smooth, dimension)
    average = (first_smooth + second_smooth) * 0.5
    contrast = (second_smooth - first_smooth)[1:-1, 1:-1, 1:-1].astype(jnp.bfloat16)
    slopes = []
    for dimension in range(3):
        length = average.shape[dimension] - 2
        forward_part = lax.slice_in_dim(average, 2, length + 2, axis=dimension)
        backward_part = lax.slice_in_dim(average, 0, length, axis=dimension)
        gradient = (forward_part - backward_part) * 0.5
        for cropped_dim in range(3):
            if cropped_dim != dimension:
                gradient = lax.slice_in_dim(
                    gradient, 1, gradient.shape[cropped_dim] - 1, axis=cropped_dim
                )
        slopes.append(gradient.astype(jnp.bfloat16))
    return jnp.stack([contrast] + slopes)


def interp_axis(volume, dimension, cells_edge):
    length = volume.shape[dimension]
    before = lax.slice_in_dim(volume, 0, length - 1, axis=dimension)
    after = lax.slice_in_dim(volume, 1, length, axis=dimension)
    shape_one = [1] * (volume.ndim + 1)
    shape_one[dimension + 1] = cells_edge
    fraction = (jnp.arange(cells_edge, dtype=jnp.float32) / cells_edge).reshape(shape_one)
    merged = (
        jnp.expand_dims(before, dimension + 1) * (1.0 - fraction)
        + jnp.expand_dims(after, dimension + 1) * fraction
    )
    new_shape = list(volume.shape)
    new_shape[dimension] = (length - 1) * cells_edge
    return merged.reshape(new_shape)


def collect_axis(volume, dimension, cells_edge, squared):
    elements = volume.shape[dimension] // cells_edge
    split_shape = (
        list(volume.shape[:dimension])
        + [elements, cells_edge]
        + list(volume.shape[dimension + 1 :])
    )
    pieces = volume.reshape(split_shape)
    shape_one = [1] * len(split_shape)
    shape_one[dimension + 1] = cells_edge
    fraction = (jnp.arange(cells_edge, dtype=jnp.float32) / cells_edge).reshape(shape_one)
    weight_low = 1.0 - fraction
    weight_high = fraction
    if squared:
        weight_low = weight_low * weight_low
        weight_high = weight_high * weight_high
    low_side = jnp.sum(pieces * weight_low, axis=dimension + 1)
    high_side = jnp.sum(pieces * weight_high, axis=dimension + 1)
    return lax.slice_in_dim(low_side, 1, elements, axis=dimension) + lax.slice_in_dim(
        high_side, 0, elements - 1, axis=dimension
    )


def pair_op(volume, dimension, factor):
    length = volume.shape[dimension]
    return lax.slice_in_dim(volume, 1, length, axis=dimension) + factor * lax.slice_in_dim(
        volume, 0, length - 1, axis=dimension
    )


def cross_pairs(volume, chosen, factor, offset):
    for dimension in range(3):
        volume = pair_op(volume, dimension + offset, factor if dimension == chosen else 1.0)
    return volume


def elastic_force(padded):
    gradients = [cross_pairs(padded, chosen, -1.0, 1) * (1.0 / (4.0 * ELEM)) for chosen in range(3)]
    deform = [
        [gradients[source][target] + (1.0 if target == source else 0.0) for source in range(3)]
        for target in range(3)
    ]
    strain = [
        [
            0.5
            * (
                deform[0][target] * deform[0][source]
                + deform[1][target] * deform[1][source]
                + deform[2][target] * deform[2][source]
            )
            - (0.5 if target == source else 0.0)
            for source in range(3)
        ]
        for target in range(3)
    ]
    trace_strain = strain[0][0] + strain[1][1] + strain[2][2]
    stress = [
        [
            2.0 * shear_modulus * strain[target][source]
            + (lame_lambda * trace_strain if target == source else 0.0)
            for source in range(3)
        ]
        for target in range(3)
    ]
    nominal = [
        [
            deform[target][0] * stress[0][source]
            + deform[target][1] * stress[1][source]
            + deform[target][2] * stress[2][source]
            for source in range(3)
        ]
        for target in range(3)
    ]
    coefficient = ELEM * ELEM / 4.0
    forces = []
    for target in range(3):
        summed = cross_pairs(nominal[target][0], 0, -1.0, 0)
        for source in range(1, 3):
            summed = summed + cross_pairs(nominal[target][source], source, -1.0, 0)
        forces.append(-coefficient * summed)
    return jnp.stack(forces)


def axis_table(nodes_len, cells_edge, squared):
    voxels = (nodes_len - 1) * cells_edge
    column = jnp.arange(voxels, dtype=jnp.int32)
    element = column // cells_edge
    fraction = (column % cells_edge).astype(jnp.float32) / cells_edge
    weight_low = 1.0 - fraction
    weight_high = fraction
    if squared:
        weight_low = weight_low * weight_low
        weight_high = weight_high * weight_high
    node_row = jnp.arange(nodes_len, dtype=jnp.int32)[:, None]
    return jnp.where(node_row == element[None, :], weight_low[None, :], 0.0) + jnp.where(
        node_row == element[None, :] + 1, weight_high[None, :], 0.0
    )


def spread(padded, weights_table):
    shape_all = padded.shape
    stretched = jnp.dot(padded.reshape(-1, shape_all[3]), weights_table, precision=highest)
    stretched = stretched.reshape(shape_all[0], shape_all[1], shape_all[2], weights_table.shape[1])
    stretched = interp_axis(stretched, 1, ELEM)
    return interp_axis(stretched, 2, ELEM)


def collect(volume, table_back, squared):
    shape_all = volume.shape
    reduced = jnp.dot(volume.reshape(-1, shape_all[3]), table_back, precision=highest)
    reduced = reduced.reshape(shape_all[0], shape_all[1], shape_all[2], table_back.shape[1])
    reduced = collect_axis(reduced, 2, ELEM, squared)
    return collect_axis(reduced, 1, ELEM, squared)


NEIGHBOURS = [(0, 0)] + [(ry, rz) for ry in (-1, 0, 1) for rz in (-1, 0, 1) if (ry, rz) != (0, 0)]
HALO_CAP = 10


def per_device(reference_image, deformed_image, roi_mask, displacement, node_map):
    stacked = jnp.stack([reference_image, deformed_image, roi_mask.astype(jnp.bfloat16)])
    stacked = with_halo(stacked, (("gy", 2),), 5)
    stacked = with_halo(stacked, (("gz", 3),), 5 + ELEM)
    nodes_shape = (
        3,
        reference_image.shape[0] // ELEM,
        reference_image.shape[1] // ELEM,
        reference_image.shape[2] // ELEM,
    )
    _, ex, ey, ez = nodes_shape
    wide_table = axis_table(ez + 4, ELEM, False)
    wide_back = wide_table[1:-1].T
    wide_square = axis_table(ez + 4, ELEM, True)[1:-1].T
    size_y = lax.axis_size("gy")
    size_z = lax.axis_size("gz")
    members = size_y * size_z
    blocks = node_map.shape[0]
    block_nodes = displacement.shape[2]
    zchunks = ez // block_nodes
    owner_tile = node_map // blocks
    tile_block = node_map % blocks
    tile_y = owner_tile // size_z
    tile_z = owner_tile % size_z
    block_y = (tile_block // zchunks) % ey
    block_zc = tile_block % zchunks
    dests, valids, labels = [], [], []
    for index, (ry, rz) in enumerate(NEIGHBOURS):
        dest_y = tile_y - ry
        dest_z = tile_z - rz
        valid = (dest_y >= 0) & (dest_y < size_y) & (dest_z >= 0) & (dest_z < size_z)
        if ry == -1:
            valid = valid & (block_y == ey - 1)
        elif ry == 1:
            valid = valid & (block_y == 0)
        if rz == -1:
            valid = valid & (block_zc == zchunks - 1)
        elif rz == 1:
            valid = valid & (block_zc == 0)
        dests.append(dest_y * size_z + dest_z)
        valids.append(valid)
        labels.append(index * blocks + tile_block + 1)
    cand_dest = jnp.concatenate(dests)
    cand_valid = jnp.concatenate(valids)
    cand_label = jnp.concatenate(labels).astype(jnp.float32)
    count = cand_dest.shape[0]
    order = jnp.arange(count, dtype=jnp.int32)
    earlier = (
        (cand_dest[:, None] == cand_dest[None, :])
        & cand_valid[None, :]
        & (order[None, :] < order[:, None])
    )
    ranking = jnp.sum(earlier.astype(jnp.int32), axis=1)
    target_slot = jnp.where(cand_valid, cand_dest * HALO_CAP + ranking, -1)
    packing = (
        target_slot[:, None] == jnp.arange(members * HALO_CAP, dtype=jnp.int32)[None, :]
    ).astype(jnp.float32)
    cand_data = jnp.concatenate(
        [
            jnp.concatenate([displacement] * len(NEIGHBOURS), axis=1),
            jnp.broadcast_to(cand_label[None, :, None], (1, count, block_nodes)),
        ]
    )
    send_channels = cand_data.shape[0]
    send_outgoing = jnp.einsum("cjn,jp->cpn", cand_data, packing, precision=highest).reshape(
        send_channels, -1
    )
    send_incoming = lax.all_to_all(
        send_outgoing, ("gy", "gz"), split_axis=1, concat_axis=1, tiled=True
    ).reshape(send_channels, members * HALO_CAP, block_nodes)
    received_labels = send_incoming[3, :, 0]
    placing = (
        received_labels[:, None] == jnp.arange(1, count + 1, dtype=jnp.float32)[None, :]
    ).astype(jnp.float32)
    around = jnp.einsum("cpn,pk->ckn", send_incoming[:3], placing, precision=highest).reshape(
        3, len(NEIGHBOURS), ex, ey, ez
    )

    def near(ry, rz):
        return around[:, NEIGHBOURS.index((ry, rz))]

    centre = near(0, 0)
    middle = jnp.concatenate(
        [near(0, -1)[..., ez - 2 :], centre, near(0, 1)[..., :2]], axis=3
    )
    low_row = jnp.concatenate(
        [
            near(-1, -1)[:, :, ey - 1 :, ez - 2 :],
            near(-1, 0)[:, :, ey - 1 :, :],
            near(-1, 1)[:, :, ey - 1 :, :2],
        ],
        axis=3,
    )
    high_row = jnp.concatenate(
        [near(1, -1)[:, :, :1, ez - 2 :], near(1, 0)[:, :, :1, :], near(1, 1)[:, :, :1, :2]],
        axis=3,
    )
    extended = jnp.concatenate([low_row, middle, high_row], axis=2)
    padded_images, first_padded = with_halo_pair(stacked, extended, (("gx", 1, 1),), (5, 1))
    padded_images = padded_images.astype(jnp.float32)
    derived = derive_fields(padded_images[0], padded_images[1])
    region = padded_images[2][3:-3, 3:-3, 3:-3]
    contrast = derived[0].astype(jnp.float32)
    slopes = derived[1:].astype(jnp.float32)
    masked_slopes = slopes * region[None]
    wide_curvature = collect(masked_slopes * slopes, wide_square, True) + diagonal_shift
    moved = spread(first_padded, wide_table)
    residual = contrast + slopes[0] * moved[0] + slopes[1] * moved[1] + slopes[2] * moved[2]
    image_part = collect(masked_slopes * residual[None], wide_back, False)
    force_total = image_part + elastic_weight * elastic_force(first_padded)
    wide_values = first_padded[:, 1:-1, 1:-1, 1:-1] - force_total / wide_curvature
    column = jnp.arange(ez + 2, dtype=jnp.int32)
    ghost = ((column == 0) & (lax.axis_index("gz") == 0)) | (
        (column == ez + 1) & (lax.axis_index("gz") == size_z - 1)
    )
    wide_values = jnp.where(ghost, 0.0, wide_values)
    padded = with_halo(wide_values, (("gx", 1), ("gy", 2)), 1)
    padded = jnp.pad(padded, ((0, 0), (0, 0), (0, 0), (1, 1)))
    moved = spread(padded, wide_table)
    residual = contrast + slopes[0] * moved[0] + slopes[1] * moved[1] + slopes[2] * moved[2]
    image_part = collect(masked_slopes * residual[None], wide_back, False)
    force_total = image_part + elastic_weight * elastic_force(padded)
    tile_values = (wide_values - force_total / wide_curvature)[..., 1:-1]
    final_blocks = tile_values.reshape(3, blocks, block_nodes)
    own_labels = received_labels.reshape(members, HALO_CAP)[:, :CAP].reshape(-1)
    position = jnp.arange(blocks, dtype=jnp.int32)
    back_placing = (own_labels[:, None] == (position + 1).astype(jnp.float32)[None, :]).astype(
        jnp.float32
    )
    outgoing = jnp.einsum("ckn,pk->cpn", final_blocks, back_placing, precision=highest).reshape(
        3, -1
    )
    incoming = lax.all_to_all(outgoing, ("gy", "gz"), split_axis=1, concat_axis=1, tiled=True)
    own_slot = owner_tile * CAP + ranking[:blocks]
    back_packing = (
        own_slot[:, None] == jnp.arange(members * CAP, dtype=jnp.int32)[None, :]
    ).astype(jnp.float32)
    return jnp.einsum(
        "cpn,jp->cjn", incoming.reshape(3, members * CAP, -1), back_packing, precision=highest
    )


def solution(mesh):
    in_specs = (
        P("gx", "gy", "gz"),
        P("gx", "gy", "gz"),
        P("gx", "gy", "gz"),
        P(None, ("gx", "gy", "gz"), None),
        P(("gx", "gy", "gz")),
    )
    out_specs = P(None, ("gx", "gy", "gz"), None)
    return jax.shard_map(
        per_device, mesh=mesh, in_specs=in_specs, out_specs=out_specs, check_vma=False
    )
```

```python
import jax
import jax.numpy as jnp
from jax import lax
from jax.sharding import PartitionSpec as P

ELEM = 4
ITERS = 2
CAP = 2


binomial = (0.0625, 0.25, 0.375, 0.25, 0.0625)
lame_lambda = 1.0
shear_modulus = 0.5
elastic_weight = 2.0
diagonal_shift = 6.0
highest = lax.Precision.HIGHEST


def with_halo(block, sides, width):
    for axis, dim in sides:
        count = lax.axis_size(axis)
        forward = [(i, i + 1) for i in range(count - 1)]
        backward = [(target, source) for source, target in forward]
        low = lax.ppermute(
            lax.slice_in_dim(block, block.shape[dim] - width, None, axis=dim), axis, forward
        )
        high = lax.ppermute(lax.slice_in_dim(block, 0, width, axis=dim), axis, backward)
        block = jnp.concatenate([low, block, high], axis=dim)
    return block


def with_halo_pair(first, second, sides, widths):
    for axis, first_dim, second_dim in sides:
        count = lax.axis_size(axis)
        forward = [(i, i + 1) for i in range(count - 1)]
        backward = [(target, source) for source, target in forward]
        parts = []
        for block, dim, width in ((first, first_dim, widths[0]), (second, second_dim, widths[1])):
            parts.append(
                (
                    lax.slice_in_dim(block, block.shape[dim] - width, None, axis=dim),
                    lax.slice_in_dim(block, 0, width, axis=dim),
                )
            )
        low_flat = jnp.concatenate([p[0].reshape(-1) for p in parts])
        high_flat = jnp.concatenate([p[1].reshape(-1) for p in parts])
        low_flat = lax.ppermute(low_flat, axis, forward)
        high_flat = lax.ppermute(high_flat, axis, backward)
        split = parts[0][0].size
        pieces = []
        for index, (block, dim) in enumerate(((first, first_dim), (second, second_dim))):
            shape = parts[index][0].shape
            begin, end = (0, split) if index == 0 else (split, low_flat.shape[0])
            low = low_flat[begin:end].reshape(shape)
            high = high_flat[begin:end].reshape(shape)
            pieces.append(jnp.concatenate([low, block, high], axis=dim))
        first, second = pieces
    return first, second


def smooth_axis(volume, dimension):
    length = volume.shape[dimension] - 4
    summed = binomial[0] * lax.slice_in_dim(volume, 0, length, axis=dimension)
    for offset in range(1, 5):
        summed = summed + binomial[offset] * lax.slice_in_dim(
            volume, offset, offset + length, axis=dimension
        )
    return summed


def derive_fields(first_padded, second_padded):
    first_smooth = first_padded
    second_smooth = second_padded
    for dimension in range(3):
        first_smooth = smooth_axis(first_smooth, dimension)
        second_smooth = smooth_axis(second_smooth, dimension)
    average = (first_smooth + second_smooth) * 0.5
    contrast = (second_smooth - first_smooth)[1:-1, 1:-1, 1:-1].astype(jnp.bfloat16)
    slopes = []
    for dimension in range(3):
        length = average.shape[dimension] - 2
        forward_part = lax.slice_in_dim(average, 2, length + 2, axis=dimension)
        backward_part = lax.slice_in_dim(average, 0, length, axis=dimension)
        gradient = (forward_part - backward_part) * 0.5
        for cropped_dim in range(3):
            if cropped_dim != dimension:
                gradient = lax.slice_in_dim(
                    gradient, 1, gradient.shape[cropped_dim] - 1, axis=cropped_dim
                )
        slopes.append(gradient.astype(jnp.bfloat16))
    return jnp.stack([contrast] + slopes)


def interp_axis(volume, dimension, cells_edge):
    length = volume.shape[dimension]
    before = lax.slice_in_dim(volume, 0, length - 1, axis=dimension)
    after = lax.slice_in_dim(volume, 1, length, axis=dimension)
    shape_one = [1] * (volume.ndim + 1)
    shape_one[dimension + 1] = cells_edge
    fraction = (jnp.arange(cells_edge, dtype=jnp.float32) / cells_edge).reshape(shape_one)
    merged = (
        jnp.expand_dims(before, dimension + 1) * (1.0 - fraction)
        + jnp.expand_dims(after, dimension + 1) * fraction
    )
    new_shape = list(volume.shape)
    new_shape[dimension] = (length - 1) * cells_edge
    return merged.reshape(new_shape)


def collect_axis(volume, dimension, cells_edge, squared):
    elements = volume.shape[dimension] // cells_edge
    split_shape = (
        list(volume.shape[:dimension])
        + [elements, cells_edge]
        + list(volume.shape[dimension + 1 :])
    )
    pieces = volume.reshape(split_shape)
    shape_one = [1] * len(split_shape)
    shape_one[dimension + 1] = cells_edge
    fraction = (jnp.arange(cells_edge, dtype=jnp.float32) / cells_edge).reshape(shape_one)
    weight_low = 1.0 - fraction
    weight_high = fraction
    if squared:
        weight_low = weight_low * weight_low
        weight_high = weight_high * weight_high
    low_side = jnp.sum(pieces * weight_low, axis=dimension + 1)
    high_side = jnp.sum(pieces * weight_high, axis=dimension + 1)
    return lax.slice_in_dim(low_side, 1, elements, axis=dimension) + lax.slice_in_dim(
        high_side, 0, elements - 1, axis=dimension
    )


def pair_op(volume, dimension, factor):
    length = volume.shape[dimension]
    return lax.slice_in_dim(volume, 1, length, axis=dimension) + factor * lax.slice_in_dim(
        volume, 0, length - 1, axis=dimension
    )


def cross_pairs(volume, chosen, factor, offset):
    for dimension in range(3):
        volume = pair_op(volume, dimension + offset, factor if dimension == chosen else 1.0)
    return volume


def elastic_force(padded):
    gradients = [cross_pairs(padded, chosen, -1.0, 1) * (1.0 / (4.0 * ELEM)) for chosen in range(3)]
    deform = [
        [gradients[source][target] + (1.0 if target == source else 0.0) for source in range(3)]
        for target in range(3)
    ]
    strain = [
        [
            0.5
            * (
                deform[0][target] * deform[0][source]
                + deform[1][target] * deform[1][source]
                + deform[2][target] * deform[2][source]
            )
            - (0.5 if target == source else 0.0)
            for source in range(3)
        ]
        for target in range(3)
    ]
    trace_strain = strain[0][0] + strain[1][1] + strain[2][2]
    stress = [
        [
            2.0 * shear_modulus * strain[target][source]
            + (lame_lambda * trace_strain if target == source else 0.0)
            for source in range(3)
        ]
        for target in range(3)
    ]
    nominal = [
        [
            deform[target][0] * stress[0][source]
            + deform[target][1] * stress[1][source]
            + deform[target][2] * stress[2][source]
            for source in range(3)
        ]
        for target in range(3)
    ]
    coefficient = ELEM * ELEM / 4.0
    forces = []
    for target in range(3):
        summed = cross_pairs(nominal[target][0], 0, -1.0, 0)
        for source in range(1, 3):
            summed = summed + cross_pairs(nominal[target][source], source, -1.0, 0)
        forces.append(-coefficient * summed)
    return jnp.stack(forces)


def axis_table(nodes_len, cells_edge, squared):
    voxels = (nodes_len - 1) * cells_edge
    column = jnp.arange(voxels, dtype=jnp.int32)
    element = column // cells_edge
    fraction = (column % cells_edge).astype(jnp.float32) / cells_edge
    weight_low = 1.0 - fraction
    weight_high = fraction
    if squared:
        weight_low = weight_low * weight_low
        weight_high = weight_high * weight_high
    node_row = jnp.arange(nodes_len, dtype=jnp.int32)[:, None]
    return jnp.where(node_row == element[None, :], weight_low[None, :], 0.0) + jnp.where(
        node_row == element[None, :] + 1, weight_high[None, :], 0.0
    )


def spread(padded, weights_table):
    shape_all = padded.shape
    stretched = jnp.dot(padded.reshape(-1, shape_all[3]), weights_table, precision=highest)
    stretched = stretched.reshape(shape_all[0], shape_all[1], shape_all[2], weights_table.shape[1])
    stretched = interp_axis(stretched, 1, ELEM)
    return interp_axis(stretched, 2, ELEM)


def collect(volume, table_back, squared):
    shape_all = volume.shape
    reduced = jnp.dot(volume.reshape(-1, shape_all[3]), table_back, precision=highest)
    reduced = reduced.reshape(shape_all[0], shape_all[1], shape_all[2], table_back.shape[1])
    reduced = collect_axis(reduced, 2, ELEM, squared)
    return collect_axis(reduced, 1, ELEM, squared)


def plane_tables(nodes_x, nodes_y, squared):
    low_x = axis_table(nodes_x, ELEM, squared)
    low_y = axis_table(nodes_y, ELEM, squared)
    return jnp.kron(low_x.T, low_y.T), jnp.kron(low_x[1:-1], low_y[1:-1])


def spread_plane(padded, plane, line):
    channels, nx, ny, nz = padded.shape
    along = jnp.einsum(
        "cij,jz->ciz", padded.reshape(channels, nx * ny, nz), line, precision=highest
    )
    return jnp.einsum("vi,ciz->cvz", plane, along, precision=highest)


def collect_plane(volume, plane_back, line_back, nodes_x, nodes_y):
    along = jnp.einsum("cvz,zk->cvk", volume, line_back, precision=highest)
    summed = jnp.einsum("av,cvk->cak", plane_back, along, precision=highest)
    return summed.reshape(volume.shape[0], nodes_x, nodes_y, line_back.shape[1])


NEIGHBOURS = [(0, 0)] + [(ry, rz) for ry in (-1, 0, 1) for rz in (-1, 0, 1) if (ry, rz) != (0, 0)]
HALO_CAP = 10


def per_device(reference_image, deformed_image, roi_mask, displacement, node_map):
    stacked = jnp.stack([reference_image, deformed_image, roi_mask.astype(jnp.bfloat16)])
    stacked = with_halo(stacked, (("gy", 2),), 5)
    stacked = with_halo(stacked, (("gz", 3),), 5 + ELEM)
    padded_images = with_halo(stacked, (("gx", 1),), 5).astype(jnp.float32)
    nodes_shape = (
        3,
        reference_image.shape[0] // ELEM,
        reference_image.shape[1] // ELEM,
        reference_image.shape[2] // ELEM,
    )
    _, ex, ey, ez = nodes_shape
    wide_table = axis_table(ez + 4, ELEM, False)
    wide_back = wide_table[1:-1].T
    wide_square = axis_table(ez + 4, ELEM, True)[1:-1].T
    size_y = lax.axis_size("gy")
    size_z = lax.axis_size("gz")
    members = size_y * size_z
    blocks = node_map.shape[0]
    block_nodes = displacement.shape[2]
    zchunks = ez // block_nodes
    owner_tile = node_map // blocks
    tile_block = node_map % blocks
    tile_y = owner_tile // size_z
    tile_z = owner_tile % size_z
    block_y = (tile_block // zchunks) % ey
    block_zc = tile_block % zchunks
    dests, valids, labels = [], [], []
    for index, (ry, rz) in enumerate(NEIGHBOURS):
        dest_y = tile_y - ry
        dest_z = tile_z - rz
        valid = (dest_y >= 0) & (dest_y < size_y) & (dest_z >= 0) & (dest_z < size_z)
        if ry == -1:
            valid = valid & (block_y == ey - 1)
        elif ry == 1:
            valid = valid & (block_y == 0)
        if rz == -1:
            valid = valid & (block_zc == zchunks - 1)
        elif rz == 1:
            valid = valid & (block_zc == 0)
        dests.append(dest_y * size_z + dest_z)
        valids.append(valid)
        labels.append(index * blocks + tile_block + 1)
    cand_dest = jnp.concatenate(dests)
    cand_valid = jnp.concatenate(valids)
    cand_label = jnp.concatenate(labels).astype(jnp.float32)
    count = cand_dest.shape[0]
    order = jnp.arange(count, dtype=jnp.int32)
    earlier = (
        (cand_dest[:, None] == cand_dest[None, :])
        & cand_valid[None, :]
        & (order[None, :] < order[:, None])
    )
    ranking = jnp.sum(earlier.astype(jnp.int32), axis=1)
    target_slot = jnp.where(cand_valid, cand_dest * HALO_CAP + ranking, -1)
    packing = (
        target_slot[:, None] == jnp.arange(members * HALO_CAP, dtype=jnp.int32)[None, :]
    ).astype(jnp.float32)
    cand_data = jnp.concatenate(
        [
            jnp.concatenate([displacement] * len(NEIGHBOURS), axis=1),
            jnp.broadcast_to(cand_label[None, :, None], (1, count, block_nodes)),
        ]
    )
    send_channels = cand_data.shape[0]
    send_outgoing = jnp.einsum("cjn,jp->cpn", cand_data, packing, precision=highest).reshape(
        send_channels, -1
    )
    send_incoming = lax.all_to_all(
        send_outgoing, ("gy", "gz"), split_axis=1, concat_axis=1, tiled=True
    ).reshape(send_channels, members * HALO_CAP, block_nodes)
    received_labels = send_incoming[3, :, 0]
    placing = (
        received_labels[:, None] == jnp.arange(1, count + 1, dtype=jnp.float32)[None, :]
    ).astype(jnp.float32)
    around = jnp.einsum("cpn,pk->ckn", send_incoming[:3], placing, precision=highest).reshape(
        3, len(NEIGHBOURS), ex, ey, ez
    )

    def near(ry, rz):
        return around[:, NEIGHBOURS.index((ry, rz))]

    centre = near(0, 0)
    middle = jnp.concatenate(
        [near(0, -1)[..., ez - 2 :], centre, near(0, 1)[..., :2]], axis=3
    )
    low_row = jnp.concatenate(
        [
            near(-1, -1)[:, :, ey - 1 :, ez - 2 :],
            near(-1, 0)[:, :, ey - 1 :, :],
            near(-1, 1)[:, :, ey - 1 :, :2],
        ],
        axis=3,
    )
    high_row = jnp.concatenate(
        [near(1, -1)[:, :, :1, ez - 2 :], near(1, 0)[:, :, :1, :], near(1, 1)[:, :, :1, :2]],
        axis=3,
    )
    extended = jnp.concatenate([low_row, middle, high_row], axis=2)
    first_padded = with_halo(extended, (("gx", 1),), 1)
    derived = derive_fields(padded_images[0], padded_images[1])
    voxels_x, voxels_y, voxels_z = derived.shape[1:]
    derived = derived.reshape(derived.shape[0], voxels_x * voxels_y, voxels_z)
    region = padded_images[2][3:-3, 3:-3, 3:-3].reshape(voxels_x * voxels_y, voxels_z)
    contrast = derived[0].astype(jnp.float32)
    slopes = derived[1:].astype(jnp.float32)
    masked_slopes = slopes * region[None]
    plane, plane_back = plane_tables(ex + 2, ey + 2, False)
    _, plane_square = plane_tables(ex + 2, ey + 2, True)
    wide_curvature = (
        collect_plane(masked_slopes * slopes, plane_square, wide_square, ex, ey) + diagonal_shift
    )
    moved = spread_plane(first_padded, plane, wide_table)
    residual = contrast + slopes[0] * moved[0] + slopes[1] * moved[1] + slopes[2] * moved[2]
    image_part = collect_plane(masked_slopes * residual[None], plane_back, wide_back, ex, ey)
    force_total = image_part + elastic_weight * elastic_force(first_padded)
    wide_values = first_padded[:, 1:-1, 1:-1, 1:-1] - force_total / wide_curvature
    column = jnp.arange(ez + 2, dtype=jnp.int32)
    ghost = ((column == 0) & (lax.axis_index("gz") == 0)) | (
        (column == ez + 1) & (lax.axis_index("gz") == size_z - 1)
    )
    wide_values = jnp.where(ghost, 0.0, wide_values)
    padded = with_halo(wide_values, (("gx", 1), ("gy", 2)), 1)
    padded = jnp.pad(padded, ((0, 0), (0, 0), (0, 0), (1, 1)))
    moved = spread_plane(padded, plane, wide_table)
    residual = contrast + slopes[0] * moved[0] + slopes[1] * moved[1] + slopes[2] * moved[2]
    image_part = collect_plane(masked_slopes * residual[None], plane_back, wide_back, ex, ey)
    force_total = image_part + elastic_weight * elastic_force(padded)
    tile_values = (wide_values - force_total / wide_curvature)[..., 1:-1]
    final_blocks = tile_values.reshape(3, blocks, block_nodes)
    own_labels = received_labels.reshape(members, HALO_CAP)[:, :CAP].reshape(-1)
    position = jnp.arange(blocks, dtype=jnp.int32)
    back_placing = (own_labels[:, None] == (position + 1).astype(jnp.float32)[None, :]).astype(
        jnp.float32
    )
    outgoing = jnp.einsum("ckn,pk->cpn", final_blocks, back_placing, precision=highest).reshape(
        3, -1
    )
    incoming = lax.all_to_all(outgoing, ("gy", "gz"), split_axis=1, concat_axis=1, tiled=True)
    own_slot = owner_tile * CAP + ranking[:blocks]
    back_packing = (
        own_slot[:, None] == jnp.arange(members * CAP, dtype=jnp.int32)[None, :]
    ).astype(jnp.float32)
    return jnp.einsum(
        "cpn,jp->cjn", incoming.reshape(3, members * CAP, -1), back_packing, precision=highest
    )


def solution(mesh):
    in_specs = (
        P("gx", "gy", "gz"),
        P("gx", "gy", "gz"),
        P("gx", "gy", "gz"),
        P(None, ("gx", "gy", "gz"), None),
        P(("gx", "gy", "gz")),
    )
    out_specs = P(None, ("gx", "gy", "gz"), None)
    return jax.shard_map(
        per_device, mesh=mesh, in_specs=in_specs, out_specs=out_specs, check_vma=False
    )
```

```python
import jax
import jax.numpy as jnp
from jax import lax
from jax.sharding import PartitionSpec as P

ELEM = 4
ITERS = 2
CAP = 2


binomial = (0.0625, 0.25, 0.375, 0.25, 0.0625)
lame_lambda = 1.0
shear_modulus = 0.5
elastic_weight = 2.0
diagonal_shift = 6.0
highest = lax.Precision.HIGHEST


def with_halo(block, sides, width):
    for axis, dim in sides:
        count = lax.axis_size(axis)
        forward = [(i, i + 1) for i in range(count - 1)]
        backward = [(target, source) for source, target in forward]
        low = lax.ppermute(
            lax.slice_in_dim(block, block.shape[dim] - width, None, axis=dim), axis, forward
        )
        high = lax.ppermute(lax.slice_in_dim(block, 0, width, axis=dim), axis, backward)
        block = jnp.concatenate([low, block, high], axis=dim)
    return block


def with_halo_pair(first, second, sides, widths):
    for axis, first_dim, second_dim in sides:
        count = lax.axis_size(axis)
        forward = [(i, i + 1) for i in range(count - 1)]
        backward = [(target, source) for source, target in forward]
        parts = []
        for block, dim, width in ((first, first_dim, widths[0]), (second, second_dim, widths[1])):
            parts.append(
                (
                    lax.slice_in_dim(block, block.shape[dim] - width, None, axis=dim),
                    lax.slice_in_dim(block, 0, width, axis=dim),
                )
            )
        low_flat = jnp.concatenate([p[0].reshape(-1) for p in parts])
        high_flat = jnp.concatenate([p[1].reshape(-1) for p in parts])
        low_flat = lax.ppermute(low_flat, axis, forward)
        high_flat = lax.ppermute(high_flat, axis, backward)
        split = parts[0][0].size
        pieces = []
        for index, (block, dim) in enumerate(((first, first_dim), (second, second_dim))):
            shape = parts[index][0].shape
            begin, end = (0, split) if index == 0 else (split, low_flat.shape[0])
            low = low_flat[begin:end].reshape(shape)
            high = high_flat[begin:end].reshape(shape)
            pieces.append(jnp.concatenate([low, block, high], axis=dim))
        first, second = pieces
    return first, second


def smooth_axis(volume, dimension):
    length = volume.shape[dimension] - 4
    summed = binomial[0] * lax.slice_in_dim(volume, 0, length, axis=dimension)
    for offset in range(1, 5):
        summed = summed + binomial[offset] * lax.slice_in_dim(
            volume, offset, offset + length, axis=dimension
        )
    return summed


def derive_fields(first_padded, second_padded):
    first_smooth = first_padded
    second_smooth = second_padded
    for dimension in range(3):
        first_smooth = smooth_axis(first_smooth, dimension)
        second_smooth = smooth_axis(second_smooth, dimension)
    average = (first_smooth + second_smooth) * 0.5
    contrast = (second_smooth - first_smooth)[1:-1, 1:-1, 1:-1].astype(jnp.bfloat16)
    slopes = []
    for dimension in range(3):
        length = average.shape[dimension] - 2
        forward_part = lax.slice_in_dim(average, 2, length + 2, axis=dimension)
        backward_part = lax.slice_in_dim(average, 0, length, axis=dimension)
        gradient = (forward_part - backward_part) * 0.5
        for cropped_dim in range(3):
            if cropped_dim != dimension:
                gradient = lax.slice_in_dim(
                    gradient, 1, gradient.shape[cropped_dim] - 1, axis=cropped_dim
                )
        slopes.append(gradient.astype(jnp.bfloat16))
    return jnp.stack([contrast] + slopes)


def interp_axis(volume, dimension, cells_edge):
    length = volume.shape[dimension]
    before = lax.slice_in_dim(volume, 0, length - 1, axis=dimension)
    after = lax.slice_in_dim(volume, 1, length, axis=dimension)
    shape_one = [1] * (volume.ndim + 1)
    shape_one[dimension + 1] = cells_edge
    fraction = (jnp.arange(cells_edge, dtype=jnp.float32) / cells_edge).reshape(shape_one)
    merged = (
        jnp.expand_dims(before, dimension + 1) * (1.0 - fraction)
        + jnp.expand_dims(after, dimension + 1) * fraction
    )
    new_shape = list(volume.shape)
    new_shape[dimension] = (length - 1) * cells_edge
    return merged.reshape(new_shape)


def collect_axis(volume, dimension, cells_edge, squared):
    elements = volume.shape[dimension] // cells_edge
    split_shape = (
        list(volume.shape[:dimension])
        + [elements, cells_edge]
        + list(volume.shape[dimension + 1 :])
    )
    pieces = volume.reshape(split_shape)
    shape_one = [1] * len(split_shape)
    shape_one[dimension + 1] = cells_edge
    fraction = (jnp.arange(cells_edge, dtype=jnp.float32) / cells_edge).reshape(shape_one)
    weight_low = 1.0 - fraction
    weight_high = fraction
    if squared:
        weight_low = weight_low * weight_low
        weight_high = weight_high * weight_high
    low_side = jnp.sum(pieces * weight_low, axis=dimension + 1)
    high_side = jnp.sum(pieces * weight_high, axis=dimension + 1)
    return lax.slice_in_dim(low_side, 1, elements, axis=dimension) + lax.slice_in_dim(
        high_side, 0, elements - 1, axis=dimension
    )


def pair_op(volume, dimension, factor):
    length = volume.shape[dimension]
    return lax.slice_in_dim(volume, 1, length, axis=dimension) + factor * lax.slice_in_dim(
        volume, 0, length - 1, axis=dimension
    )


def cross_pairs(volume, chosen, factor, offset):
    for dimension in range(3):
        volume = pair_op(volume, dimension + offset, factor if dimension == chosen else 1.0)
    return volume


def elastic_force(padded):
    gradients = [cross_pairs(padded, chosen, -1.0, 1) * (1.0 / (4.0 * ELEM)) for chosen in range(3)]
    deform = [
        [gradients[source][target] + (1.0 if target == source else 0.0) for source in range(3)]
        for target in range(3)
    ]
    strain = [
        [
            0.5
            * (
                deform[0][target] * deform[0][source]
                + deform[1][target] * deform[1][source]
                + deform[2][target] * deform[2][source]
            )
            - (0.5 if target == source else 0.0)
            for source in range(3)
        ]
        for target in range(3)
    ]
    trace_strain = strain[0][0] + strain[1][1] + strain[2][2]
    stress = [
        [
            2.0 * shear_modulus * strain[target][source]
            + (lame_lambda * trace_strain if target == source else 0.0)
            for source in range(3)
        ]
        for target in range(3)
    ]
    nominal = [
        [
            deform[target][0] * stress[0][source]
            + deform[target][1] * stress[1][source]
            + deform[target][2] * stress[2][source]
            for source in range(3)
        ]
        for target in range(3)
    ]
    coefficient = ELEM * ELEM / 4.0
    forces = []
    for target in range(3):
        summed = cross_pairs(nominal[target][0], 0, -1.0, 0)
        for source in range(1, 3):
            summed = summed + cross_pairs(nominal[target][source], source, -1.0, 0)
        forces.append(-coefficient * summed)
    return jnp.stack(forces)


def axis_table(nodes_len, cells_edge, squared):
    voxels = (nodes_len - 1) * cells_edge
    column = jnp.arange(voxels, dtype=jnp.int32)
    element = column // cells_edge
    fraction = (column % cells_edge).astype(jnp.float32) / cells_edge
    weight_low = 1.0 - fraction
    weight_high = fraction
    if squared:
        weight_low = weight_low * weight_low
        weight_high = weight_high * weight_high
    node_row = jnp.arange(nodes_len, dtype=jnp.int32)[:, None]
    return jnp.where(node_row == element[None, :], weight_low[None, :], 0.0) + jnp.where(
        node_row == element[None, :] + 1, weight_high[None, :], 0.0
    )


def spread(padded, weights_table):
    shape_all = padded.shape
    stretched = jnp.dot(padded.reshape(-1, shape_all[3]), weights_table, precision=highest)
    stretched = stretched.reshape(shape_all[0], shape_all[1], shape_all[2], weights_table.shape[1])
    stretched = interp_axis(stretched, 1, ELEM)
    return interp_axis(stretched, 2, ELEM)


def collect(volume, table_back, squared):
    shape_all = volume.shape
    reduced = jnp.dot(volume.reshape(-1, shape_all[3]), table_back, precision=highest)
    reduced = reduced.reshape(shape_all[0], shape_all[1], shape_all[2], table_back.shape[1])
    reduced = collect_axis(reduced, 2, ELEM, squared)
    return collect_axis(reduced, 1, ELEM, squared)


def plane_tables(nodes_x, nodes_y, squared):
    low_x = axis_table(nodes_x, ELEM, squared)
    low_y = axis_table(nodes_y, ELEM, squared)
    return jnp.kron(low_x.T, low_y.T), jnp.kron(low_x[1:-1], low_y[1:-1])


def spread_plane(padded, plane, line):
    channels, nx, ny, nz = padded.shape
    return [
        jnp.dot(
            plane,
            jnp.dot(padded[c].reshape(nx * ny, nz), line, precision=highest),
            precision=highest,
        )
        for c in range(channels)
    ]


def collect_plane(volumes, plane_back, line_back, nodes_x, nodes_y):
    return jnp.stack(
        [
            jnp.dot(
                plane_back, jnp.dot(volume, line_back, precision=highest), precision=highest
            ).reshape(nodes_x, nodes_y, line_back.shape[1])
            for volume in volumes
        ]
    )


NEIGHBOURS = [(0, 0)] + [(ry, rz) for ry in (-1, 0, 1) for rz in (-1, 0, 1) if (ry, rz) != (0, 0)]
HALO_CAP = 10


def per_device(reference_image, deformed_image, roi_mask, displacement, node_map):
    stacked = jnp.stack([reference_image, deformed_image, roi_mask.astype(jnp.bfloat16)])
    stacked = with_halo(stacked, (("gy", 2),), 5)
    stacked = with_halo(stacked, (("gz", 3),), 5 + ELEM)
    padded_images = with_halo(stacked, (("gx", 1),), 5).astype(jnp.float32)
    nodes_shape = (
        3,
        reference_image.shape[0] // ELEM,
        reference_image.shape[1] // ELEM,
        reference_image.shape[2] // ELEM,
    )
    _, ex, ey, ez = nodes_shape
    wide_table = axis_table(ez + 4, ELEM, False)
    wide_back = wide_table[1:-1].T
    wide_square = axis_table(ez + 4, ELEM, True)[1:-1].T
    size_y = lax.axis_size("gy")
    size_z = lax.axis_size("gz")
    members = size_y * size_z
    blocks = node_map.shape[0]
    block_nodes = displacement.shape[2]
    zchunks = ez // block_nodes
    owner_tile = node_map // blocks
    tile_block = node_map % blocks
    tile_y = owner_tile // size_z
    tile_z = owner_tile % size_z
    block_y = (tile_block // zchunks) % ey
    block_zc = tile_block % zchunks
    dests, valids, labels = [], [], []
    for index, (ry, rz) in enumerate(NEIGHBOURS):
        dest_y = tile_y - ry
        dest_z = tile_z - rz
        valid = (dest_y >= 0) & (dest_y < size_y) & (dest_z >= 0) & (dest_z < size_z)
        if ry == -1:
            valid = valid & (block_y == ey - 1)
        elif ry == 1:
            valid = valid & (block_y == 0)
        if rz == -1:
            valid = valid & (block_zc == zchunks - 1)
        elif rz == 1:
            valid = valid & (block_zc == 0)
        dests.append(dest_y * size_z + dest_z)
        valids.append(valid)
        labels.append(index * blocks + tile_block + 1)
    cand_dest = jnp.concatenate(dests)
    cand_valid = jnp.concatenate(valids)
    cand_label = jnp.concatenate(labels).astype(jnp.float32)
    count = cand_dest.shape[0]
    order = jnp.arange(count, dtype=jnp.int32)
    earlier = (
        (cand_dest[:, None] == cand_dest[None, :])
        & cand_valid[None, :]
        & (order[None, :] < order[:, None])
    )
    ranking = jnp.sum(earlier.astype(jnp.int32), axis=1)
    target_slot = jnp.where(cand_valid, cand_dest * HALO_CAP + ranking, -1)
    packing = (
        target_slot[:, None] == jnp.arange(members * HALO_CAP, dtype=jnp.int32)[None, :]
    ).astype(jnp.float32)
    cand_data = jnp.concatenate(
        [
            jnp.concatenate([displacement] * len(NEIGHBOURS), axis=1),
            jnp.broadcast_to(cand_label[None, :, None], (1, count, block_nodes)),
        ]
    )
    send_channels = cand_data.shape[0]
    send_outgoing = jnp.einsum("cjn,jp->cpn", cand_data, packing, precision=highest).reshape(
        send_channels, -1
    )
    send_incoming = lax.all_to_all(
        send_outgoing, ("gy", "gz"), split_axis=1, concat_axis=1, tiled=True
    ).reshape(send_channels, members * HALO_CAP, block_nodes)
    received_labels = send_incoming[3, :, 0]
    placing = (
        received_labels[:, None] == jnp.arange(1, count + 1, dtype=jnp.float32)[None, :]
    ).astype(jnp.float32)
    around = jnp.einsum("cpn,pk->ckn", send_incoming[:3], placing, precision=highest).reshape(
        3, len(NEIGHBOURS), ex, ey, ez
    )

    def near(ry, rz):
        return around[:, NEIGHBOURS.index((ry, rz))]

    centre = near(0, 0)
    middle = jnp.concatenate(
        [near(0, -1)[..., ez - 2 :], centre, near(0, 1)[..., :2]], axis=3
    )
    low_row = jnp.concatenate(
        [
            near(-1, -1)[:, :, ey - 1 :, ez - 2 :],
            near(-1, 0)[:, :, ey - 1 :, :],
            near(-1, 1)[:, :, ey - 1 :, :2],
        ],
        axis=3,
    )
    high_row = jnp.concatenate(
        [near(1, -1)[:, :, :1, ez - 2 :], near(1, 0)[:, :, :1, :], near(1, 1)[:, :, :1, :2]],
        axis=3,
    )
    extended = jnp.concatenate([low_row, middle, high_row], axis=2)
    first_padded = with_halo(extended, (("gx", 1),), 1)
    derived = derive_fields(padded_images[0], padded_images[1])
    voxels_x, voxels_y, voxels_z = derived.shape[1:]
    derived = derived.reshape(derived.shape[0], voxels_x * voxels_y, voxels_z)
    region = padded_images[2][3:-3, 3:-3, 3:-3].reshape(voxels_x * voxels_y, voxels_z)
    contrast = derived[0].astype(jnp.float32)
    slopes = derived[1:].astype(jnp.float32)
    masked_slopes = slopes * region[None]
    plane, plane_back = plane_tables(ex + 2, ey + 2, False)
    _, plane_square = plane_tables(ex + 2, ey + 2, True)
    wide_curvature = (
        collect_plane(
            [masked_slopes[c] * slopes[c] for c in range(3)], plane_square, wide_square, ex, ey
        )
        + diagonal_shift
    )
    moved = spread_plane(first_padded, plane, wide_table)
    residual = contrast + slopes[0] * moved[0] + slopes[1] * moved[1] + slopes[2] * moved[2]
    image_part = collect_plane(
        [masked_slopes[c] * residual for c in range(3)], plane_back, wide_back, ex, ey
    )
    force_total = image_part + elastic_weight * elastic_force(first_padded)
    wide_values = first_padded[:, 1:-1, 1:-1, 1:-1] - force_total / wide_curvature
    column = jnp.arange(ez + 2, dtype=jnp.int32)
    ghost = ((column == 0) & (lax.axis_index("gz") == 0)) | (
        (column == ez + 1) & (lax.axis_index("gz") == size_z - 1)
    )
    wide_values = jnp.where(ghost, 0.0, wide_values)
    padded = with_halo(wide_values, (("gx", 1), ("gy", 2)), 1)
    padded = jnp.pad(padded, ((0, 0), (0, 0), (0, 0), (1, 1)))
    moved = spread_plane(padded, plane, wide_table)
    residual = contrast + slopes[0] * moved[0] + slopes[1] * moved[1] + slopes[2] * moved[2]
    image_part = collect_plane(
        [masked_slopes[c] * residual for c in range(3)], plane_back, wide_back, ex, ey
    )
    force_total = image_part + elastic_weight * elastic_force(padded)
    tile_values = (wide_values - force_total / wide_curvature)[..., 1:-1]
    final_blocks = tile_values.reshape(3, blocks, block_nodes)
    own_labels = received_labels.reshape(members, HALO_CAP)[:, :CAP].reshape(-1)
    position = jnp.arange(blocks, dtype=jnp.int32)
    back_placing = (own_labels[:, None] == (position + 1).astype(jnp.float32)[None, :]).astype(
        jnp.float32
    )
    outgoing = jnp.einsum("ckn,pk->cpn", final_blocks, back_placing, precision=highest).reshape(
        3, -1
    )
    incoming = lax.all_to_all(outgoing, ("gy", "gz"), split_axis=1, concat_axis=1, tiled=True)
    own_slot = owner_tile * CAP + ranking[:blocks]
    back_packing = (
        own_slot[:, None] == jnp.arange(members * CAP, dtype=jnp.int32)[None, :]
    ).astype(jnp.float32)
    return jnp.einsum(
        "cpn,jp->cjn", incoming.reshape(3, members * CAP, -1), back_packing, precision=highest
    )


def solution(mesh):
    in_specs = (
        P("gx", "gy", "gz"),
        P("gx", "gy", "gz"),
        P("gx", "gy", "gz"),
        P(None, ("gx", "gy", "gz"), None),
        P(("gx", "gy", "gz")),
    )
    out_specs = P(None, ("gx", "gy", "gz"), None)
    return jax.shard_map(
        per_device, mesh=mesh, in_specs=in_specs, out_specs=out_specs, check_vma=False
    )
```

```python
import jax
import jax.numpy as jnp
from jax import lax
from jax.sharding import PartitionSpec as P

ELEM = 4
ITERS = 2
CAP = 2


binomial = (0.0625, 0.25, 0.375, 0.25, 0.0625)
lame_lambda = 1.0
shear_modulus = 0.5
elastic_weight = 2.0
diagonal_shift = 6.0
highest = lax.Precision.HIGHEST


def with_halo(block, sides, width):
    for axis, dim in sides:
        count = lax.axis_size(axis)
        forward = [(i, i + 1) for i in range(count - 1)]
        backward = [(target, source) for source, target in forward]
        low = lax.ppermute(
            lax.slice_in_dim(block, block.shape[dim] - width, None, axis=dim), axis, forward
        )
        high = lax.ppermute(lax.slice_in_dim(block, 0, width, axis=dim), axis, backward)
        block = jnp.concatenate([low, block, high], axis=dim)
    return block


def with_halo_pair(first, second, sides, widths):
    for axis, first_dim, second_dim in sides:
        count = lax.axis_size(axis)
        forward = [(i, i + 1) for i in range(count - 1)]
        backward = [(target, source) for source, target in forward]
        parts = []
        for block, dim, width in ((first, first_dim, widths[0]), (second, second_dim, widths[1])):
            parts.append(
                (
                    lax.slice_in_dim(block, block.shape[dim] - width, None, axis=dim),
                    lax.slice_in_dim(block, 0, width, axis=dim),
                )
            )
        low_flat = jnp.concatenate([p[0].reshape(-1) for p in parts])
        high_flat = jnp.concatenate([p[1].reshape(-1) for p in parts])
        low_flat = lax.ppermute(low_flat, axis, forward)
        high_flat = lax.ppermute(high_flat, axis, backward)
        split = parts[0][0].size
        pieces = []
        for index, (block, dim) in enumerate(((first, first_dim), (second, second_dim))):
            shape = parts[index][0].shape
            begin, end = (0, split) if index == 0 else (split, low_flat.shape[0])
            low = low_flat[begin:end].reshape(shape)
            high = high_flat[begin:end].reshape(shape)
            pieces.append(jnp.concatenate([low, block, high], axis=dim))
        first, second = pieces
    return first, second


def smooth_axis(volume, dimension):
    length = volume.shape[dimension] - 4
    summed = binomial[0] * lax.slice_in_dim(volume, 0, length, axis=dimension)
    for offset in range(1, 5):
        summed = summed + binomial[offset] * lax.slice_in_dim(
            volume, offset, offset + length, axis=dimension
        )
    return summed


def derive_fields(first_padded, second_padded):
    first_smooth = first_padded
    second_smooth = second_padded
    for dimension in range(3):
        first_smooth = smooth_axis(first_smooth, dimension)
        second_smooth = smooth_axis(second_smooth, dimension)
    average = (first_smooth + second_smooth) * 0.5
    contrast = (second_smooth - first_smooth)[1:-1, 1:-1, 1:-1].astype(jnp.bfloat16)
    slopes = []
    for dimension in range(3):
        length = average.shape[dimension] - 2
        forward_part = lax.slice_in_dim(average, 2, length + 2, axis=dimension)
        backward_part = lax.slice_in_dim(average, 0, length, axis=dimension)
        gradient = (forward_part - backward_part) * 0.5
        for cropped_dim in range(3):
            if cropped_dim != dimension:
                gradient = lax.slice_in_dim(
                    gradient, 1, gradient.shape[cropped_dim] - 1, axis=cropped_dim
                )
        slopes.append(gradient.astype(jnp.bfloat16))
    return jnp.stack([contrast] + slopes)


def interp_axis(volume, dimension, cells_edge):
    length = volume.shape[dimension]
    before = lax.slice_in_dim(volume, 0, length - 1, axis=dimension)
    after = lax.slice_in_dim(volume, 1, length, axis=dimension)
    shape_one = [1] * (volume.ndim + 1)
    shape_one[dimension + 1] = cells_edge
    fraction = (jnp.arange(cells_edge, dtype=jnp.float32) / cells_edge).reshape(shape_one)
    merged = (
        jnp.expand_dims(before, dimension + 1) * (1.0 - fraction)
        + jnp.expand_dims(after, dimension + 1) * fraction
    )
    new_shape = list(volume.shape)
    new_shape[dimension] = (length - 1) * cells_edge
    return merged.reshape(new_shape)


def collect_axis(volume, dimension, cells_edge, squared):
    elements = volume.shape[dimension] // cells_edge
    split_shape = (
        list(volume.shape[:dimension])
        + [elements, cells_edge]
        + list(volume.shape[dimension + 1 :])
    )
    pieces = volume.reshape(split_shape)
    shape_one = [1] * len(split_shape)
    shape_one[dimension + 1] = cells_edge
    fraction = (jnp.arange(cells_edge, dtype=jnp.float32) / cells_edge).reshape(shape_one)
    weight_low = 1.0 - fraction
    weight_high = fraction
    if squared:
        weight_low = weight_low * weight_low
        weight_high = weight_high * weight_high
    low_side = jnp.sum(pieces * weight_low, axis=dimension + 1)
    high_side = jnp.sum(pieces * weight_high, axis=dimension + 1)
    return lax.slice_in_dim(low_side, 1, elements, axis=dimension) + lax.slice_in_dim(
        high_side, 0, elements - 1, axis=dimension
    )


def pair_op(volume, dimension, factor):
    length = volume.shape[dimension]
    return lax.slice_in_dim(volume, 1, length, axis=dimension) + factor * lax.slice_in_dim(
        volume, 0, length - 1, axis=dimension
    )


def cross_pairs(volume, chosen, factor, offset):
    for dimension in range(3):
        volume = pair_op(volume, dimension + offset, factor if dimension == chosen else 1.0)
    return volume


def elastic_force(padded):
    gradients = [cross_pairs(padded, chosen, -1.0, 1) * (1.0 / (4.0 * ELEM)) for chosen in range(3)]
    deform = [
        [gradients[source][target] + (1.0 if target == source else 0.0) for source in range(3)]
        for target in range(3)
    ]
    strain = [
        [
            0.5
            * (
                deform[0][target] * deform[0][source]
                + deform[1][target] * deform[1][source]
                + deform[2][target] * deform[2][source]
            )
            - (0.5 if target == source else 0.0)
            for source in range(3)
        ]
        for target in range(3)
    ]
    trace_strain = strain[0][0] + strain[1][1] + strain[2][2]
    stress = [
        [
            2.0 * shear_modulus * strain[target][source]
            + (lame_lambda * trace_strain if target == source else 0.0)
            for source in range(3)
        ]
        for target in range(3)
    ]
    nominal = [
        [
            deform[target][0] * stress[0][source]
            + deform[target][1] * stress[1][source]
            + deform[target][2] * stress[2][source]
            for source in range(3)
        ]
        for target in range(3)
    ]
    coefficient = ELEM * ELEM / 4.0
    forces = []
    for target in range(3):
        summed = cross_pairs(nominal[target][0], 0, -1.0, 0)
        for source in range(1, 3):
            summed = summed + cross_pairs(nominal[target][source], source, -1.0, 0)
        forces.append(-coefficient * summed)
    return jnp.stack(forces)


def axis_table(nodes_len, cells_edge, squared):
    voxels = (nodes_len - 1) * cells_edge
    column = jnp.arange(voxels, dtype=jnp.int32)
    element = column // cells_edge
    fraction = (column % cells_edge).astype(jnp.float32) / cells_edge
    weight_low = 1.0 - fraction
    weight_high = fraction
    if squared:
        weight_low = weight_low * weight_low
        weight_high = weight_high * weight_high
    node_row = jnp.arange(nodes_len, dtype=jnp.int32)[:, None]
    return jnp.where(node_row == element[None, :], weight_low[None, :], 0.0) + jnp.where(
        node_row == element[None, :] + 1, weight_high[None, :], 0.0
    )


def spread(padded, weights_table):
    shape_all = padded.shape
    stretched = jnp.dot(padded.reshape(-1, shape_all[3]), weights_table, precision=highest)
    stretched = stretched.reshape(shape_all[0], shape_all[1], shape_all[2], weights_table.shape[1])
    stretched = interp_axis(stretched, 1, ELEM)
    return interp_axis(stretched, 2, ELEM)


def collect(volume, table_back, squared):
    shape_all = volume.shape
    reduced = jnp.dot(volume.reshape(-1, shape_all[3]), table_back, precision=highest)
    reduced = reduced.reshape(shape_all[0], shape_all[1], shape_all[2], table_back.shape[1])
    reduced = collect_axis(reduced, 2, ELEM, squared)
    return collect_axis(reduced, 1, ELEM, squared)


def split_exact(values):
    high = lax.reduce_precision(values, exponent_bits=8, mantissa_bits=7)
    rest = values - high
    middle = lax.reduce_precision(rest, exponent_bits=8, mantissa_bits=7)
    return jnp.stack([high, middle, rest - middle]).astype(jnp.bfloat16)


def join_exact(pieces):
    pieces = pieces.astype(jnp.float32)
    return (pieces[0] + pieces[1]) + pieces[2]


def x_round(images, nodes, image_width):
    count = lax.axis_size("gx")
    forward = [(i, i + 1) for i in range(count - 1)]
    backward = [(target, source) for source, target in forward]
    face_shape = (1, image_width) + images.shape[2:]
    node_face = (nodes.shape[0], 1) + nodes.shape[2:]
    used = 3 * nodes.shape[0] * node_face[2] * node_face[3]
    room = image_width * images.shape[2] * images.shape[3]

    def pack(image_face, node_slice):
        coded = split_exact(node_slice).reshape(-1)
        coded = jnp.pad(coded, (0, room - used)).reshape(face_shape)
        return jnp.concatenate([image_face, coded])

    low = lax.ppermute(
        pack(images[:, images.shape[1] - image_width :], nodes[:, nodes.shape[1] - 1 :]),
        "gx",
        forward,
    )
    high = lax.ppermute(pack(images[:, :image_width], nodes[:, :1]), "gx", backward)
    channels = images.shape[0]

    def unpack(buffer):
        coded = buffer[channels:].reshape(-1)[:used].reshape((3,) + node_face)
        return join_exact(coded)

    padded_images = jnp.concatenate([low[:channels], images, high[:channels]], axis=1)
    padded_nodes = jnp.concatenate([unpack(low), nodes, unpack(high)], axis=1)
    return padded_images, padded_nodes


NEIGHBOURS = [(0, 0)] + [(ry, rz) for ry in (-1, 0, 1) for rz in (-1, 0, 1) if (ry, rz) != (0, 0)]
HALO_CAP = 10


def per_device(reference_image, deformed_image, roi_mask, displacement, node_map):
    stacked = jnp.stack([reference_image, deformed_image, roi_mask.astype(jnp.bfloat16)])
    stacked = with_halo(stacked, (("gy", 2),), 5)
    stacked = with_halo(stacked, (("gz", 3),), 5 + ELEM)
    nodes_shape = (
        3,
        reference_image.shape[0] // ELEM,
        reference_image.shape[1] // ELEM,
        reference_image.shape[2] // ELEM,
    )
    _, ex, ey, ez = nodes_shape
    wide_table = axis_table(ez + 4, ELEM, False)
    wide_back = wide_table[1:-1].T
    wide_square = axis_table(ez + 4, ELEM, True)[1:-1].T
    size_y = lax.axis_size("gy")
    size_z = lax.axis_size("gz")
    members = size_y * size_z
    blocks = node_map.shape[0]
    block_nodes = displacement.shape[2]
    zchunks = ez // block_nodes
    owner_tile = node_map // blocks
    tile_block = node_map % blocks
    tile_y = owner_tile // size_z
    tile_z = owner_tile % size_z
    block_y = (tile_block // zchunks) % ey
    block_zc = tile_block % zchunks
    dests, valids, labels = [], [], []
    for index, (ry, rz) in enumerate(NEIGHBOURS):
        dest_y = tile_y - ry
        dest_z = tile_z - rz
        valid = (dest_y >= 0) & (dest_y < size_y) & (dest_z >= 0) & (dest_z < size_z)
        if ry == -1:
            valid = valid & (block_y == ey - 1)
        elif ry == 1:
            valid = valid & (block_y == 0)
        if rz == -1:
            valid = valid & (block_zc == zchunks - 1)
        elif rz == 1:
            valid = valid & (block_zc == 0)
        dests.append(dest_y * size_z + dest_z)
        valids.append(valid)
        labels.append(index * blocks + tile_block + 1)
    cand_dest = jnp.concatenate(dests)
    cand_valid = jnp.concatenate(valids)
    cand_label = jnp.concatenate(labels).astype(jnp.float32)
    count = cand_dest.shape[0]
    order = jnp.arange(count, dtype=jnp.int32)
    earlier = (
        (cand_dest[:, None] == cand_dest[None, :])
        & cand_valid[None, :]
        & (order[None, :] < order[:, None])
    )
    ranking = jnp.sum(earlier.astype(jnp.int32), axis=1)
    target_slot = jnp.where(cand_valid, cand_dest * HALO_CAP + ranking, -1)
    packing = (
        target_slot[:, None] == jnp.arange(members * HALO_CAP, dtype=jnp.int32)[None, :]
    ).astype(jnp.float32)
    cand_data = jnp.concatenate(
        [
            jnp.concatenate([displacement] * len(NEIGHBOURS), axis=1),
            jnp.broadcast_to(cand_label[None, :, None], (1, count, block_nodes)),
        ]
    )
    send_channels = cand_data.shape[0]
    send_outgoing = jnp.einsum("cjn,jp->cpn", cand_data, packing, precision=highest).reshape(
        send_channels, -1
    )
    send_incoming = lax.all_to_all(
        send_outgoing, ("gy", "gz"), split_axis=1, concat_axis=1, tiled=True
    ).reshape(send_channels, members * HALO_CAP, block_nodes)
    received_labels = send_incoming[3, :, 0]
    placing = (
        received_labels[:, None] == jnp.arange(1, count + 1, dtype=jnp.float32)[None, :]
    ).astype(jnp.float32)
    around = jnp.einsum("cpn,pk->ckn", send_incoming[:3], placing, precision=highest).reshape(
        3, len(NEIGHBOURS), ex, ey, ez
    )

    def near(ry, rz):
        return around[:, NEIGHBOURS.index((ry, rz))]

    centre = near(0, 0)
    middle = jnp.concatenate(
        [near(0, -1)[..., ez - 2 :], centre, near(0, 1)[..., :2]], axis=3
    )
    low_row = jnp.concatenate(
        [
            near(-1, -1)[:, :, ey - 1 :, ez - 2 :],
            near(-1, 0)[:, :, ey - 1 :, :],
            near(-1, 1)[:, :, ey - 1 :, :2],
        ],
        axis=3,
    )
    high_row = jnp.concatenate(
        [near(1, -1)[:, :, :1, ez - 2 :], near(1, 0)[:, :, :1, :], near(1, 1)[:, :, :1, :2]],
        axis=3,
    )
    extended = jnp.concatenate([low_row, middle, high_row], axis=2)
    padded_images, first_padded = x_round(stacked, extended, 5)
    padded_images = padded_images.astype(jnp.float32)
    derived = derive_fields(padded_images[0], padded_images[1])
    region = padded_images[2][3:-3, 3:-3, 3:-3]
    contrast = derived[0].astype(jnp.float32)
    slopes = derived[1:].astype(jnp.float32)
    masked_slopes = slopes * region[None]
    wide_curvature = collect(masked_slopes * slopes, wide_square, True) + diagonal_shift
    moved = spread(first_padded, wide_table)
    residual = contrast + slopes[0] * moved[0] + slopes[1] * moved[1] + slopes[2] * moved[2]
    image_part = collect(masked_slopes * residual[None], wide_back, False)
    force_total = image_part + elastic_weight * elastic_force(first_padded)
    wide_values = first_padded[:, 1:-1, 1:-1, 1:-1] - force_total / wide_curvature
    column = jnp.arange(ez + 2, dtype=jnp.int32)
    ghost = ((column == 0) & (lax.axis_index("gz") == 0)) | (
        (column == ez + 1) & (lax.axis_index("gz") == size_z - 1)
    )
    wide_values = jnp.where(ghost, 0.0, wide_values)
    padded = with_halo(wide_values, (("gx", 1), ("gy", 2)), 1)
    padded = jnp.pad(padded, ((0, 0), (0, 0), (0, 0), (1, 1)))
    moved = spread(padded, wide_table)
    residual = contrast + slopes[0] * moved[0] + slopes[1] * moved[1] + slopes[2] * moved[2]
    image_part = collect(masked_slopes * residual[None], wide_back, False)
    force_total = image_part + elastic_weight * elastic_force(padded)
    tile_values = (wide_values - force_total / wide_curvature)[..., 1:-1]
    final_blocks = tile_values.reshape(3, blocks, block_nodes)
    own_labels = received_labels.reshape(members, HALO_CAP)[:, :CAP].reshape(-1)
    position = jnp.arange(blocks, dtype=jnp.int32)
    back_placing = (own_labels[:, None] == (position + 1).astype(jnp.float32)[None, :]).astype(
        jnp.float32
    )
    outgoing = jnp.einsum("ckn,pk->cpn", final_blocks, back_placing, precision=highest).reshape(
        3, -1
    )
    incoming = lax.all_to_all(outgoing, ("gy", "gz"), split_axis=1, concat_axis=1, tiled=True)
    own_slot = owner_tile * CAP + ranking[:blocks]
    back_packing = (
        own_slot[:, None] == jnp.arange(members * CAP, dtype=jnp.int32)[None, :]
    ).astype(jnp.float32)
    return jnp.einsum(
        "cpn,jp->cjn", incoming.reshape(3, members * CAP, -1), back_packing, precision=highest
    )


def solution(mesh):
    in_specs = (
        P("gx", "gy", "gz"),
        P("gx", "gy", "gz"),
        P("gx", "gy", "gz"),
        P(None, ("gx", "gy", "gz"), None),
        P(("gx", "gy", "gz")),
    )
    out_specs = P(None, ("gx", "gy", "gz"), None)
    return jax.shard_map(
        per_device, mesh=mesh, in_specs=in_specs, out_specs=out_specs, check_vma=False
    )
```

```python
import jax
import jax.numpy as jnp
from jax import lax
from jax.sharding import PartitionSpec as P

ELEM = 4
ITERS = 2
CAP = 2


binomial = (0.0625, 0.25, 0.375, 0.25, 0.0625)
lame_lambda = 1.0
shear_modulus = 0.5
elastic_weight = 2.0
diagonal_shift = 6.0
highest = lax.Precision.HIGHEST


def with_halo(block, sides, width):
    for axis, dim in sides:
        count = lax.axis_size(axis)
        forward = [(i, i + 1) for i in range(count - 1)]
        backward = [(target, source) for source, target in forward]
        low = lax.ppermute(
            lax.slice_in_dim(block, block.shape[dim] - width, None, axis=dim), axis, forward
        )
        high = lax.ppermute(lax.slice_in_dim(block, 0, width, axis=dim), axis, backward)
        block = jnp.concatenate([low, block, high], axis=dim)
    return block


def with_halo_pair(first, second, sides, widths):
    for axis, first_dim, second_dim in sides:
        count = lax.axis_size(axis)
        forward = [(i, i + 1) for i in range(count - 1)]
        backward = [(target, source) for source, target in forward]
        parts = []
        for block, dim, width in ((first, first_dim, widths[0]), (second, second_dim, widths[1])):
            parts.append(
                (
                    lax.slice_in_dim(block, block.shape[dim] - width, None, axis=dim),
                    lax.slice_in_dim(block, 0, width, axis=dim),
                )
            )
        low_flat = jnp.concatenate([p[0].reshape(-1) for p in parts])
        high_flat = jnp.concatenate([p[1].reshape(-1) for p in parts])
        low_flat = lax.ppermute(low_flat, axis, forward)
        high_flat = lax.ppermute(high_flat, axis, backward)
        split = parts[0][0].size
        pieces = []
        for index, (block, dim) in enumerate(((first, first_dim), (second, second_dim))):
            shape = parts[index][0].shape
            begin, end = (0, split) if index == 0 else (split, low_flat.shape[0])
            low = low_flat[begin:end].reshape(shape)
            high = high_flat[begin:end].reshape(shape)
            pieces.append(jnp.concatenate([low, block, high], axis=dim))
        first, second = pieces
    return first, second


def smooth_axis(volume, dimension):
    length = volume.shape[dimension] - 4
    summed = binomial[0] * lax.slice_in_dim(volume, 0, length, axis=dimension)
    for offset in range(1, 5):
        summed = summed + binomial[offset] * lax.slice_in_dim(
            volume, offset, offset + length, axis=dimension
        )
    return summed


def derive_fields(first_padded, second_padded):
    first_smooth = first_padded
    second_smooth = second_padded
    for dimension in range(3):
        first_smooth = smooth_axis(first_smooth, dimension)
        second_smooth = smooth_axis(second_smooth, dimension)
    average = (first_smooth + second_smooth) * 0.5
    contrast = (second_smooth - first_smooth)[1:-1, 1:-1, 1:-1].astype(jnp.bfloat16)
    slopes = []
    for dimension in range(3):
        length = average.shape[dimension] - 2
        forward_part = lax.slice_in_dim(average, 2, length + 2, axis=dimension)
        backward_part = lax.slice_in_dim(average, 0, length, axis=dimension)
        gradient = (forward_part - backward_part) * 0.5
        for cropped_dim in range(3):
            if cropped_dim != dimension:
                gradient = lax.slice_in_dim(
                    gradient, 1, gradient.shape[cropped_dim] - 1, axis=cropped_dim
                )
        slopes.append(gradient.astype(jnp.bfloat16))
    return jnp.stack([contrast] + slopes)


def interp_axis(volume, dimension, cells_edge):
    length = volume.shape[dimension]
    before = lax.slice_in_dim(volume, 0, length - 1, axis=dimension)
    after = lax.slice_in_dim(volume, 1, length, axis=dimension)
    shape_one = [1] * (volume.ndim + 1)
    shape_one[dimension + 1] = cells_edge
    fraction = (jnp.arange(cells_edge, dtype=jnp.float32) / cells_edge).reshape(shape_one)
    merged = (
        jnp.expand_dims(before, dimension + 1) * (1.0 - fraction)
        + jnp.expand_dims(after, dimension + 1) * fraction
    )
    new_shape = list(volume.shape)
    new_shape[dimension] = (length - 1) * cells_edge
    return merged.reshape(new_shape)


def collect_axis(volume, dimension, cells_edge, squared):
    elements = volume.shape[dimension] // cells_edge
    split_shape = (
        list(volume.shape[:dimension])
        + [elements, cells_edge]
        + list(volume.shape[dimension + 1 :])
    )
    pieces = volume.reshape(split_shape)
    shape_one = [1] * len(split_shape)
    shape_one[dimension + 1] = cells_edge
    fraction = (jnp.arange(cells_edge, dtype=jnp.float32) / cells_edge).reshape(shape_one)
    weight_low = 1.0 - fraction
    weight_high = fraction
    if squared:
        weight_low = weight_low * weight_low
        weight_high = weight_high * weight_high
    low_side = jnp.sum(pieces * weight_low, axis=dimension + 1)
    high_side = jnp.sum(pieces * weight_high, axis=dimension + 1)
    return lax.slice_in_dim(low_side, 1, elements, axis=dimension) + lax.slice_in_dim(
        high_side, 0, elements - 1, axis=dimension
    )


def pair_op(volume, dimension, factor):
    length = volume.shape[dimension]
    return lax.slice_in_dim(volume, 1, length, axis=dimension) + factor * lax.slice_in_dim(
        volume, 0, length - 1, axis=dimension
    )


def cross_pairs(volume, chosen, factor, offset):
    for dimension in range(3):
        volume = pair_op(volume, dimension + offset, factor if dimension == chosen else 1.0)
    return volume


def elastic_force(padded):
    gradients = [cross_pairs(padded, chosen, -1.0, 1) * (1.0 / (4.0 * ELEM)) for chosen in range(3)]
    deform = [
        [gradients[source][target] + (1.0 if target == source else 0.0) for source in range(3)]
        for target in range(3)
    ]
    strain = [
        [
            0.5
            * (
                deform[0][target] * deform[0][source]
                + deform[1][target] * deform[1][source]
                + deform[2][target] * deform[2][source]
            )
            - (0.5 if target == source else 0.0)
            for source in range(3)
        ]
        for target in range(3)
    ]
    trace_strain = strain[0][0] + strain[1][1] + strain[2][2]
    stress = [
        [
            2.0 * shear_modulus * strain[target][source]
            + (lame_lambda * trace_strain if target == source else 0.0)
            for source in range(3)
        ]
        for target in range(3)
    ]
    nominal = [
        [
            deform[target][0] * stress[0][source]
            + deform[target][1] * stress[1][source]
            + deform[target][2] * stress[2][source]
            for source in range(3)
        ]
        for target in range(3)
    ]
    coefficient = ELEM * ELEM / 4.0
    forces = []
    for target in range(3):
        summed = cross_pairs(nominal[target][0], 0, -1.0, 0)
        for source in range(1, 3):
            summed = summed + cross_pairs(nominal[target][source], source, -1.0, 0)
        forces.append(-coefficient * summed)
    return jnp.stack(forces)


def axis_table(nodes_len, cells_edge, squared):
    voxels = (nodes_len - 1) * cells_edge
    column = jnp.arange(voxels, dtype=jnp.int32)
    element = column // cells_edge
    fraction = (column % cells_edge).astype(jnp.float32) / cells_edge
    weight_low = 1.0 - fraction
    weight_high = fraction
    if squared:
        weight_low = weight_low * weight_low
        weight_high = weight_high * weight_high
    node_row = jnp.arange(nodes_len, dtype=jnp.int32)[:, None]
    return jnp.where(node_row == element[None, :], weight_low[None, :], 0.0) + jnp.where(
        node_row == element[None, :] + 1, weight_high[None, :], 0.0
    )


def spread(padded, weights_table):
    shape_all = padded.shape
    stretched = jnp.dot(padded.reshape(-1, shape_all[3]), weights_table, precision=highest)
    stretched = stretched.reshape(shape_all[0], shape_all[1], shape_all[2], weights_table.shape[1])
    stretched = interp_axis(stretched, 1, ELEM)
    return interp_axis(stretched, 2, ELEM)


def collect(volume, table_back, squared):
    shape_all = volume.shape
    reduced = jnp.dot(volume.reshape(-1, shape_all[3]), table_back, precision=highest)
    reduced = reduced.reshape(shape_all[0], shape_all[1], shape_all[2], table_back.shape[1])
    reduced = collect_axis(reduced, 2, ELEM, squared)
    return collect_axis(reduced, 1, ELEM, squared)


NEIGHBOURS = [(0, 0)] + [(ry, rz) for ry in (-1, 0, 1) for rz in (-1, 0, 1) if (ry, rz) != (0, 0)]
HALO_CAP = 10


def per_device(reference_image, deformed_image, roi_mask, displacement, node_map):
    stacked = jnp.stack([reference_image, deformed_image, roi_mask.astype(jnp.bfloat16)])
    stacked = with_halo(stacked, (("gy", 2),), 5)
    stacked = with_halo(stacked, (("gz", 3),), 5 + ELEM)
    padded_images = with_halo(stacked, (("gx", 1),), 5).astype(jnp.float32)
    nodes_shape = (
        3,
        reference_image.shape[0] // ELEM,
        reference_image.shape[1] // ELEM,
        reference_image.shape[2] // ELEM,
    )
    _, ex, ey, ez = nodes_shape
    wide_table = axis_table(ez + 4, ELEM, False)
    wide_back = wide_table[1:-1].T
    wide_square = axis_table(ez + 4, ELEM, True)[1:-1].T
    size_y = lax.axis_size("gy")
    size_z = lax.axis_size("gz")
    members = size_y * size_z
    blocks = node_map.shape[0]
    block_nodes = displacement.shape[2]
    zchunks = ez // block_nodes
    owner_tile = node_map // blocks
    tile_block = node_map % blocks
    tile_y = owner_tile // size_z
    tile_z = owner_tile % size_z
    block_y = (tile_block // zchunks) % ey
    block_zc = tile_block % zchunks
    dests, valids, labels = [], [], []
    for index, (ry, rz) in enumerate(NEIGHBOURS):
        dest_y = tile_y - ry
        dest_z = tile_z - rz
        valid = (dest_y >= 0) & (dest_y < size_y) & (dest_z >= 0) & (dest_z < size_z)
        if ry == -1:
            valid = valid & (block_y == ey - 1)
        elif ry == 1:
            valid = valid & (block_y == 0)
        if rz == -1:
            valid = valid & (block_zc == zchunks - 1)
        elif rz == 1:
            valid = valid & (block_zc == 0)
        dests.append(dest_y * size_z + dest_z)
        valids.append(valid)
        labels.append(index * blocks + tile_block + 1)
    cand_dest = jnp.concatenate(dests)
    cand_valid = jnp.concatenate(valids)
    cand_label = jnp.concatenate(labels).astype(jnp.float32)
    count = cand_dest.shape[0]
    order = jnp.arange(count, dtype=jnp.int32)
    earlier = (
        (cand_dest[:, None] == cand_dest[None, :])
        & cand_valid[None, :]
        & (order[None, :] < order[:, None])
    )
    ranking = jnp.sum(earlier.astype(jnp.int32), axis=1)
    target_slot = jnp.where(cand_valid, cand_dest * HALO_CAP + ranking, -1)
    packing = (
        target_slot[:, None] == jnp.arange(members * HALO_CAP, dtype=jnp.int32)[None, :]
    ).astype(jnp.float32)
    block_packing = jnp.sum(packing.reshape(len(NEIGHBOURS), blocks, -1), axis=0)
    label_row = jnp.dot(cand_label, packing, precision=highest)
    send_outgoing = jnp.concatenate(
        [
            jnp.einsum("cjn,jp->cpn", displacement, block_packing, precision=highest),
            jnp.broadcast_to(label_row[None, :, None], (1, label_row.shape[0], block_nodes)),
        ]
    )
    send_channels = send_outgoing.shape[0]
    send_outgoing = send_outgoing.reshape(send_channels, -1)
    send_incoming = lax.all_to_all(
        send_outgoing, ("gy", "gz"), split_axis=1, concat_axis=1, tiled=True
    ).reshape(send_channels, members * HALO_CAP, block_nodes)
    received_labels = send_incoming[3, :, 0]
    placing = (
        received_labels[:, None] == jnp.arange(1, count + 1, dtype=jnp.float32)[None, :]
    ).astype(jnp.float32)
    around = jnp.einsum("cpn,pk->ckn", send_incoming[:3], placing, precision=highest).reshape(
        3, len(NEIGHBOURS), ex, ey, ez
    )

    def near(ry, rz):
        return around[:, NEIGHBOURS.index((ry, rz))]

    centre = near(0, 0)
    middle = jnp.concatenate(
        [near(0, -1)[..., ez - 2 :], centre, near(0, 1)[..., :2]], axis=3
    )
    low_row = jnp.concatenate(
        [
            near(-1, -1)[:, :, ey - 1 :, ez - 2 :],
            near(-1, 0)[:, :, ey - 1 :, :],
            near(-1, 1)[:, :, ey - 1 :, :2],
        ],
        axis=3,
    )
    high_row = jnp.concatenate(
        [near(1, -1)[:, :, :1, ez - 2 :], near(1, 0)[:, :, :1, :], near(1, 1)[:, :, :1, :2]],
        axis=3,
    )
    extended = jnp.concatenate([low_row, middle, high_row], axis=2)
    first_padded = with_halo(extended, (("gx", 1),), 1)
    derived = derive_fields(padded_images[0], padded_images[1])
    region = padded_images[2][3:-3, 3:-3, 3:-3]
    contrast = derived[0].astype(jnp.float32)
    slopes = derived[1:].astype(jnp.float32)
    masked_slopes = slopes * region[None]
    wide_curvature = collect(masked_slopes * slopes, wide_square, True) + diagonal_shift
    moved = spread(first_padded, wide_table)
    residual = contrast + slopes[0] * moved[0] + slopes[1] * moved[1] + slopes[2] * moved[2]
    image_part = collect(masked_slopes * residual[None], wide_back, False)
    force_total = image_part + elastic_weight * elastic_force(first_padded)
    wide_values = first_padded[:, 1:-1, 1:-1, 1:-1] - force_total / wide_curvature
    column = jnp.arange(ez + 2, dtype=jnp.int32)
    ghost = ((column == 0) & (lax.axis_index("gz") == 0)) | (
        (column == ez + 1) & (lax.axis_index("gz") == size_z - 1)
    )
    wide_values = jnp.where(ghost, 0.0, wide_values)
    padded = with_halo(wide_values, (("gx", 1), ("gy", 2)), 1)
    padded = jnp.pad(padded, ((0, 0), (0, 0), (0, 0), (1, 1)))
    moved = spread(padded, wide_table)
    residual = contrast + slopes[0] * moved[0] + slopes[1] * moved[1] + slopes[2] * moved[2]
    image_part = collect(masked_slopes * residual[None], wide_back, False)
    force_total = image_part + elastic_weight * elastic_force(padded)
    tile_values = (wide_values - force_total / wide_curvature)[..., 1:-1]
    final_blocks = tile_values.reshape(3, blocks, block_nodes)
    own_labels = received_labels.reshape(members, HALO_CAP)[:, :CAP].reshape(-1)
    position = jnp.arange(blocks, dtype=jnp.int32)
    back_placing = (own_labels[:, None] == (position + 1).astype(jnp.float32)[None, :]).astype(
        jnp.float32
    )
    outgoing = jnp.einsum("ckn,pk->cpn", final_blocks, back_placing, precision=highest).reshape(
        3, -1
    )
    incoming = lax.all_to_all(outgoing, ("gy", "gz"), split_axis=1, concat_axis=1, tiled=True)
    own_slot = owner_tile * CAP + ranking[:blocks]
    back_packing = (
        own_slot[:, None] == jnp.arange(members * CAP, dtype=jnp.int32)[None, :]
    ).astype(jnp.float32)
    return jnp.einsum(
        "cpn,jp->cjn", incoming.reshape(3, members * CAP, -1), back_packing, precision=highest
    )


def solution(mesh):
    in_specs = (
        P("gx", "gy", "gz"),
        P("gx", "gy", "gz"),
        P("gx", "gy", "gz"),
        P(None, ("gx", "gy", "gz"), None),
        P(("gx", "gy", "gz")),
    )
    out_specs = P(None, ("gx", "gy", "gz"), None)
    return jax.shard_map(
        per_device, mesh=mesh, in_specs=in_specs, out_specs=out_specs, check_vma=False
    )
```

```python
import jax
import jax.numpy as jnp
from jax import lax
from jax.sharding import PartitionSpec as P

ELEM = 4
ITERS = 2
CAP = 2


binomial = (0.0625, 0.25, 0.375, 0.25, 0.0625)
lame_lambda = 1.0
shear_modulus = 0.5
elastic_weight = 2.0
diagonal_shift = 6.0
highest = lax.Precision.HIGHEST


def with_halo(block, sides, width):
    for axis, dim in sides:
        count = lax.axis_size(axis)
        forward = [(i, i + 1) for i in range(count - 1)]
        backward = [(target, source) for source, target in forward]
        low = lax.ppermute(
            lax.slice_in_dim(block, block.shape[dim] - width, None, axis=dim), axis, forward
        )
        high = lax.ppermute(lax.slice_in_dim(block, 0, width, axis=dim), axis, backward)
        block = jnp.concatenate([low, block, high], axis=dim)
    return block


def with_halo_pair(first, second, sides, widths):
    for axis, first_dim, second_dim in sides:
        count = lax.axis_size(axis)
        forward = [(i, i + 1) for i in range(count - 1)]
        backward = [(target, source) for source, target in forward]
        parts = []
        for block, dim, width in ((first, first_dim, widths[0]), (second, second_dim, widths[1])):
            parts.append(
                (
                    lax.slice_in_dim(block, block.shape[dim] - width, None, axis=dim),
                    lax.slice_in_dim(block, 0, width, axis=dim),
                )
            )
        low_flat = jnp.concatenate([p[0].reshape(-1) for p in parts])
        high_flat = jnp.concatenate([p[1].reshape(-1) for p in parts])
        low_flat = lax.ppermute(low_flat, axis, forward)
        high_flat = lax.ppermute(high_flat, axis, backward)
        split = parts[0][0].size
        pieces = []
        for index, (block, dim) in enumerate(((first, first_dim), (second, second_dim))):
            shape = parts[index][0].shape
            begin, end = (0, split) if index == 0 else (split, low_flat.shape[0])
            low = low_flat[begin:end].reshape(shape)
            high = high_flat[begin:end].reshape(shape)
            pieces.append(jnp.concatenate([low, block, high], axis=dim))
        first, second = pieces
    return first, second


def smooth_axis(volume, dimension):
    length = volume.shape[dimension] - 4
    summed = binomial[0] * lax.slice_in_dim(volume, 0, length, axis=dimension)
    for offset in range(1, 5):
        summed = summed + binomial[offset] * lax.slice_in_dim(
            volume, offset, offset + length, axis=dimension
        )
    return summed


def derive_fields(first_padded, second_padded, dimensions=(0, 1, 2)):
    first_smooth = first_padded
    second_smooth = second_padded
    for dimension in dimensions:
        first_smooth = smooth_axis(first_smooth, dimension)
        second_smooth = smooth_axis(second_smooth, dimension)
    average = (first_smooth + second_smooth) * 0.5
    contrast = (second_smooth - first_smooth)[1:-1, 1:-1, 1:-1].astype(jnp.bfloat16)
    slopes = []
    for dimension in range(3):
        length = average.shape[dimension] - 2
        forward_part = lax.slice_in_dim(average, 2, length + 2, axis=dimension)
        backward_part = lax.slice_in_dim(average, 0, length, axis=dimension)
        gradient = (forward_part - backward_part) * 0.5
        for cropped_dim in range(3):
            if cropped_dim != dimension:
                gradient = lax.slice_in_dim(
                    gradient, 1, gradient.shape[cropped_dim] - 1, axis=cropped_dim
                )
        slopes.append(gradient.astype(jnp.bfloat16))
    return jnp.stack([contrast] + slopes)


def interp_axis(volume, dimension, cells_edge):
    length = volume.shape[dimension]
    before = lax.slice_in_dim(volume, 0, length - 1, axis=dimension)
    after = lax.slice_in_dim(volume, 1, length, axis=dimension)
    shape_one = [1] * (volume.ndim + 1)
    shape_one[dimension + 1] = cells_edge
    fraction = (jnp.arange(cells_edge, dtype=jnp.float32) / cells_edge).reshape(shape_one)
    merged = (
        jnp.expand_dims(before, dimension + 1) * (1.0 - fraction)
        + jnp.expand_dims(after, dimension + 1) * fraction
    )
    new_shape = list(volume.shape)
    new_shape[dimension] = (length - 1) * cells_edge
    return merged.reshape(new_shape)


def collect_axis(volume, dimension, cells_edge, squared):
    elements = volume.shape[dimension] // cells_edge
    split_shape = (
        list(volume.shape[:dimension])
        + [elements, cells_edge]
        + list(volume.shape[dimension + 1 :])
    )
    pieces = volume.reshape(split_shape)
    shape_one = [1] * len(split_shape)
    shape_one[dimension + 1] = cells_edge
    fraction = (jnp.arange(cells_edge, dtype=jnp.float32) / cells_edge).reshape(shape_one)
    weight_low = 1.0 - fraction
    weight_high = fraction
    if squared:
        weight_low = weight_low * weight_low
        weight_high = weight_high * weight_high
    low_side = jnp.sum(pieces * weight_low, axis=dimension + 1)
    high_side = jnp.sum(pieces * weight_high, axis=dimension + 1)
    return lax.slice_in_dim(low_side, 1, elements, axis=dimension) + lax.slice_in_dim(
        high_side, 0, elements - 1, axis=dimension
    )


def pair_op(volume, dimension, factor):
    length = volume.shape[dimension]
    return lax.slice_in_dim(volume, 1, length, axis=dimension) + factor * lax.slice_in_dim(
        volume, 0, length - 1, axis=dimension
    )


def cross_pairs(volume, chosen, factor, offset):
    for dimension in range(3):
        volume = pair_op(volume, dimension + offset, factor if dimension == chosen else 1.0)
    return volume


def elastic_force(padded):
    gradients = [cross_pairs(padded, chosen, -1.0, 1) * (1.0 / (4.0 * ELEM)) for chosen in range(3)]
    deform = [
        [gradients[source][target] + (1.0 if target == source else 0.0) for source in range(3)]
        for target in range(3)
    ]
    strain = [
        [
            0.5
            * (
                deform[0][target] * deform[0][source]
                + deform[1][target] * deform[1][source]
                + deform[2][target] * deform[2][source]
            )
            - (0.5 if target == source else 0.0)
            for source in range(3)
        ]
        for target in range(3)
    ]
    trace_strain = strain[0][0] + strain[1][1] + strain[2][2]
    stress = [
        [
            2.0 * shear_modulus * strain[target][source]
            + (lame_lambda * trace_strain if target == source else 0.0)
            for source in range(3)
        ]
        for target in range(3)
    ]
    nominal = [
        [
            deform[target][0] * stress[0][source]
            + deform[target][1] * stress[1][source]
            + deform[target][2] * stress[2][source]
            for source in range(3)
        ]
        for target in range(3)
    ]
    coefficient = ELEM * ELEM / 4.0
    forces = []
    for target in range(3):
        summed = cross_pairs(nominal[target][0], 0, -1.0, 0)
        for source in range(1, 3):
            summed = summed + cross_pairs(nominal[target][source], source, -1.0, 0)
        forces.append(-coefficient * summed)
    return jnp.stack(forces)


def axis_table(nodes_len, cells_edge, squared):
    voxels = (nodes_len - 1) * cells_edge
    column = jnp.arange(voxels, dtype=jnp.int32)
    element = column // cells_edge
    fraction = (column % cells_edge).astype(jnp.float32) / cells_edge
    weight_low = 1.0 - fraction
    weight_high = fraction
    if squared:
        weight_low = weight_low * weight_low
        weight_high = weight_high * weight_high
    node_row = jnp.arange(nodes_len, dtype=jnp.int32)[:, None]
    return jnp.where(node_row == element[None, :], weight_low[None, :], 0.0) + jnp.where(
        node_row == element[None, :] + 1, weight_high[None, :], 0.0
    )


def spread(padded, weights_table):
    shape_all = padded.shape
    stretched = jnp.dot(padded.reshape(-1, shape_all[3]), weights_table, precision=highest)
    stretched = stretched.reshape(shape_all[0], shape_all[1], shape_all[2], weights_table.shape[1])
    stretched = interp_axis(stretched, 1, ELEM)
    return interp_axis(stretched, 2, ELEM)


def collect(volume, table_back, squared):
    shape_all = volume.shape
    reduced = jnp.dot(volume.reshape(-1, shape_all[3]), table_back, precision=highest)
    reduced = reduced.reshape(shape_all[0], shape_all[1], shape_all[2], table_back.shape[1])
    reduced = collect_axis(reduced, 2, ELEM, squared)
    return collect_axis(reduced, 1, ELEM, squared)


NEIGHBOURS = [(0, 0)] + [(ry, rz) for ry in (-1, 0, 1) for rz in (-1, 0, 1) if (ry, rz) != (0, 0)]
HALO_CAP = 10


def per_device(reference_image, deformed_image, roi_mask, displacement, node_map):
    stacked = jnp.stack([reference_image, deformed_image, roi_mask.astype(jnp.bfloat16)])
    stacked = with_halo(stacked, (("gy", 2),), 5)
    stacked = with_halo(stacked, (("gz", 3),), 5 + ELEM)
    count_x = lax.axis_size("gx")
    forward_x = [(i, i + 1) for i in range(count_x - 1)]
    backward_x = [(target, source) for source, target in forward_x]
    low_face = lax.ppermute(stacked[:, stacked.shape[1] - 5 :], "gx", forward_x)
    high_face = lax.ppermute(stacked[:, :5], "gx", backward_x)

    def smooth_yz(volume):
        return smooth_axis(smooth_axis(volume.astype(jnp.float32), 2), 3)

    smoothed = jnp.concatenate(
        [smooth_yz(low_face[:2]), smooth_yz(stacked[:2]), smooth_yz(high_face[:2])], axis=1
    )
    mask_padded = jnp.concatenate([low_face[2], stacked[2], high_face[2]], axis=0)
    nodes_shape = (
        3,
        reference_image.shape[0] // ELEM,
        reference_image.shape[1] // ELEM,
        reference_image.shape[2] // ELEM,
    )
    _, ex, ey, ez = nodes_shape
    wide_table = axis_table(ez + 4, ELEM, False)
    wide_back = wide_table[1:-1].T
    wide_square = axis_table(ez + 4, ELEM, True)[1:-1].T
    size_y = lax.axis_size("gy")
    size_z = lax.axis_size("gz")
    members = size_y * size_z
    blocks = node_map.shape[0]
    block_nodes = displacement.shape[2]
    zchunks = ez // block_nodes
    owner_tile = node_map // blocks
    tile_block = node_map % blocks
    tile_y = owner_tile // size_z
    tile_z = owner_tile % size_z
    block_y = (tile_block // zchunks) % ey
    block_zc = tile_block % zchunks
    dests, valids, labels = [], [], []
    for index, (ry, rz) in enumerate(NEIGHBOURS):
        dest_y = tile_y - ry
        dest_z = tile_z - rz
        valid = (dest_y >= 0) & (dest_y < size_y) & (dest_z >= 0) & (dest_z < size_z)
        if ry == -1:
            valid = valid & (block_y == ey - 1)
        elif ry == 1:
            valid = valid & (block_y == 0)
        if rz == -1:
            valid = valid & (block_zc == zchunks - 1)
        elif rz == 1:
            valid = valid & (block_zc == 0)
        dests.append(dest_y * size_z + dest_z)
        valids.append(valid)
        labels.append(index * blocks + tile_block + 1)
    cand_dest = jnp.concatenate(dests)
    cand_valid = jnp.concatenate(valids)
    cand_label = jnp.concatenate(labels).astype(jnp.float32)
    count = cand_dest.shape[0]
    order = jnp.arange(count, dtype=jnp.int32)
    earlier = (
        (cand_dest[:, None] == cand_dest[None, :])
        & cand_valid[None, :]
        & (order[None, :] < order[:, None])
    )
    ranking = jnp.sum(earlier.astype(jnp.int32), axis=1)
    target_slot = jnp.where(cand_valid, cand_dest * HALO_CAP + ranking, -1)
    packing = (
        target_slot[:, None] == jnp.arange(members * HALO_CAP, dtype=jnp.int32)[None, :]
    ).astype(jnp.float32)
    cand_data = jnp.concatenate(
        [
            jnp.concatenate([displacement] * len(NEIGHBOURS), axis=1),
            jnp.broadcast_to(cand_label[None, :, None], (1, count, block_nodes)),
        ]
    )
    send_channels = cand_data.shape[0]
    send_outgoing = jnp.einsum("cjn,jp->cpn", cand_data, packing, precision=highest).reshape(
        send_channels, -1
    )
    send_incoming = lax.all_to_all(
        send_outgoing, ("gy", "gz"), split_axis=1, concat_axis=1, tiled=True
    ).reshape(send_channels, members * HALO_CAP, block_nodes)
    received_labels = send_incoming[3, :, 0]
    placing = (
        received_labels[:, None] == jnp.arange(1, count + 1, dtype=jnp.float32)[None, :]
    ).astype(jnp.float32)
    around = jnp.einsum("cpn,pk->ckn", send_incoming[:3], placing, precision=highest).reshape(
        3, len(NEIGHBOURS), ex, ey, ez
    )

    def near(ry, rz):
        return around[:, NEIGHBOURS.index((ry, rz))]

    centre = near(0, 0)
    middle = jnp.concatenate(
        [near(0, -1)[..., ez - 2 :], centre, near(0, 1)[..., :2]], axis=3
    )
    low_row = jnp.concatenate(
        [
            near(-1, -1)[:, :, ey - 1 :, ez - 2 :],
            near(-1, 0)[:, :, ey - 1 :, :],
            near(-1, 1)[:, :, ey - 1 :, :2],
        ],
        axis=3,
    )
    high_row = jnp.concatenate(
        [near(1, -1)[:, :, :1, ez - 2 :], near(1, 0)[:, :, :1, :], near(1, 1)[:, :, :1, :2]],
        axis=3,
    )
    extended = jnp.concatenate([low_row, middle, high_row], axis=2)
    first_padded = with_halo(extended, (("gx", 1),), 1)
    derived = derive_fields(smoothed[0], smoothed[1], (0,))
    region = mask_padded[3:-3, 3:-3, 3:-3].astype(jnp.float32)
    contrast = derived[0].astype(jnp.float32)
    slopes = derived[1:].astype(jnp.float32)
    masked_slopes = slopes * region[None]
    wide_curvature = collect(masked_slopes * slopes, wide_square, True) + diagonal_shift
    moved = spread(first_padded, wide_table)
    residual = contrast + slopes[0] * moved[0] + slopes[1] * moved[1] + slopes[2] * moved[2]
    image_part = collect(masked_slopes * residual[None], wide_back, False)
    force_total = image_part + elastic_weight * elastic_force(first_padded)
    wide_values = first_padded[:, 1:-1, 1:-1, 1:-1] - force_total / wide_curvature
    column = jnp.arange(ez + 2, dtype=jnp.int32)
    ghost = ((column == 0) & (lax.axis_index("gz") == 0)) | (
        (column == ez + 1) & (lax.axis_index("gz") == size_z - 1)
    )
    wide_values = jnp.where(ghost, 0.0, wide_values)
    padded = with_halo(wide_values, (("gx", 1), ("gy", 2)), 1)
    padded = jnp.pad(padded, ((0, 0), (0, 0), (0, 0), (1, 1)))
    moved = spread(padded, wide_table)
    residual = contrast + slopes[0] * moved[0] + slopes[1] * moved[1] + slopes[2] * moved[2]
    image_part = collect(masked_slopes * residual[None], wide_back, False)
    force_total = image_part + elastic_weight * elastic_force(padded)
    tile_values = (wide_values - force_total / wide_curvature)[..., 1:-1]
    final_blocks = tile_values.reshape(3, blocks, block_nodes)
    own_labels = received_labels.reshape(members, HALO_CAP)[:, :CAP].reshape(-1)
    position = jnp.arange(blocks, dtype=jnp.int32)
    back_placing = (own_labels[:, None] == (position + 1).astype(jnp.float32)[None, :]).astype(
        jnp.float32
    )
    outgoing = jnp.einsum("ckn,pk->cpn", final_blocks, back_placing, precision=highest).reshape(
        3, -1
    )
    incoming = lax.all_to_all(outgoing, ("gy", "gz"), split_axis=1, concat_axis=1, tiled=True)
    own_slot = owner_tile * CAP + ranking[:blocks]
    back_packing = (
        own_slot[:, None] == jnp.arange(members * CAP, dtype=jnp.int32)[None, :]
    ).astype(jnp.float32)
    return jnp.einsum(
        "cpn,jp->cjn", incoming.reshape(3, members * CAP, -1), back_packing, precision=highest
    )


def solution(mesh):
    in_specs = (
        P("gx", "gy", "gz"),
        P("gx", "gy", "gz"),
        P("gx", "gy", "gz"),
        P(None, ("gx", "gy", "gz"), None),
        P(("gx", "gy", "gz")),
    )
    out_specs = P(None, ("gx", "gy", "gz"), None)
    return jax.shard_map(
        per_device, mesh=mesh, in_specs=in_specs, out_specs=out_specs, check_vma=False
    )
```

```python
import jax
import jax.numpy as jnp
from jax import lax
from jax.sharding import PartitionSpec as P

ELEM = 4
ITERS = 2
CAP = 2


binomial = (0.0625, 0.25, 0.375, 0.25, 0.0625)
lame_lambda = 1.0
shear_modulus = 0.5
elastic_weight = 2.0
diagonal_shift = 6.0
highest = lax.Precision.HIGHEST


def with_halo(block, sides, width):
    for axis, dim in sides:
        count = lax.axis_size(axis)
        forward = [(i, i + 1) for i in range(count - 1)]
        backward = [(target, source) for source, target in forward]
        low = lax.ppermute(
            lax.slice_in_dim(block, block.shape[dim] - width, None, axis=dim), axis, forward
        )
        high = lax.ppermute(lax.slice_in_dim(block, 0, width, axis=dim), axis, backward)
        block = jnp.concatenate([low, block, high], axis=dim)
    return block


def with_halo_pair(first, second, sides, widths):
    for axis, first_dim, second_dim in sides:
        count = lax.axis_size(axis)
        forward = [(i, i + 1) for i in range(count - 1)]
        backward = [(target, source) for source, target in forward]
        parts = []
        for block, dim, width in ((first, first_dim, widths[0]), (second, second_dim, widths[1])):
            parts.append(
                (
                    lax.slice_in_dim(block, block.shape[dim] - width, None, axis=dim),
                    lax.slice_in_dim(block, 0, width, axis=dim),
                )
            )
        low_flat = jnp.concatenate([p[0].reshape(-1) for p in parts])
        high_flat = jnp.concatenate([p[1].reshape(-1) for p in parts])
        low_flat = lax.ppermute(low_flat, axis, forward)
        high_flat = lax.ppermute(high_flat, axis, backward)
        split = parts[0][0].size
        pieces = []
        for index, (block, dim) in enumerate(((first, first_dim), (second, second_dim))):
            shape = parts[index][0].shape
            begin, end = (0, split) if index == 0 else (split, low_flat.shape[0])
            low = low_flat[begin:end].reshape(shape)
            high = high_flat[begin:end].reshape(shape)
            pieces.append(jnp.concatenate([low, block, high], axis=dim))
        first, second = pieces
    return first, second


def smooth_axis(volume, dimension):
    length = volume.shape[dimension] - 4
    summed = binomial[0] * lax.slice_in_dim(volume, 0, length, axis=dimension)
    for offset in range(1, 5):
        summed = summed + binomial[offset] * lax.slice_in_dim(
            volume, offset, offset + length, axis=dimension
        )
    return summed


def derive_fields(first_padded, second_padded):
    first_smooth = first_padded
    second_smooth = second_padded
    for dimension in range(3):
        first_smooth = smooth_axis(first_smooth, dimension)
        second_smooth = smooth_axis(second_smooth, dimension)
    average = (first_smooth + second_smooth) * 0.5
    contrast = (second_smooth - first_smooth)[1:-1, 1:-1, 1:-1].astype(jnp.bfloat16)
    slopes = []
    for dimension in range(3):
        length = average.shape[dimension] - 2
        forward_part = lax.slice_in_dim(average, 2, length + 2, axis=dimension)
        backward_part = lax.slice_in_dim(average, 0, length, axis=dimension)
        gradient = (forward_part - backward_part) * 0.5
        for cropped_dim in range(3):
            if cropped_dim != dimension:
                gradient = lax.slice_in_dim(
                    gradient, 1, gradient.shape[cropped_dim] - 1, axis=cropped_dim
                )
        slopes.append(gradient.astype(jnp.bfloat16))
    return jnp.stack([contrast] + slopes)


def interp_axis(volume, dimension, cells_edge):
    length = volume.shape[dimension]
    before = lax.slice_in_dim(volume, 0, length - 1, axis=dimension)
    after = lax.slice_in_dim(volume, 1, length, axis=dimension)
    shape_one = [1] * (volume.ndim + 1)
    shape_one[dimension + 1] = cells_edge
    fraction = (jnp.arange(cells_edge, dtype=jnp.float32) / cells_edge).reshape(shape_one)
    merged = (
        jnp.expand_dims(before, dimension + 1) * (1.0 - fraction)
        + jnp.expand_dims(after, dimension + 1) * fraction
    )
    new_shape = list(volume.shape)
    new_shape[dimension] = (length - 1) * cells_edge
    return merged.reshape(new_shape)


def collect_axis(volume, dimension, cells_edge, squared):
    elements = volume.shape[dimension] // cells_edge
    split_shape = (
        list(volume.shape[:dimension])
        + [elements, cells_edge]
        + list(volume.shape[dimension + 1 :])
    )
    pieces = volume.reshape(split_shape)
    shape_one = [1] * len(split_shape)
    shape_one[dimension + 1] = cells_edge
    fraction = (jnp.arange(cells_edge, dtype=jnp.float32) / cells_edge).reshape(shape_one)
    weight_low = 1.0 - fraction
    weight_high = fraction
    if squared:
        weight_low = weight_low * weight_low
        weight_high = weight_high * weight_high
    low_side = jnp.sum(pieces * weight_low, axis=dimension + 1)
    high_side = jnp.sum(pieces * weight_high, axis=dimension + 1)
    return lax.slice_in_dim(low_side, 1, elements, axis=dimension) + lax.slice_in_dim(
        high_side, 0, elements - 1, axis=dimension
    )


def pair_op(volume, dimension, factor):
    length = volume.shape[dimension]
    return lax.slice_in_dim(volume, 1, length, axis=dimension) + factor * lax.slice_in_dim(
        volume, 0, length - 1, axis=dimension
    )


def cross_pairs(volume, chosen, factor, offset):
    for dimension in range(3):
        volume = pair_op(volume, dimension + offset, factor if dimension == chosen else 1.0)
    return volume


def elastic_force(padded):
    gradients = [cross_pairs(padded, chosen, -1.0, 1) * (1.0 / (4.0 * ELEM)) for chosen in range(3)]
    deform = [
        [gradients[source][target] + (1.0 if target == source else 0.0) for source in range(3)]
        for target in range(3)
    ]
    strain = [
        [
            0.5
            * (
                deform[0][target] * deform[0][source]
                + deform[1][target] * deform[1][source]
                + deform[2][target] * deform[2][source]
            )
            - (0.5 if target == source else 0.0)
            for source in range(3)
        ]
        for target in range(3)
    ]
    trace_strain = strain[0][0] + strain[1][1] + strain[2][2]
    stress = [
        [
            2.0 * shear_modulus * strain[target][source]
            + (lame_lambda * trace_strain if target == source else 0.0)
            for source in range(3)
        ]
        for target in range(3)
    ]
    nominal = [
        [
            deform[target][0] * stress[0][source]
            + deform[target][1] * stress[1][source]
            + deform[target][2] * stress[2][source]
            for source in range(3)
        ]
        for target in range(3)
    ]
    coefficient = ELEM * ELEM / 4.0
    forces = []
    for target in range(3):
        summed = cross_pairs(nominal[target][0], 0, -1.0, 0)
        for source in range(1, 3):
            summed = summed + cross_pairs(nominal[target][source], source, -1.0, 0)
        forces.append(-coefficient * summed)
    return jnp.stack(forces)


def axis_table(nodes_len, cells_edge, squared):
    voxels = (nodes_len - 1) * cells_edge
    column = jnp.arange(voxels, dtype=jnp.int32)
    element = column // cells_edge
    fraction = (column % cells_edge).astype(jnp.float32) / cells_edge
    weight_low = 1.0 - fraction
    weight_high = fraction
    if squared:
        weight_low = weight_low * weight_low
        weight_high = weight_high * weight_high
    node_row = jnp.arange(nodes_len, dtype=jnp.int32)[:, None]
    return jnp.where(node_row == element[None, :], weight_low[None, :], 0.0) + jnp.where(
        node_row == element[None, :] + 1, weight_high[None, :], 0.0
    )


def spread(padded, weights_table):
    shape_all = padded.shape
    stretched = jnp.dot(padded.reshape(-1, shape_all[3]), weights_table, precision=highest)
    stretched = stretched.reshape(shape_all[0], shape_all[1], shape_all[2], weights_table.shape[1])
    stretched = interp_axis(stretched, 1, ELEM)
    return interp_axis(stretched, 2, ELEM)


def collect(volume, table_back, squared):
    shape_all = volume.shape
    reduced = jnp.dot(volume.reshape(-1, shape_all[3]), table_back, precision=highest)
    reduced = reduced.reshape(shape_all[0], shape_all[1], shape_all[2], table_back.shape[1])
    reduced = collect_axis(reduced, 2, ELEM, squared)
    return collect_axis(reduced, 1, ELEM, squared)


NEIGHBOURS = [(0, 0)] + [(ry, rz) for ry in (-1, 0, 1) for rz in (-1, 0, 1) if (ry, rz) != (0, 0)]
HALO_CAP = 10


def per_device(reference_image, deformed_image, roi_mask, displacement, node_map):
    stacked = jnp.stack([reference_image, deformed_image, roi_mask.astype(jnp.bfloat16)])
    stacked = with_halo(stacked, (("gy", 2),), 5)
    stacked = with_halo(stacked, (("gz", 3),), 5 + ELEM)
    padded_images = with_halo(stacked, (("gx", 1),), 5).astype(jnp.float32)
    nodes_shape = (
        3,
        reference_image.shape[0] // ELEM,
        reference_image.shape[1] // ELEM,
        reference_image.shape[2] // ELEM,
    )
    _, ex, ey, ez = nodes_shape
    wide_table = axis_table(ez + 4, ELEM, False)
    wide_back = wide_table[1:-1].T
    wide_square = axis_table(ez + 4, ELEM, True)[1:-1].T
    size_y = lax.axis_size("gy")
    size_z = lax.axis_size("gz")
    members = size_y * size_z
    blocks = node_map.shape[0]
    block_nodes = displacement.shape[2]
    zchunks = ez // block_nodes
    owner_tile = node_map // blocks
    tile_block = node_map % blocks
    tile_y = owner_tile // size_z
    tile_z = owner_tile % size_z
    block_y = (tile_block // zchunks) % ey
    block_zc = tile_block % zchunks
    dests, valids, labels = [], [], []
    for index, (ry, rz) in enumerate(NEIGHBOURS):
        dest_y = tile_y - ry
        dest_z = tile_z - rz
        valid = (dest_y >= 0) & (dest_y < size_y) & (dest_z >= 0) & (dest_z < size_z)
        if ry == -1:
            valid = valid & (block_y == ey - 1)
        elif ry == 1:
            valid = valid & (block_y == 0)
        if rz == -1:
            valid = valid & (block_zc == zchunks - 1)
        elif rz == 1:
            valid = valid & (block_zc == 0)
        dests.append(dest_y * size_z + dest_z)
        valids.append(valid)
        labels.append(index * blocks + tile_block + 1)
    cand_dest = jnp.concatenate(dests)
    cand_valid = jnp.concatenate(valids)
    cand_label = jnp.concatenate(labels).astype(jnp.float32)
    count = cand_dest.shape[0]
    order = jnp.arange(count, dtype=jnp.int32)
    earlier = (
        (cand_dest[:, None] == cand_dest[None, :])
        & cand_valid[None, :]
        & (order[None, :] < order[:, None])
    )
    ranking = jnp.sum(earlier.astype(jnp.int32), axis=1)
    target_slot = jnp.where(cand_valid, cand_dest * HALO_CAP + ranking, -1)
    packing = (
        target_slot[:, None] == jnp.arange(members * HALO_CAP, dtype=jnp.int32)[None, :]
    ).astype(jnp.float32)
    cand_data = jnp.concatenate(
        [
            jnp.concatenate([displacement] * len(NEIGHBOURS), axis=1),
            jnp.broadcast_to(cand_label[None, :, None], (1, count, block_nodes)),
        ]
    )
    send_channels = cand_data.shape[0]
    send_outgoing = jnp.einsum("cjn,jp->cpn", cand_data, packing, precision=highest).reshape(
        send_channels, -1
    )
    send_incoming = lax.all_to_all(
        send_outgoing, ("gy", "gz"), split_axis=1, concat_axis=1, tiled=True
    ).reshape(send_channels, members * HALO_CAP, block_nodes)
    received_labels = send_incoming[3, :, 0]
    placing = (
        received_labels[:, None] == jnp.arange(1, count + 1, dtype=jnp.float32)[None, :]
    ).astype(jnp.float32)
    around = jnp.einsum("cpn,pk->ckn", send_incoming[:3], placing, precision=highest).reshape(
        3, len(NEIGHBOURS), ex, ey, ez
    )

    def near(ry, rz):
        return around[:, NEIGHBOURS.index((ry, rz))]

    centre = near(0, 0)
    middle = jnp.concatenate(
        [near(0, -1)[..., ez - 2 :], centre, near(0, 1)[..., :2]], axis=3
    )
    low_row = jnp.concatenate(
        [
            near(-1, -1)[:, :, ey - 1 :, ez - 2 :],
            near(-1, 0)[:, :, ey - 1 :, :],
            near(-1, 1)[:, :, ey - 1 :, :2],
        ],
        axis=3,
    )
    high_row = jnp.concatenate(
        [near(1, -1)[:, :, :1, ez - 2 :], near(1, 0)[:, :, :1, :], near(1, 1)[:, :, :1, :2]],
        axis=3,
    )
    extended = jnp.concatenate([low_row, middle, high_row], axis=2)
    first_padded = with_halo(extended, (("gx", 1),), 1)
    derived = derive_fields(padded_images[0], padded_images[1])
    region = padded_images[2][3:-3, 3:-3, 3:-3]
    contrast = derived[0].astype(jnp.float32)
    slopes = derived[1:].astype(jnp.float32)
    masked_slopes = slopes * region[None]
    wide_curvature = collect(masked_slopes * slopes, wide_square, True) + diagonal_shift
    moved = spread(first_padded, wide_table)
    residual = contrast + slopes[0] * moved[0] + slopes[1] * moved[1] + slopes[2] * moved[2]
    image_part = collect(masked_slopes * residual[None], wide_back, False)
    force_total = image_part + elastic_weight * elastic_force(first_padded)
    wide_values = first_padded[:, 1:-1, 1:-1, 1:-1] - force_total / wide_curvature
    column = jnp.arange(ez + 2, dtype=jnp.int32)
    ghost = ((column == 0) & (lax.axis_index("gz") == 0)) | (
        (column == ez + 1) & (lax.axis_index("gz") == size_z - 1)
    )
    wide_values = jnp.where(ghost, 0.0, wide_values)
    padded = with_halo(wide_values, (("gy", 2), ("gx", 1)), 1)
    padded = jnp.pad(padded, ((0, 0), (0, 0), (0, 0), (1, 1)))
    moved = spread(padded, wide_table)
    residual = contrast + slopes[0] * moved[0] + slopes[1] * moved[1] + slopes[2] * moved[2]
    image_part = collect(masked_slopes * residual[None], wide_back, False)
    force_total = image_part + elastic_weight * elastic_force(padded)
    tile_values = (wide_values - force_total / wide_curvature)[..., 1:-1]
    final_blocks = tile_values.reshape(3, blocks, block_nodes)
    own_labels = received_labels.reshape(members, HALO_CAP)[:, :CAP].reshape(-1)
    position = jnp.arange(blocks, dtype=jnp.int32)
    back_placing = (own_labels[:, None] == (position + 1).astype(jnp.float32)[None, :]).astype(
        jnp.float32
    )
    outgoing = jnp.einsum("ckn,pk->cpn", final_blocks, back_placing, precision=highest).reshape(
        3, -1
    )
    incoming = lax.all_to_all(outgoing, ("gy", "gz"), split_axis=1, concat_axis=1, tiled=True)
    own_slot = owner_tile * CAP + ranking[:blocks]
    back_packing = (
        own_slot[:, None] == jnp.arange(members * CAP, dtype=jnp.int32)[None, :]
    ).astype(jnp.float32)
    return jnp.einsum(
        "cpn,jp->cjn", incoming.reshape(3, members * CAP, -1), back_packing, precision=highest
    )


def solution(mesh):
    in_specs = (
        P("gx", "gy", "gz"),
        P("gx", "gy", "gz"),
        P("gx", "gy", "gz"),
        P(None, ("gx", "gy", "gz"), None),
        P(("gx", "gy", "gz")),
    )
    out_specs = P(None, ("gx", "gy", "gz"), None)
    return jax.shard_map(
        per_device, mesh=mesh, in_specs=in_specs, out_specs=out_specs, check_vma=False
    )
```

```python
import jax
import jax.numpy as jnp
from jax import lax
from jax.sharding import PartitionSpec as P

ELEM = 4
ITERS = 2
CAP = 2


binomial = (0.0625, 0.25, 0.375, 0.25, 0.0625)
lame_lambda = 1.0
shear_modulus = 0.5
elastic_weight = 2.0
diagonal_shift = 6.0
highest = lax.Precision.HIGHEST


def with_halo(block, sides, width):
    for axis, dim in sides:
        count = lax.axis_size(axis)
        forward = [(i, i + 1) for i in range(count - 1)]
        backward = [(target, source) for source, target in forward]
        low = lax.ppermute(
            lax.slice_in_dim(block, block.shape[dim] - width, None, axis=dim), axis, forward
        )
        high = lax.ppermute(lax.slice_in_dim(block, 0, width, axis=dim), axis, backward)
        block = jnp.concatenate([low, block, high], axis=dim)
    return block


def with_halo_pair(first, second, sides, widths):
    for axis, first_dim, second_dim in sides:
        count = lax.axis_size(axis)
        forward = [(i, i + 1) for i in range(count - 1)]
        backward = [(target, source) for source, target in forward]
        parts = []
        for block, dim, width in ((first, first_dim, widths[0]), (second, second_dim, widths[1])):
            parts.append(
                (
                    lax.slice_in_dim(block, block.shape[dim] - width, None, axis=dim),
                    lax.slice_in_dim(block, 0, width, axis=dim),
                )
            )
        low_flat = jnp.concatenate([p[0].reshape(-1) for p in parts])
        high_flat = jnp.concatenate([p[1].reshape(-1) for p in parts])
        low_flat = lax.ppermute(low_flat, axis, forward)
        high_flat = lax.ppermute(high_flat, axis, backward)
        split = parts[0][0].size
        pieces = []
        for index, (block, dim) in enumerate(((first, first_dim), (second, second_dim))):
            shape = parts[index][0].shape
            begin, end = (0, split) if index == 0 else (split, low_flat.shape[0])
            low = low_flat[begin:end].reshape(shape)
            high = high_flat[begin:end].reshape(shape)
            pieces.append(jnp.concatenate([low, block, high], axis=dim))
        first, second = pieces
    return first, second


def smooth_axis(volume, dimension):
    length = volume.shape[dimension] - 4
    summed = binomial[0] * lax.slice_in_dim(volume, 0, length, axis=dimension)
    for offset in range(1, 5):
        summed = summed + binomial[offset] * lax.slice_in_dim(
            volume, offset, offset + length, axis=dimension
        )
    return summed


def derive_fields(first_padded, second_padded):
    first_smooth = first_padded
    second_smooth = second_padded
    for dimension in range(3):
        first_smooth = smooth_axis(first_smooth, dimension)
        second_smooth = smooth_axis(second_smooth, dimension)
    average = (first_smooth + second_smooth) * 0.5
    contrast = (second_smooth - first_smooth)[1:-1, 1:-1, 1:-1].astype(jnp.bfloat16)
    slopes = []
    for dimension in range(3):
        length = average.shape[dimension] - 2
        forward_part = lax.slice_in_dim(average, 2, length + 2, axis=dimension)
        backward_part = lax.slice_in_dim(average, 0, length, axis=dimension)
        gradient = (forward_part - backward_part) * 0.5
        for cropped_dim in range(3):
            if cropped_dim != dimension:
                gradient = lax.slice_in_dim(
                    gradient, 1, gradient.shape[cropped_dim] - 1, axis=cropped_dim
                )
        slopes.append(gradient.astype(jnp.bfloat16))
    return jnp.stack([contrast] + slopes)


def interp_axis(volume, dimension, cells_edge):
    length = volume.shape[dimension]
    before = lax.slice_in_dim(volume, 0, length - 1, axis=dimension)
    after = lax.slice_in_dim(volume, 1, length, axis=dimension)
    shape_one = [1] * (volume.ndim + 1)
    shape_one[dimension + 1] = cells_edge
    fraction = (jnp.arange(cells_edge, dtype=jnp.float32) / cells_edge).reshape(shape_one)
    merged = (
        jnp.expand_dims(before, dimension + 1) * (1.0 - fraction)
        + jnp.expand_dims(after, dimension + 1) * fraction
    )
    new_shape = list(volume.shape)
    new_shape[dimension] = (length - 1) * cells_edge
    return merged.reshape(new_shape)


def collect_axis(volume, dimension, cells_edge, squared):
    elements = volume.shape[dimension] // cells_edge
    split_shape = (
        list(volume.shape[:dimension])
        + [elements, cells_edge]
        + list(volume.shape[dimension + 1 :])
    )
    pieces = volume.reshape(split_shape)
    shape_one = [1] * len(split_shape)
    shape_one[dimension + 1] = cells_edge
    fraction = (jnp.arange(cells_edge, dtype=jnp.float32) / cells_edge).reshape(shape_one)
    weight_low = 1.0 - fraction
    weight_high = fraction
    if squared:
        weight_low = weight_low * weight_low
        weight_high = weight_high * weight_high
    low_side = jnp.sum(pieces * weight_low, axis=dimension + 1)
    high_side = jnp.sum(pieces * weight_high, axis=dimension + 1)
    return lax.slice_in_dim(low_side, 1, elements, axis=dimension) + lax.slice_in_dim(
        high_side, 0, elements - 1, axis=dimension
    )


def pair_op(volume, dimension, factor):
    length = volume.shape[dimension]
    return lax.slice_in_dim(volume, 1, length, axis=dimension) + factor * lax.slice_in_dim(
        volume, 0, length - 1, axis=dimension
    )


def cross_pairs(volume, chosen, factor, offset):
    for dimension in range(3):
        volume = pair_op(volume, dimension + offset, factor if dimension == chosen else 1.0)
    return volume


def elastic_force(padded):
    gradients = [cross_pairs(padded, chosen, -1.0, 1) * (1.0 / (4.0 * ELEM)) for chosen in range(3)]
    deform = [
        [gradients[source][target] + (1.0 if target == source else 0.0) for source in range(3)]
        for target in range(3)
    ]
    strain = [
        [
            0.5
            * (
                deform[0][target] * deform[0][source]
                + deform[1][target] * deform[1][source]
                + deform[2][target] * deform[2][source]
            )
            - (0.5 if target == source else 0.0)
            for source in range(3)
        ]
        for target in range(3)
    ]
    trace_strain = strain[0][0] + strain[1][1] + strain[2][2]
    stress = [
        [
            2.0 * shear_modulus * strain[target][source]
            + (lame_lambda * trace_strain if target == source else 0.0)
            for source in range(3)
        ]
        for target in range(3)
    ]
    nominal = [
        [
            deform[target][0] * stress[0][source]
            + deform[target][1] * stress[1][source]
            + deform[target][2] * stress[2][source]
            for source in range(3)
        ]
        for target in range(3)
    ]
    coefficient = ELEM * ELEM / 4.0
    forces = []
    for target in range(3):
        summed = cross_pairs(nominal[target][0], 0, -1.0, 0)
        for source in range(1, 3):
            summed = summed + cross_pairs(nominal[target][source], source, -1.0, 0)
        forces.append(-coefficient * summed)
    return jnp.stack(forces)


def axis_table(nodes_len, cells_edge, squared):
    voxels = (nodes_len - 1) * cells_edge
    column = jnp.arange(voxels, dtype=jnp.int32)
    element = column // cells_edge
    fraction = (column % cells_edge).astype(jnp.float32) / cells_edge
    weight_low = 1.0 - fraction
    weight_high = fraction
    if squared:
        weight_low = weight_low * weight_low
        weight_high = weight_high * weight_high
    node_row = jnp.arange(nodes_len, dtype=jnp.int32)[:, None]
    return jnp.where(node_row == element[None, :], weight_low[None, :], 0.0) + jnp.where(
        node_row == element[None, :] + 1, weight_high[None, :], 0.0
    )


def spread(padded, weights_table):
    shape_all = padded.shape
    stretched = jnp.dot(padded.reshape(-1, shape_all[3]), weights_table, precision=highest)
    stretched = stretched.reshape(shape_all[0], shape_all[1], shape_all[2], weights_table.shape[1])
    stretched = interp_axis(stretched, 1, ELEM)
    return interp_axis(stretched, 2, ELEM)


def collect(volume, table_back, squared):
    shape_all = volume.shape
    reduced = jnp.dot(volume.reshape(-1, shape_all[3]), table_back, precision=highest)
    reduced = reduced.reshape(shape_all[0], shape_all[1], shape_all[2], table_back.shape[1])
    reduced = collect_axis(reduced, 2, ELEM, squared)
    return collect_axis(reduced, 1, ELEM, squared)


NEIGHBOURS = [(0, 0)] + [(ry, rz) for ry in (-1, 0, 1) for rz in (-1, 0, 1) if (ry, rz) != (0, 0)]
HALO_CAP = 10


def per_device(reference_image, deformed_image, roi_mask, displacement, node_map):
    stacked = jnp.stack([reference_image, deformed_image, roi_mask.astype(jnp.bfloat16)])
    stacked = with_halo(stacked, (("gy", 2),), 5)
    stacked = with_halo(stacked, (("gz", 3),), 5 + ELEM)
    padded_images = with_halo(stacked, (("gx", 1),), 5)
    nodes_shape = (
        3,
        reference_image.shape[0] // ELEM,
        reference_image.shape[1] // ELEM,
        reference_image.shape[2] // ELEM,
    )
    _, ex, ey, ez = nodes_shape
    wide_table = axis_table(ez + 4, ELEM, False)
    wide_back = wide_table[1:-1].T
    wide_square = axis_table(ez + 4, ELEM, True)[1:-1].T
    size_y = lax.axis_size("gy")
    size_z = lax.axis_size("gz")
    members = size_y * size_z
    blocks = node_map.shape[0]
    block_nodes = displacement.shape[2]
    zchunks = ez // block_nodes
    owner_tile = node_map // blocks
    tile_block = node_map % blocks
    tile_y = owner_tile // size_z
    tile_z = owner_tile % size_z
    block_y = (tile_block // zchunks) % ey
    block_zc = tile_block % zchunks
    dests, valids, labels = [], [], []
    for index, (ry, rz) in enumerate(NEIGHBOURS):
        dest_y = tile_y - ry
        dest_z = tile_z - rz
        valid = (dest_y >= 0) & (dest_y < size_y) & (dest_z >= 0) & (dest_z < size_z)
        if ry == -1:
            valid = valid & (block_y == ey - 1)
        elif ry == 1:
            valid = valid & (block_y == 0)
        if rz == -1:
            valid = valid & (block_zc == zchunks - 1)
        elif rz == 1:
            valid = valid & (block_zc == 0)
        dests.append(dest_y * size_z + dest_z)
        valids.append(valid)
        labels.append(index * blocks + tile_block + 1)
    cand_dest = jnp.concatenate(dests)
    cand_valid = jnp.concatenate(valids)
    cand_label = jnp.concatenate(labels).astype(jnp.float32)
    count = cand_dest.shape[0]
    order = jnp.arange(count, dtype=jnp.int32)
    earlier = (
        (cand_dest[:, None] == cand_dest[None, :])
        & cand_valid[None, :]
        & (order[None, :] < order[:, None])
    )
    ranking = jnp.sum(earlier.astype(jnp.int32), axis=1)
    target_slot = jnp.where(cand_valid, cand_dest * HALO_CAP + ranking, -1)
    packing = (
        target_slot[:, None] == jnp.arange(members * HALO_CAP, dtype=jnp.int32)[None, :]
    ).astype(jnp.float32)
    cand_data = jnp.concatenate(
        [
            jnp.concatenate([displacement] * len(NEIGHBOURS), axis=1),
            jnp.broadcast_to(cand_label[None, :, None], (1, count, block_nodes)),
        ]
    )
    send_channels = cand_data.shape[0]
    send_outgoing = jnp.einsum("cjn,jp->cpn", cand_data, packing, precision=highest).reshape(
        send_channels, -1
    )
    send_incoming = lax.all_to_all(
        send_outgoing, ("gy", "gz"), split_axis=1, concat_axis=1, tiled=True
    ).reshape(send_channels, members * HALO_CAP, block_nodes)
    received_labels = send_incoming[3, :, 0]
    placing = (
        received_labels[:, None] == jnp.arange(1, count + 1, dtype=jnp.float32)[None, :]
    ).astype(jnp.float32)
    around = jnp.einsum("cpn,pk->ckn", send_incoming[:3], placing, precision=highest).reshape(
        3, len(NEIGHBOURS), ex, ey, ez
    )

    def near(ry, rz):
        return around[:, NEIGHBOURS.index((ry, rz))]

    centre = near(0, 0)
    middle = jnp.concatenate(
        [near(0, -1)[..., ez - 2 :], centre, near(0, 1)[..., :2]], axis=3
    )
    low_row = jnp.concatenate(
        [
            near(-1, -1)[:, :, ey - 1 :, ez - 2 :],
            near(-1, 0)[:, :, ey - 1 :, :],
            near(-1, 1)[:, :, ey - 1 :, :2],
        ],
        axis=3,
    )
    high_row = jnp.concatenate(
        [near(1, -1)[:, :, :1, ez - 2 :], near(1, 0)[:, :, :1, :], near(1, 1)[:, :, :1, :2]],
        axis=3,
    )
    extended = jnp.concatenate([low_row, middle, high_row], axis=2)
    first_padded = with_halo(extended, (("gx", 1),), 1)
    derived = derive_fields(
        padded_images[0].astype(jnp.float32), padded_images[1].astype(jnp.float32)
    )
    region = padded_images[2][3:-3, 3:-3, 3:-3].astype(jnp.float32)
    contrast = derived[0].astype(jnp.float32)
    slopes = derived[1:].astype(jnp.float32)
    masked_slopes = slopes * region[None]
    wide_curvature = collect(masked_slopes * slopes, wide_square, True) + diagonal_shift
    moved = spread(first_padded, wide_table)
    residual = contrast + slopes[0] * moved[0] + slopes[1] * moved[1] + slopes[2] * moved[2]
    image_part = collect(masked_slopes * residual[None], wide_back, False)
    force_total = image_part + elastic_weight * elastic_force(first_padded)
    wide_values = first_padded[:, 1:-1, 1:-1, 1:-1] - force_total / wide_curvature
    column = jnp.arange(ez + 2, dtype=jnp.int32)
    ghost = ((column == 0) & (lax.axis_index("gz") == 0)) | (
        (column == ez + 1) & (lax.axis_index("gz") == size_z - 1)
    )
    wide_values = jnp.where(ghost, 0.0, wide_values)
    padded = with_halo(wide_values, (("gx", 1), ("gy", 2)), 1)
    padded = jnp.pad(padded, ((0, 0), (0, 0), (0, 0), (1, 1)))
    moved = spread(padded, wide_table)
    residual = contrast + slopes[0] * moved[0] + slopes[1] * moved[1] + slopes[2] * moved[2]
    image_part = collect(masked_slopes * residual[None], wide_back, False)
    force_total = image_part + elastic_weight * elastic_force(padded)
    tile_values = (wide_values - force_total / wide_curvature)[..., 1:-1]
    final_blocks = tile_values.reshape(3, blocks, block_nodes)
    own_labels = received_labels.reshape(members, HALO_CAP)[:, :CAP].reshape(-1)
    position = jnp.arange(blocks, dtype=jnp.int32)
    back_placing = (own_labels[:, None] == (position + 1).astype(jnp.float32)[None, :]).astype(
        jnp.float32
    )
    outgoing = jnp.einsum("ckn,pk->cpn", final_blocks, back_placing, precision=highest).reshape(
        3, -1
    )
    incoming = lax.all_to_all(outgoing, ("gy", "gz"), split_axis=1, concat_axis=1, tiled=True)
    own_slot = owner_tile * CAP + ranking[:blocks]
    back_packing = (
        own_slot[:, None] == jnp.arange(members * CAP, dtype=jnp.int32)[None, :]
    ).astype(jnp.float32)
    return jnp.einsum(
        "cpn,jp->cjn", incoming.reshape(3, members * CAP, -1), back_packing, precision=highest
    )


def solution(mesh):
    in_specs = (
        P("gx", "gy", "gz"),
        P("gx", "gy", "gz"),
        P("gx", "gy", "gz"),
        P(None, ("gx", "gy", "gz"), None),
        P(("gx", "gy", "gz")),
    )
    out_specs = P(None, ("gx", "gy", "gz"), None)
    return jax.shard_map(
        per_device, mesh=mesh, in_specs=in_specs, out_specs=out_specs, check_vma=False
    )
```

```python
import jax
import jax.numpy as jnp
from jax import lax
from jax.sharding import PartitionSpec as P

ELEM = 4
ITERS = 2
CAP = 2


binomial = (0.0625, 0.25, 0.375, 0.25, 0.0625)
lame_lambda = 1.0
shear_modulus = 0.5
elastic_weight = 2.0
diagonal_shift = 6.0
highest = lax.Precision.HIGHEST


def with_halo(block, sides, width):
    for axis, dim in sides:
        count = lax.axis_size(axis)
        forward = [(i, i + 1) for i in range(count - 1)]
        backward = [(target, source) for source, target in forward]
        low = lax.ppermute(
            lax.slice_in_dim(block, block.shape[dim] - width, None, axis=dim), axis, forward
        )
        high = lax.ppermute(lax.slice_in_dim(block, 0, width, axis=dim), axis, backward)
        block = jnp.concatenate([low, block, high], axis=dim)
    return block


def with_halo_pair(first, second, sides, widths):
    for axis, first_dim, second_dim in sides:
        count = lax.axis_size(axis)
        forward = [(i, i + 1) for i in range(count - 1)]
        backward = [(target, source) for source, target in forward]
        parts = []
        for block, dim, width in ((first, first_dim, widths[0]), (second, second_dim, widths[1])):
            parts.append(
                (
                    lax.slice_in_dim(block, block.shape[dim] - width, None, axis=dim),
                    lax.slice_in_dim(block, 0, width, axis=dim),
                )
            )
        low_flat = jnp.concatenate([p[0].reshape(-1) for p in parts])
        high_flat = jnp.concatenate([p[1].reshape(-1) for p in parts])
        low_flat = lax.ppermute(low_flat, axis, forward)
        high_flat = lax.ppermute(high_flat, axis, backward)
        split = parts[0][0].size
        pieces = []
        for index, (block, dim) in enumerate(((first, first_dim), (second, second_dim))):
            shape = parts[index][0].shape
            begin, end = (0, split) if index == 0 else (split, low_flat.shape[0])
            low = low_flat[begin:end].reshape(shape)
            high = high_flat[begin:end].reshape(shape)
            pieces.append(jnp.concatenate([low, block, high], axis=dim))
        first, second = pieces
    return first, second


def smooth_axis(volume, dimension):
    length = volume.shape[dimension] - 4
    summed = binomial[0] * lax.slice_in_dim(volume, 0, length, axis=dimension)
    for offset in range(1, 5):
        summed = summed + binomial[offset] * lax.slice_in_dim(
            volume, offset, offset + length, axis=dimension
        )
    return summed


def derive_fields(first_padded, second_padded):
    first_smooth = first_padded
    second_smooth = second_padded
    for dimension in range(3):
        first_smooth = smooth_axis(first_smooth, dimension)
        second_smooth = smooth_axis(second_smooth, dimension)
    average = (first_smooth + second_smooth) * 0.5
    contrast = (second_smooth - first_smooth)[1:-1, 1:-1, 1:-1].astype(jnp.bfloat16)
    slopes = []
    for dimension in range(3):
        length = average.shape[dimension] - 2
        forward_part = lax.slice_in_dim(average, 2, length + 2, axis=dimension)
        backward_part = lax.slice_in_dim(average, 0, length, axis=dimension)
        gradient = (forward_part - backward_part) * 0.5
        for cropped_dim in range(3):
            if cropped_dim != dimension:
                gradient = lax.slice_in_dim(
                    gradient, 1, gradient.shape[cropped_dim] - 1, axis=cropped_dim
                )
        slopes.append(gradient.astype(jnp.bfloat16))
    return jnp.stack([contrast] + slopes)


def interp_axis(volume, dimension, cells_edge):
    length = volume.shape[dimension]
    before = lax.slice_in_dim(volume, 0, length - 1, axis=dimension)
    after = lax.slice_in_dim(volume, 1, length, axis=dimension)
    shape_one = [1] * (volume.ndim + 1)
    shape_one[dimension + 1] = cells_edge
    fraction = (jnp.arange(cells_edge, dtype=jnp.float32) / cells_edge).reshape(shape_one)
    merged = (
        jnp.expand_dims(before, dimension + 1) * (1.0 - fraction)
        + jnp.expand_dims(after, dimension + 1) * fraction
    )
    new_shape = list(volume.shape)
    new_shape[dimension] = (length - 1) * cells_edge
    return merged.reshape(new_shape)


def collect_axis(volume, dimension, cells_edge, squared):
    elements = volume.shape[dimension] // cells_edge
    split_shape = (
        list(volume.shape[:dimension])
        + [elements, cells_edge]
        + list(volume.shape[dimension + 1 :])
    )
    pieces = volume.reshape(split_shape)
    shape_one = [1] * len(split_shape)
    shape_one[dimension + 1] = cells_edge
    fraction = (jnp.arange(cells_edge, dtype=jnp.float32) / cells_edge).reshape(shape_one)
    weight_low = 1.0 - fraction
    weight_high = fraction
    if squared:
        weight_low = weight_low * weight_low
        weight_high = weight_high * weight_high
    low_side = jnp.sum(pieces * weight_low, axis=dimension + 1)
    high_side = jnp.sum(pieces * weight_high, axis=dimension + 1)
    return lax.slice_in_dim(low_side, 1, elements, axis=dimension) + lax.slice_in_dim(
        high_side, 0, elements - 1, axis=dimension
    )


def pair_op(volume, dimension, factor):
    length = volume.shape[dimension]
    return lax.slice_in_dim(volume, 1, length, axis=dimension) + factor * lax.slice_in_dim(
        volume, 0, length - 1, axis=dimension
    )


def cross_pairs(volume, chosen, factor, offset):
    for dimension in range(3):
        volume = pair_op(volume, dimension + offset, factor if dimension == chosen else 1.0)
    return volume


def elastic_force(padded):
    gradients = [cross_pairs(padded, chosen, -1.0, 1) * (1.0 / (4.0 * ELEM)) for chosen in range(3)]
    deform = [
        [gradients[source][target] + (1.0 if target == source else 0.0) for source in range(3)]
        for target in range(3)
    ]
    strain = [
        [
            0.5
            * (
                deform[0][target] * deform[0][source]
                + deform[1][target] * deform[1][source]
                + deform[2][target] * deform[2][source]
            )
            - (0.5 if target == source else 0.0)
            for source in range(3)
        ]
        for target in range(3)
    ]
    trace_strain = strain[0][0] + strain[1][1] + strain[2][2]
    stress = [
        [
            2.0 * shear_modulus * strain[target][source]
            + (lame_lambda * trace_strain if target == source else 0.0)
            for source in range(3)
        ]
        for target in range(3)
    ]
    nominal = [
        [
            deform[target][0] * stress[0][source]
            + deform[target][1] * stress[1][source]
            + deform[target][2] * stress[2][source]
            for source in range(3)
        ]
        for target in range(3)
    ]
    coefficient = ELEM * ELEM / 4.0
    forces = []
    for target in range(3):
        summed = cross_pairs(nominal[target][0], 0, -1.0, 0)
        for source in range(1, 3):
            summed = summed + cross_pairs(nominal[target][source], source, -1.0, 0)
        forces.append(-coefficient * summed)
    return jnp.stack(forces)


def axis_table(nodes_len, cells_edge, squared):
    voxels = (nodes_len - 1) * cells_edge
    column = jnp.arange(voxels, dtype=jnp.int32)
    element = column // cells_edge
    fraction = (column % cells_edge).astype(jnp.float32) / cells_edge
    weight_low = 1.0 - fraction
    weight_high = fraction
    if squared:
        weight_low = weight_low * weight_low
        weight_high = weight_high * weight_high
    node_row = jnp.arange(nodes_len, dtype=jnp.int32)[:, None]
    return jnp.where(node_row == element[None, :], weight_low[None, :], 0.0) + jnp.where(
        node_row == element[None, :] + 1, weight_high[None, :], 0.0
    )


def spread(padded, weights_table):
    shape_all = padded.shape
    stretched = jnp.dot(padded.reshape(-1, shape_all[3]), weights_table, precision=highest)
    stretched = stretched.reshape(shape_all[0], shape_all[1], shape_all[2], weights_table.shape[1])
    stretched = interp_axis(stretched, 1, ELEM)
    return interp_axis(stretched, 2, ELEM)


def collect(volume, table_back, squared):
    shape_all = volume.shape
    reduced = jnp.dot(volume.reshape(-1, shape_all[3]), table_back, precision=highest)
    reduced = reduced.reshape(shape_all[0], shape_all[1], shape_all[2], table_back.shape[1])
    reduced = collect_axis(reduced, 2, ELEM, squared)
    return collect_axis(reduced, 1, ELEM, squared)


NEIGHBOURS = [(0, 0)] + [(ry, rz) for ry in (-1, 0, 1) for rz in (-1, 0, 1) if (ry, rz) != (0, 0)]
HALO_CAP = 10


def per_device(reference_image, deformed_image, roi_mask, displacement, node_map):
    stacked = jnp.stack([reference_image, deformed_image, roi_mask.astype(jnp.bfloat16)])
    stacked = with_halo(stacked, (("gy", 2),), 5)
    stacked = with_halo(stacked, (("gz", 3),), 5 + ELEM)
    padded_images = with_halo(stacked, (("gx", 1),), 5)
    nodes_shape = (
        3,
        reference_image.shape[0] // ELEM,
        reference_image.shape[1] // ELEM,
        reference_image.shape[2] // ELEM,
    )
    _, ex, ey, ez = nodes_shape
    wide_table = axis_table(ez + 4, ELEM, False)
    wide_back = wide_table[1:-1].T
    wide_square = axis_table(ez + 4, ELEM, True)[1:-1].T
    size_y = lax.axis_size("gy")
    size_z = lax.axis_size("gz")
    members = size_y * size_z
    blocks = node_map.shape[0]
    block_nodes = displacement.shape[2]
    zchunks = ez // block_nodes
    owner_tile = node_map // blocks
    tile_block = node_map % blocks
    tile_y = owner_tile // size_z
    tile_z = owner_tile % size_z
    block_y = (tile_block // zchunks) % ey
    block_zc = tile_block % zchunks
    dests, valids, labels = [], [], []
    for index, (ry, rz) in enumerate(NEIGHBOURS):
        dest_y = tile_y - ry
        dest_z = tile_z - rz
        valid = (dest_y >= 0) & (dest_y < size_y) & (dest_z >= 0) & (dest_z < size_z)
        if ry == -1:
            valid = valid & (block_y == ey - 1)
        elif ry == 1:
            valid = valid & (block_y == 0)
        if rz == -1:
            valid = valid & (block_zc == zchunks - 1)
        elif rz == 1:
            valid = valid & (block_zc == 0)
        dests.append(dest_y * size_z + dest_z)
        valids.append(valid)
        labels.append(index * blocks + tile_block + 1)
    cand_dest = jnp.concatenate(dests)
    cand_valid = jnp.concatenate(valids)
    cand_label = jnp.concatenate(labels).astype(jnp.float32)
    count = cand_dest.shape[0]
    order = jnp.arange(count, dtype=jnp.int32)
    earlier = (
        (cand_dest[:, None] == cand_dest[None, :])
        & cand_valid[None, :]
        & (order[None, :] < order[:, None])
    )
    ranking = jnp.sum(earlier.astype(jnp.int32), axis=1)
    target_slot = jnp.where(cand_valid, cand_dest * HALO_CAP + ranking, -1)
    packing = (
        target_slot[:, None] == jnp.arange(members * HALO_CAP, dtype=jnp.int32)[None, :]
    ).astype(jnp.float32)
    cand_data = jnp.concatenate(
        [
            jnp.concatenate([displacement] * len(NEIGHBOURS), axis=1),
            jnp.broadcast_to(cand_label[None, :, None], (1, count, block_nodes)),
        ]
    )
    send_channels = cand_data.shape[0]
    send_outgoing = jnp.einsum("cjn,jp->cpn", cand_data, packing, precision=highest).reshape(
        send_channels, -1
    )
    send_incoming = lax.all_to_all(
        send_outgoing, ("gy", "gz"), split_axis=1, concat_axis=1, tiled=True
    ).reshape(send_channels, members * HALO_CAP, block_nodes)
    received_labels = send_incoming[3, :, 0]
    placing = (
        received_labels[:, None] == jnp.arange(1, count + 1, dtype=jnp.float32)[None, :]
    ).astype(jnp.float32)
    around = jnp.einsum("cpn,pk->ckn", send_incoming[:3], placing, precision=highest).reshape(
        3, len(NEIGHBOURS), ex, ey, ez
    )

    def near(ry, rz):
        return around[:, NEIGHBOURS.index((ry, rz))]

    centre = near(0, 0)
    middle = jnp.concatenate(
        [near(0, -1)[..., ez - 2 :], centre, near(0, 1)[..., :2]], axis=3
    )
    low_row = jnp.concatenate(
        [
            near(-1, -1)[:, :, ey - 1 :, ez - 2 :],
            near(-1, 0)[:, :, ey - 1 :, :],
            near(-1, 1)[:, :, ey - 1 :, :2],
        ],
        axis=3,
    )
    high_row = jnp.concatenate(
        [near(1, -1)[:, :, :1, ez - 2 :], near(1, 0)[:, :, :1, :], near(1, 1)[:, :, :1, :2]],
        axis=3,
    )
    extended = jnp.concatenate([low_row, middle, high_row], axis=2)
    first_padded = with_halo(extended, (("gx", 1),), 1)
    derived = derive_fields(
        padded_images[0].astype(jnp.float32), padded_images[1].astype(jnp.float32)
    )
    region = padded_images[2][3:-3, 3:-3, 3:-3].astype(jnp.float32)
    contrast = derived[0].astype(jnp.float32)
    slopes = derived[1:].astype(jnp.float32)
    masked_slopes = slopes * region[None]
    wide_curvature = collect(masked_slopes * slopes, wide_square, True) + diagonal_shift
    moved = spread(first_padded, wide_table)
    residual = contrast + slopes[0] * moved[0] + slopes[1] * moved[1] + slopes[2] * moved[2]
    image_part = collect(masked_slopes * residual[None], wide_back, False)
    force_total = image_part + elastic_weight * elastic_force(first_padded)
    wide_values = first_padded[:, 1:-1, 1:-1, 1:-1] - force_total / wide_curvature
    column = jnp.arange(ez + 2, dtype=jnp.int32)
    ghost = ((column == 0) & (lax.axis_index("gz") == 0)) | (
        (column == ez + 1) & (lax.axis_index("gz") == size_z - 1)
    )
    wide_values = jnp.where(ghost, 0.0, wide_values)
    padded = with_halo(wide_values, (("gy", 2), ("gx", 1)), 1)
    padded = jnp.pad(padded, ((0, 0), (0, 0), (0, 0), (1, 1)))
    moved = spread(padded, wide_table)
    residual = contrast + slopes[0] * moved[0] + slopes[1] * moved[1] + slopes[2] * moved[2]
    image_part = collect(masked_slopes * residual[None], wide_back, False)
    force_total = image_part + elastic_weight * elastic_force(padded)
    tile_values = (wide_values - force_total / wide_curvature)[..., 1:-1]
    final_blocks = tile_values.reshape(3, blocks, block_nodes)
    own_labels = received_labels.reshape(members, HALO_CAP)[:, :CAP].reshape(-1)
    position = jnp.arange(blocks, dtype=jnp.int32)
    back_placing = (own_labels[:, None] == (position + 1).astype(jnp.float32)[None, :]).astype(
        jnp.float32
    )
    outgoing = jnp.einsum("ckn,pk->cpn", final_blocks, back_placing, precision=highest).reshape(
        3, -1
    )
    incoming = lax.all_to_all(outgoing, ("gy", "gz"), split_axis=1, concat_axis=1, tiled=True)
    own_slot = owner_tile * CAP + ranking[:blocks]
    back_packing = (
        own_slot[:, None] == jnp.arange(members * CAP, dtype=jnp.int32)[None, :]
    ).astype(jnp.float32)
    return jnp.einsum(
        "cpn,jp->cjn", incoming.reshape(3, members * CAP, -1), back_packing, precision=highest
    )


def solution(mesh):
    in_specs = (
        P("gx", "gy", "gz"),
        P("gx", "gy", "gz"),
        P("gx", "gy", "gz"),
        P(None, ("gx", "gy", "gz"), None),
        P(("gx", "gy", "gz")),
    )
    out_specs = P(None, ("gx", "gy", "gz"), None)
    return jax.shard_map(
        per_device, mesh=mesh, in_specs=in_specs, out_specs=out_specs, check_vma=False
    )
```

```python
import jax
import jax.numpy as jnp
from jax import lax
from jax.sharding import PartitionSpec as P

ELEM = 4
ITERS = 2
CAP = 2


binomial = (0.0625, 0.25, 0.375, 0.25, 0.0625)
lame_lambda = 1.0
shear_modulus = 0.5
elastic_weight = 2.0
diagonal_shift = 6.0
highest = lax.Precision.HIGHEST


def with_halo(block, sides, width):
    for axis, dim in sides:
        count = lax.axis_size(axis)
        forward = [(i, i + 1) for i in range(count - 1)]
        backward = [(target, source) for source, target in forward]
        low = lax.ppermute(
            lax.slice_in_dim(block, block.shape[dim] - width, None, axis=dim), axis, forward
        )
        high = lax.ppermute(lax.slice_in_dim(block, 0, width, axis=dim), axis, backward)
        block = jnp.concatenate([low, block, high], axis=dim)
    return block


def with_halo_pair(first, second, sides, widths):
    for axis, first_dim, second_dim in sides:
        count = lax.axis_size(axis)
        forward = [(i, i + 1) for i in range(count - 1)]
        backward = [(target, source) for source, target in forward]
        parts = []
        for block, dim, width in ((first, first_dim, widths[0]), (second, second_dim, widths[1])):
            parts.append(
                (
                    lax.slice_in_dim(block, block.shape[dim] - width, None, axis=dim),
                    lax.slice_in_dim(block, 0, width, axis=dim),
                )
            )
        low_flat = jnp.concatenate([p[0].reshape(-1) for p in parts])
        high_flat = jnp.concatenate([p[1].reshape(-1) for p in parts])
        low_flat = lax.ppermute(low_flat, axis, forward)
        high_flat = lax.ppermute(high_flat, axis, backward)
        split = parts[0][0].size
        pieces = []
        for index, (block, dim) in enumerate(((first, first_dim), (second, second_dim))):
            shape = parts[index][0].shape
            begin, end = (0, split) if index == 0 else (split, low_flat.shape[0])
            low = low_flat[begin:end].reshape(shape)
            high = high_flat[begin:end].reshape(shape)
            pieces.append(jnp.concatenate([low, block, high], axis=dim))
        first, second = pieces
    return first, second


def smooth_axis(volume, dimension):
    length = volume.shape[dimension] - 4
    summed = binomial[0] * lax.slice_in_dim(volume, 0, length, axis=dimension)
    for offset in range(1, 5):
        summed = summed + binomial[offset] * lax.slice_in_dim(
            volume, offset, offset + length, axis=dimension
        )
    return summed


def derive_fields(first_padded, second_padded):
    first_smooth = first_padded
    second_smooth = second_padded
    for dimension in range(3):
        first_smooth = smooth_axis(first_smooth, dimension)
        second_smooth = smooth_axis(second_smooth, dimension)
    average = (first_smooth + second_smooth) * 0.5
    contrast = (second_smooth - first_smooth)[1:-1, 1:-1, 1:-1].astype(jnp.bfloat16)
    slopes = []
    for dimension in range(3):
        length = average.shape[dimension] - 2
        forward_part = lax.slice_in_dim(average, 2, length + 2, axis=dimension)
        backward_part = lax.slice_in_dim(average, 0, length, axis=dimension)
        gradient = (forward_part - backward_part) * 0.5
        for cropped_dim in range(3):
            if cropped_dim != dimension:
                gradient = lax.slice_in_dim(
                    gradient, 1, gradient.shape[cropped_dim] - 1, axis=cropped_dim
                )
        slopes.append(gradient.astype(jnp.bfloat16))
    return jnp.stack([contrast] + slopes)


def interp_axis(volume, dimension, cells_edge):
    length = volume.shape[dimension]
    before = lax.slice_in_dim(volume, 0, length - 1, axis=dimension)
    after = lax.slice_in_dim(volume, 1, length, axis=dimension)
    shape_one = [1] * (volume.ndim + 1)
    shape_one[dimension + 1] = cells_edge
    fraction = (jnp.arange(cells_edge, dtype=jnp.float32) / cells_edge).reshape(shape_one)
    merged = (
        jnp.expand_dims(before, dimension + 1) * (1.0 - fraction)
        + jnp.expand_dims(after, dimension + 1) * fraction
    )
    new_shape = list(volume.shape)
    new_shape[dimension] = (length - 1) * cells_edge
    return merged.reshape(new_shape)


def collect_axis(volume, dimension, cells_edge, squared):
    elements = volume.shape[dimension] // cells_edge
    split_shape = (
        list(volume.shape[:dimension])
        + [elements, cells_edge]
        + list(volume.shape[dimension + 1 :])
    )
    pieces = volume.reshape(split_shape)
    shape_one = [1] * len(split_shape)
    shape_one[dimension + 1] = cells_edge
    fraction = (jnp.arange(cells_edge, dtype=jnp.float32) / cells_edge).reshape(shape_one)
    weight_low = 1.0 - fraction
    weight_high = fraction
    if squared:
        weight_low = weight_low * weight_low
        weight_high = weight_high * weight_high
    low_side = jnp.sum(pieces * weight_low, axis=dimension + 1)
    high_side = jnp.sum(pieces * weight_high, axis=dimension + 1)
    return lax.slice_in_dim(low_side, 1, elements, axis=dimension) + lax.slice_in_dim(
        high_side, 0, elements - 1, axis=dimension
    )


def pair_op(volume, dimension, factor):
    length = volume.shape[dimension]
    return lax.slice_in_dim(volume, 1, length, axis=dimension) + factor * lax.slice_in_dim(
        volume, 0, length - 1, axis=dimension
    )


def cross_pairs(volume, chosen, factor, offset):
    for dimension in range(3):
        volume = pair_op(volume, dimension + offset, factor if dimension == chosen else 1.0)
    return volume


def elastic_force(padded):
    gradients = [cross_pairs(padded, chosen, -1.0, 1) * (1.0 / (4.0 * ELEM)) for chosen in range(3)]
    deform = [
        [gradients[source][target] + (1.0 if target == source else 0.0) for source in range(3)]
        for target in range(3)
    ]
    strain = [
        [
            0.5
            * (
                deform[0][target] * deform[0][source]
                + deform[1][target] * deform[1][source]
                + deform[2][target] * deform[2][source]
            )
            - (0.5 if target == source else 0.0)
            for source in range(3)
        ]
        for target in range(3)
    ]
    trace_strain = strain[0][0] + strain[1][1] + strain[2][2]
    stress = [
        [
            2.0 * shear_modulus * strain[target][source]
            + (lame_lambda * trace_strain if target == source else 0.0)
            for source in range(3)
        ]
        for target in range(3)
    ]
    nominal = [
        [
            deform[target][0] * stress[0][source]
            + deform[target][1] * stress[1][source]
            + deform[target][2] * stress[2][source]
            for source in range(3)
        ]
        for target in range(3)
    ]
    coefficient = ELEM * ELEM / 4.0
    forces = []
    for target in range(3):
        summed = cross_pairs(nominal[target][0], 0, -1.0, 0)
        for source in range(1, 3):
            summed = summed + cross_pairs(nominal[target][source], source, -1.0, 0)
        forces.append(-coefficient * summed)
    return jnp.stack(forces)


def axis_table(nodes_len, cells_edge, squared):
    voxels = (nodes_len - 1) * cells_edge
    column = jnp.arange(voxels, dtype=jnp.int32)
    element = column // cells_edge
    fraction = (column % cells_edge).astype(jnp.float32) / cells_edge
    weight_low = 1.0 - fraction
    weight_high = fraction
    if squared:
        weight_low = weight_low * weight_low
        weight_high = weight_high * weight_high
    node_row = jnp.arange(nodes_len, dtype=jnp.int32)[:, None]
    return jnp.where(node_row == element[None, :], weight_low[None, :], 0.0) + jnp.where(
        node_row == element[None, :] + 1, weight_high[None, :], 0.0
    )


def spread(padded, weights_table):
    shape_all = padded.shape
    stretched = jnp.dot(padded.reshape(-1, shape_all[3]), weights_table, precision=highest)
    stretched = stretched.reshape(shape_all[0], shape_all[1], shape_all[2], weights_table.shape[1])
    stretched = interp_axis(stretched, 1, ELEM)
    return interp_axis(stretched, 2, ELEM)


def collect(volume, table_back, squared):
    shape_all = volume.shape
    reduced = jnp.dot(volume.reshape(-1, shape_all[3]), table_back, precision=highest)
    reduced = reduced.reshape(shape_all[0], shape_all[1], shape_all[2], table_back.shape[1])
    reduced = collect_axis(reduced, 2, ELEM, squared)
    return collect_axis(reduced, 1, ELEM, squared)


NEIGHBOURS = [(0, 0)] + [(ry, rz) for ry in (-1, 0, 1) for rz in (-1, 0, 1) if (ry, rz) != (0, 0)]
HALO_CAP = 10


def per_device(reference_image, deformed_image, roi_mask, displacement, node_map):
    stacked = jnp.stack([reference_image, deformed_image, roi_mask.astype(jnp.bfloat16)])
    stacked = with_halo(stacked, (("gy", 2),), 5)
    stacked = with_halo(stacked, (("gz", 3),), 5 + ELEM)
    padded_images = with_halo(stacked, (("gx", 1),), 5)
    nodes_shape = (
        3,
        reference_image.shape[0] // ELEM,
        reference_image.shape[1] // ELEM,
        reference_image.shape[2] // ELEM,
    )
    _, ex, ey, ez = nodes_shape
    wide_table = axis_table(ez + 4, ELEM, False)
    wide_back = wide_table[1:-1].T
    wide_square = axis_table(ez + 4, ELEM, True)[1:-1].T
    size_y = lax.axis_size("gy")
    size_z = lax.axis_size("gz")
    members = size_y * size_z
    blocks = node_map.shape[0]
    block_nodes = displacement.shape[2]
    zchunks = ez // block_nodes
    owner_tile = node_map // blocks
    tile_block = node_map % blocks
    tile_y = owner_tile // size_z
    tile_z = owner_tile % size_z
    block_y = (tile_block // zchunks) % ey
    block_zc = tile_block % zchunks
    dests, valids, labels = [], [], []
    for index, (ry, rz) in enumerate(NEIGHBOURS):
        dest_y = tile_y - ry
        dest_z = tile_z - rz
        valid = (dest_y >= 0) & (dest_y < size_y) & (dest_z >= 0) & (dest_z < size_z)
        if ry == -1:
            valid = valid & (block_y == ey - 1)
        elif ry == 1:
            valid = valid & (block_y == 0)
        if rz == -1:
            valid = valid & (block_zc == zchunks - 1)
        elif rz == 1:
            valid = valid & (block_zc == 0)
        dests.append(dest_y * size_z + dest_z)
        valids.append(valid)
        labels.append(index * blocks + tile_block + 1)
    cand_dest = jnp.concatenate(dests)
    cand_valid = jnp.concatenate(valids)
    cand_label = jnp.concatenate(labels).astype(jnp.float32)
    count = cand_dest.shape[0]
    order = jnp.arange(count, dtype=jnp.int32)
    earlier = (
        (cand_dest[:, None] == cand_dest[None, :])
        & cand_valid[None, :]
        & (order[None, :] < order[:, None])
    )
    ranking = jnp.sum(earlier.astype(jnp.int32), axis=1)
    target_slot = jnp.where(cand_valid, cand_dest * HALO_CAP + ranking, -1)
    packing = (
        target_slot[:, None] == jnp.arange(members * HALO_CAP, dtype=jnp.int32)[None, :]
    ).astype(jnp.float32)
    cand_data = jnp.concatenate(
        [
            jnp.concatenate([displacement] * len(NEIGHBOURS), axis=1),
            jnp.broadcast_to(cand_label[None, :, None], (1, count, block_nodes)),
        ]
    )
    send_channels = cand_data.shape[0]
    send_outgoing = jnp.einsum("cjn,jp->cpn", cand_data, packing, precision=highest).reshape(
        send_channels, -1
    )
    send_incoming = lax.all_to_all(
        send_outgoing, ("gy", "gz"), split_axis=1, concat_axis=1, tiled=True
    ).reshape(send_channels, members * HALO_CAP, block_nodes)
    received_labels = send_incoming[3, :, 0]
    placing = (
        received_labels[:, None] == jnp.arange(1, count + 1, dtype=jnp.float32)[None, :]
    ).astype(jnp.float32)
    around = jnp.einsum("cpn,pk->ckn", send_incoming[:3], placing, precision=highest).reshape(
        3, len(NEIGHBOURS), ex, ey, ez
    )

    def near(ry, rz):
        return around[:, NEIGHBOURS.index((ry, rz))]

    centre = near(0, 0)
    middle = jnp.concatenate(
        [near(0, -1)[..., ez - 2 :], centre, near(0, 1)[..., :2]], axis=3
    )
    low_row = jnp.concatenate(
        [
            near(-1, -1)[:, :, ey - 1 :, ez - 2 :],
            near(-1, 0)[:, :, ey - 1 :, :],
            near(-1, 1)[:, :, ey - 1 :, :2],
        ],
        axis=3,
    )
    high_row = jnp.concatenate(
        [near(1, -1)[:, :, :1, ez - 2 :], near(1, 0)[:, :, :1, :], near(1, 1)[:, :, :1, :2]],
        axis=3,
    )
    extended = jnp.concatenate([low_row, middle, high_row], axis=2)
    first_padded = with_halo(extended, (("gx", 1),), 1)
    image_pair = padded_images[:2].astype(jnp.float32)
    derived = derive_fields(image_pair[0], image_pair[1])
    region = padded_images[2][3:-3, 3:-3, 3:-3].astype(jnp.float32)
    contrast = derived[0].astype(jnp.float32)
    slopes = derived[1:].astype(jnp.float32)
    masked_slopes = slopes * region[None]
    wide_curvature = collect(masked_slopes * slopes, wide_square, True) + diagonal_shift
    moved = spread(first_padded, wide_table)
    residual = contrast + slopes[0] * moved[0] + slopes[1] * moved[1] + slopes[2] * moved[2]
    image_part = collect(masked_slopes * residual[None], wide_back, False)
    force_total = image_part + elastic_weight * elastic_force(first_padded)
    wide_values = first_padded[:, 1:-1, 1:-1, 1:-1] - force_total / wide_curvature
    column = jnp.arange(ez + 2, dtype=jnp.int32)
    ghost = ((column == 0) & (lax.axis_index("gz") == 0)) | (
        (column == ez + 1) & (lax.axis_index("gz") == size_z - 1)
    )
    wide_values = jnp.where(ghost, 0.0, wide_values)
    padded = with_halo(wide_values, (("gx", 1), ("gy", 2)), 1)
    padded = jnp.pad(padded, ((0, 0), (0, 0), (0, 0), (1, 1)))
    moved = spread(padded, wide_table)
    residual = contrast + slopes[0] * moved[0] + slopes[1] * moved[1] + slopes[2] * moved[2]
    image_part = collect(masked_slopes * residual[None], wide_back, False)
    force_total = image_part + elastic_weight * elastic_force(padded)
    tile_values = (wide_values - force_total / wide_curvature)[..., 1:-1]
    final_blocks = tile_values.reshape(3, blocks, block_nodes)
    own_labels = received_labels.reshape(members, HALO_CAP)[:, :CAP].reshape(-1)
    position = jnp.arange(blocks, dtype=jnp.int32)
    back_placing = (own_labels[:, None] == (position + 1).astype(jnp.float32)[None, :]).astype(
        jnp.float32
    )
    outgoing = jnp.einsum("ckn,pk->cpn", final_blocks, back_placing, precision=highest).reshape(
        3, -1
    )
    incoming = lax.all_to_all(outgoing, ("gy", "gz"), split_axis=1, concat_axis=1, tiled=True)
    own_slot = owner_tile * CAP + ranking[:blocks]
    back_packing = (
        own_slot[:, None] == jnp.arange(members * CAP, dtype=jnp.int32)[None, :]
    ).astype(jnp.float32)
    return jnp.einsum(
        "cpn,jp->cjn", incoming.reshape(3, members * CAP, -1), back_packing, precision=highest
    )


def solution(mesh):
    in_specs = (
        P("gx", "gy", "gz"),
        P("gx", "gy", "gz"),
        P("gx", "gy", "gz"),
        P(None, ("gx", "gy", "gz"), None),
        P(("gx", "gy", "gz")),
    )
    out_specs = P(None, ("gx", "gy", "gz"), None)
    return jax.shard_map(
        per_device, mesh=mesh, in_specs=in_specs, out_specs=out_specs, check_vma=False
    )
```
